32 devices in a mesh: groups: 2 (over y), seq: 4 (over z), head: 2 (over x), cfg: 2 (over core).
Axes of the slice: x: 2, y: 2, z: 4, core: 2. Of those that a mesh axis runs over, the one named last changes fastest.
Arguments:
- q_img: bfloat16 [2, 4096, 1536], P('cfg', ('groups', 'seq'), 'head'), parts along dimension 1
- k_img: bfloat16 [2, 4096, 1536], P('cfg', ('groups', 'seq'), 'head'), parts along dimension 1
- v_img: bfloat16 [2, 4096, 1536], P('cfg', ('groups', 'seq'), 'head'), parts along dimension 1, may hold values from -6 to 6
- text_keys: bfloat16 [2, 8, 333, 1536], P('cfg', 'groups', None, 'head'), parts along dimension 1
- text_values: bfloat16 [2, 8, 333, 1536], P('cfg', 'groups', None, 'head'), parts along dimension 1, may hold values from -6 to 6
- text_lengths: int32 [2, 8], P('cfg', 'groups'), parts along dimension 1, may hold values from 1 to 333, as said below
- img_lengths: int32 [8], P('groups'), parts along dimension 0, may hold values from 1 to 1024, 2048 in all
- out_weight: bfloat16 [1536, 2432], P(None, 'head'), may hold values from -0.15625 to 0.15625
Outputs:
- guided: bfloat16 [4096, 2432], P(('groups', 'seq'), ('head', 'cfg')), parts along dimension 0
The draws below stay inside these ranges and needn't reach their ends.
There are 2 independent parts, one for each index of `groups`. The reference program is written for one: setup_inputs(seed, part) draws one part's arguments, and reference() takes and returns one part's arrays. A program takes and returns all parts, laid end to end along the dimension named above; an argument that names none is the same for every part. Nothing has to cross between parts.
Inputs may be any that keep to these rules, and one draw needn't show every extreme that they name: `img_lengths`: request r holds the image positions from the sum of the earlier lengths on; the lengths sum to 2048. text_lengths[b, r] of request r's 333 text slots are live in branch b, the first ones.
All inputs are finite; a program needn't handle non-finite values.
Results may differ from the reference program's by a relative error of at most 0.009.
Values may be sent and summed in bfloat16 or wider, within the bound.
No kernel may reach another device: no remote copies, remote signals or barrier semaphores. Data moves between devices by JAX's collectives and lax.ppermute only.
A program may use at most 128 MiB of HBM per device.

```python
import math
import jax
import jax.numpy as jnp
import numpy as np
from jax import lax

D = 2432
HEADS = 24
HDIM = 64
TEXT = 333
REQS = 4
TOKENS = 2048
LONGEST = 1024


def draw_q_img(key, part):
    shape = (2, TOKENS, HEADS * HDIM)
    base = jax.random.normal(jax.random.fold_in(key, 1), shape, jnp.float32)
    return base.astype(jnp.bfloat16)


def draw_k_img(key, part):
    shape = (2, TOKENS, HEADS * HDIM)
    base = jax.random.normal(jax.random.fold_in(key, 2), shape, jnp.float32)
    return base.astype(jnp.bfloat16)


def draw_text_keys(key, part):
    shape = (2, REQS, TEXT, HEADS * HDIM)
    base = jax.random.normal(jax.random.fold_in(key, 3), shape, jnp.float32)
    return base.astype(jnp.bfloat16)


def draw_text_lengths(key, part):
    count = 2 * REQS
    values = jax.random.randint(jax.random.fold_in(key, 11), (count,), 1, TEXT + 1)
    order = jax.random.permutation(jax.random.fold_in(key, 12), count)
    flat = jnp.where(order == 0, TEXT, jnp.where(order == 1, 1, values))
    return flat.reshape(2, REQS).astype(jnp.int32)


def block_scale(stream_key, shape, pieces, smallest, high):
    def one(position, blocks):
        steps = jax.random.uniform(jax.random.fold_in(jax.random.fold_in(stream_key, 6), position), (blocks,), jnp.float32, smallest / len(pieces), high / len(pieces))
        return jnp.repeat(jnp.exp(steps), shape[position] // blocks).reshape((-1,) + (1,) * (len(shape) - position - 1))

    factor_of = one(*pieces[0])
    for cut in pieces[1:]:
        factor_of = factor_of * one(*cut)
    return factor_of


def split_up(number_of, total, most, slope):
    portions = [(1 << 20) // math.isqrt(standing ** slope) + 1 for standing in range(2, number_of + 1)]
    surplus, holding = total - most - (number_of - 1), [1] * (number_of - 1)
    while surplus > 0:
        movable = [i for i in range(number_of - 1) if holding[i] < most]
        pool, budget = sum([portions[i] for i in movable]), surplus
        for i in movable:
            more = min(most - holding[i], max(1, budget * portions[i] // pool), surplus)
            holding[i] = holding[i] + more
            surplus = surplus - more
    return np.array([most] + holding)


def ragged(key, number_of, total, reach, lean):
    if number_of == 2:
        one = jax.random.randint(key, (), max(1, total - reach), min(reach, total - 1) + 1)
        return jnp.stack([one, total - one])
    tallies = jnp.asarray(split_up(number_of, total, reach, lean), jnp.int32)
    pairs = (number_of - 1) // 2
    donor, receiver = tallies[1:1 + 2 * pairs:2], tallies[2:2 + 2 * pairs:2]
    slack = jnp.minimum(donor - 1, reach - receiver)
    shifted = jax.random.randint(jax.random.fold_in(key, 1), (pairs,), 0, 1 << 20) % (slack + 1)
    tallies = tallies.at[1:1 + 2 * pairs:2].set(donor - shifted).at[2:2 + 2 * pairs:2].set(receiver + shifted)
    return tallies[jax.random.permutation(jax.random.fold_in(key, 2), number_of)]


def gaussian(own_key, dims, width, most, cuts=(), held_as=jnp.bfloat16):
    values = width * jax.random.normal(own_key, dims, jnp.float32)
    if cuts:
        values = values * block_scale(own_key, dims, cuts, -0.22, 0.18)
    return jnp.clip(values, -most, most).astype(held_as)


def setup_inputs(seed: int = 0, part: int = 0) -> dict:
    key_list = jax.random.split(jax.random.key(seed), 9)
    part_splits = jax.random.split(jax.random.fold_in(key_list[8], part), 9)
    q_img = draw_q_img(jax.random.fold_in(jax.random.fold_in(key_list[8], part), 71), part)
    k_img = draw_k_img(jax.random.fold_in(jax.random.fold_in(key_list[8], part), 71), part)
    v_img = gaussian(part_splits[2], (2, TOKENS, HEADS * HDIM), 1.0, 6.0, ((0, 2), (1, 4), (2, 2)))
    text_keys = draw_text_keys(jax.random.fold_in(jax.random.fold_in(key_list[8], part), 71), part)
    text_values = gaussian(part_splits[4], (2, REQS, TEXT, HEADS * HDIM), 1.0, 6.0, ((0, 2), (3, 2)))
    text_lengths = draw_text_lengths(jax.random.fold_in(jax.random.fold_in(key_list[8], part), 71), part)
    img_lengths = ragged(part_splits[6], REQS, TOKENS, LONGEST, 2).astype(jnp.int32)
    out_weight = gaussian(key_list[7], (HEADS * HDIM, D), (HEADS * HDIM) ** -0.5, 0.15625, ((1, 2),))
    return {"q_img": q_img, "k_img": k_img, "v_img": v_img, "text_keys": text_keys, "text_values": text_values, "text_lengths": text_lengths, "img_lengths": img_lengths, "out_weight": out_weight}


guidance = 4.0
score_scale = 0.125
neg_large = -1e30


def segment_ids(img_lengths, positions):
    ends = jnp.cumsum(img_lengths).astype(jnp.int32)
    return jnp.sum((positions[:, None] >= ends[None, :]).astype(jnp.int32), axis=1).astype(jnp.int32)


def reference(q_img, k_img, v_img, text_keys, text_values, text_lengths, img_lengths, out_weight):
    positions = jnp.arange(TOKENS, dtype=jnp.int32)
    seg_all = segment_ids(img_lengths, positions)
    text_req = jnp.repeat(jnp.arange(REQS, dtype=jnp.int32), TEXT)
    text_pos = jnp.tile(jnp.arange(TEXT, dtype=jnp.int32), REQS)
    block = math.gcd(TOKENS, 512)
    nblocks = TOKENS // block

    def branch_attn(branch):
        queries = q_img[branch].reshape(TOKENS, HEADS, HDIM)
        keys_all = jnp.concatenate([k_img[branch], text_keys[branch].reshape(REQS * TEXT, HEADS * HDIM)], 0).reshape(-1, HEADS, HDIM)
        vals_all = jnp.concatenate([v_img[branch], text_values[branch].reshape(REQS * TEXT, HEADS * HDIM)], 0).reshape(-1, HEADS, HDIM)
        text_ok = text_pos < text_lengths[branch][text_req]
        key_seg = jnp.concatenate([seg_all, text_req], 0)
        key_ok = jnp.concatenate([jnp.ones((TOKENS,), bool), text_ok], 0)

        def one_block(index):
            q_rows = lax.dynamic_slice_in_dim(queries, index * block, block, 0)
            q_seg = lax.dynamic_slice_in_dim(seg_all, index * block, block, 0)
            mask = (q_seg[:, None] == key_seg[None, :]) & key_ok[None, :]

            def one_head(head):
                q_head = q_rows[:, head, :]
                k_head = keys_all[:, head, :]
                v_head = vals_all[:, head, :]
                scores = jnp.dot(q_head, k_head.T, preferred_element_type=jnp.float32) * score_scale
                scores = jnp.where(mask, scores, neg_large)
                largest = jnp.max(scores, axis=1, keepdims=True)
                weights = jnp.where(mask, jnp.exp(scores - largest), 0.0)
                total = jnp.sum(weights, axis=1, keepdims=True)
                numer = jnp.dot(weights.astype(jnp.bfloat16), v_head, preferred_element_type=jnp.float32)
                return (numer / total).astype(jnp.bfloat16)

            return lax.map(one_head, jnp.arange(HEADS, dtype=jnp.int32))

        result = lax.map(one_block, jnp.arange(nblocks, dtype=jnp.int32))
        return result.transpose(0, 2, 1, 3).reshape(TOKENS, HEADS * HDIM)

    cond_out = jnp.dot(branch_attn(0), out_weight, preferred_element_type=jnp.float32)
    uncond_out = jnp.dot(branch_attn(1), out_weight, preferred_element_type=jnp.float32)
    return (guidance * cond_out + (1.0 - guidance) * uncond_out).astype(jnp.bfloat16)
```

```python
import math

import jax
import jax.numpy as jnp
from jax import lax
from jax.sharding import PartitionSpec as P

HDIM = 64


guidance = 4.0
score_scale = 0.125
neg_large = -1e30


def partner_2(x, axis, distance):
    return lax.ppermute(x, axis, [(i, i ^ 1 << distance) for i in range(lax.axis_size(axis))])


def segment_ids(img_lengths, positions):
    ends = jnp.cumsum(img_lengths)
    return jnp.sum((positions[:, None] >= ends[None, :]).astype(jnp.int32), axis=1)


def split_heads(values, heads_here):
    return values.reshape(values.shape[0], heads_here, HDIM).transpose(1, 0, 2)


def attend(state, queries, keys, values, mask):
    largest, total, numer = state
    scores = (
        jnp.einsum("hqd,hkd->hqk", queries, keys, preferred_element_type=jnp.float32) * score_scale
    )
    scores = jnp.where(mask[None], scores, neg_large)
    fresh = jnp.maximum(largest, jnp.max(scores, axis=2))
    weights = jnp.where(mask[None], jnp.exp(scores - fresh[..., None]), 0.0)
    factor = jnp.exp(largest - fresh)
    total = total * factor + jnp.sum(weights, axis=2)
    numer = numer * factor[..., None] + jnp.einsum(
        "hqk,hkd->hqd", weights.astype(jnp.bfloat16), values, preferred_element_type=jnp.float32
    )
    return (fresh, total, numer)


def local(q_img, k_img, v_img, text_keys, text_values, text_lengths, img_lengths, out_weight):
    tok_dev = q_img.shape[1]
    width = q_img.shape[2]
    heads_here = width // HDIM
    reqs = text_keys.shape[1]
    text_slots = text_keys.shape[2]
    first_pos = lax.axis_index("seq") * tok_dev
    q_seg = segment_ids(img_lengths, first_pos + jnp.arange(tok_dev, dtype=jnp.int32))
    queries = split_heads(q_img[0], heads_here)
    text_req = jnp.repeat(jnp.arange(reqs, dtype=jnp.int32), text_slots)
    text_pos = jnp.tile(jnp.arange(text_slots, dtype=jnp.int32), reqs)
    live_count = jnp.sum(
        jnp.where(
            text_req[:, None] == jnp.arange(reqs, dtype=jnp.int32)[None, :],
            text_lengths[0][None, :],
            0,
        ),
        axis=1,
    )
    text_mask = (q_seg[:, None] == text_req[None, :]) & (text_pos < live_count)[None, :]
    start_state = (
        jnp.full((heads_here, tok_dev), neg_large, jnp.float32),
        jnp.zeros((heads_here, tok_dev), jnp.float32),
        jnp.zeros((heads_here, tok_dev, HDIM), jnp.float32),
    )
    text_k = split_heads(text_keys[0].reshape(reqs * text_slots, width), heads_here)
    text_v = split_heads(text_values[0].reshape(reqs * text_slots, width), heads_here)
    state = attend(start_state, queries, text_k, text_v, text_mask)
    nseq = lax.axis_size("seq")
    me = lax.axis_index("seq")
    total = tok_dev * nseq
    longest = total // 2
    reach = min(nseq - 1, (longest + tok_dev - 2) // tok_dev)
    to_right = [(i, i + 1) for i in range(nseq - 1)]
    to_left = [(i + 1, i) for i in range(nseq - 1)]
    chunks = [(k_img[0], v_img[0], me * tok_dev)]
    left_k, left_v, right_k, right_v = k_img[0], v_img[0], k_img[0], v_img[0]
    for step in range(1, reach + 1):
        left_k = lax.ppermute(left_k, "seq", to_right)
        left_v = lax.ppermute(left_v, "seq", to_right)
        right_k = lax.ppermute(right_k, "seq", to_left)
        right_v = lax.ppermute(right_v, "seq", to_left)
        chunks.append((left_k, left_v, (me - step) * tok_dev))
        chunks.append((right_k, right_v, (me + step) * tok_dev))
    for key_rows, val_rows, lower in chunks:
        k_pos = lower + jnp.arange(tok_dev, dtype=jnp.int32)
        k_seg = segment_ids(img_lengths, k_pos)
        inside = (k_pos >= 0) & (k_pos < total)
        mask = (q_seg[:, None] == k_seg[None, :]) & inside[None, :]
        state = attend(
            state,
            queries,
            split_heads(key_rows, heads_here),
            split_heads(val_rows, heads_here),
            mask,
        )
    largest, total, numer = state
    attn = (
        (numer / total[..., None]).astype(jnp.bfloat16).transpose(1, 0, 2).reshape(tok_dev, width)
    )
    own_cfg = lax.axis_index("cfg")
    cols = out_weight.shape[1]
    half = cols // 2
    mine_weight = jnp.where(own_cfg == 0, guidance, 1.0 - guidance)
    mine = jnp.dot(
        lax.all_gather(attn, "head", axis=1, tiled=True),
        out_weight,
        preferred_element_type=jnp.float32,
    )
    keep = lax.dynamic_slice_in_dim(mine, own_cfg * half, half, 1)
    outgoing = lax.dynamic_slice_in_dim(mine, (1 - own_cfg) * half, half, 1)
    partner = partner_2(outgoing.astype(jnp.bfloat16), "cfg", 0).astype(outgoing.dtype)
    guided = mine_weight * keep + (1.0 - mine_weight) * partner
    return guided.astype(jnp.bfloat16)


def solution(mesh):
    placed = (
        P("cfg", ("groups", "seq"), "head"),
        P("cfg", ("groups", "seq"), "head"),
        P("cfg", ("groups", "seq"), "head"),
        P("cfg", "groups", None, "head"),
        P("cfg", "groups", None, "head"),
        P("cfg", "groups"),
        P("groups"),
        P(None, "head"),
    )
    return jax.shard_map(
        local,
        mesh=mesh,
        in_specs=placed,
        out_specs=P(("groups", "seq"), ("head", "cfg")),
        check_vma=False,
    )
```

```python
import functools

import jax
import jax.numpy as jnp
from jax import lax
from jax.experimental import pallas as pl
from jax.experimental.pallas import tpu as pltpu
from jax.sharding import PartitionSpec as P

HDIM = 64


guidance = 4.0
score_scale = 0.125
neg_large = -1e30


def partner_2(x, axis, distance):
    return lax.ppermute(x, axis, [(i, i ^ 1 << distance) for i in range(lax.axis_size(axis))])


def seg_scalar(info_ref, pos, reqs):
    seg = jnp.int32(0)
    for r in range(reqs):
        seg = seg + jnp.where(pos >= info_ref[2 + r], 1, 0).astype(jnp.int32)
    return seg


def seg_vector(info_ref, pos, reqs):
    seg = jnp.zeros(pos.shape, jnp.int32)
    for r in range(reqs):
        seg = seg + (pos >= info_ref[2 + r]).astype(jnp.int32)
    return seg


def attn_kernel(info_ref, q_ref, k_ref, v_ref, *refs, kind, heads, reqs, tq, tk, total, first, last):
    if first:
        ins, outs = (), refs[:-3]
    else:
        ins, outs = refs[:3], refs[3:-3]
    m_sc, l_sc, a_sc = refs[-3:]
    qi = pl.program_id(0)
    b = pl.program_id(1)
    nb = pl.num_programs(1)
    width = heads * HDIM

    @pl.when(b == 0)
    def _():
        if first:
            m_sc[...] = jnp.full(m_sc.shape, neg_large, jnp.float32)
            l_sc[...] = jnp.zeros(l_sc.shape, jnp.float32)
            a_sc[...] = jnp.zeros(a_sc.shape, jnp.float32)
        else:
            m_sc[...] = ins[0][...]
            l_sc[...] = ins[1][...]
            a_sc[...] = ins[2][...]

    qpos0 = info_ref[0] + qi * tq
    qlo = seg_scalar(info_ref, qpos0, reqs)
    qhi = seg_scalar(info_ref, qpos0 + tq - 1, reqs)
    if kind == "text":
        active = (qlo <= b) & (b <= qhi)
    else:
        kpos0 = info_ref[1] + b * tk
        klo = seg_scalar(info_ref, kpos0, reqs)
        khi = seg_scalar(info_ref, kpos0 + tk - 1, reqs)
        active = (kpos0 >= 0) & (kpos0 < total) & (klo <= qhi) & (qlo <= khi)

    @pl.when(active)
    def _():
        qseg = seg_vector(info_ref, qpos0 + lax.broadcasted_iota(jnp.int32, (tq, 1), 0), reqs)
        col = lax.broadcasted_iota(jnp.int32, (1, tk), 1)
        if kind == "text":
            mask = (qseg == b) & (col < info_ref[2 + reqs + b])
        else:
            mask = qseg == seg_vector(info_ref, kpos0 + col, reqs)
        for g0 in range(0, width, 128):
            gw = min(128, width - g0)
            qg = q_ref[:, g0:g0 + gw]
            kg = k_ref[0, :, g0:g0 + gw]
            vg = v_ref[0, :, g0:g0 + gw]
            acc = a_sc[:, g0:g0 + gw]
            lane = lax.broadcasted_iota(jnp.int32, (1, gw), 1)
            lo = lane < HDIM
            parts = []
            for i in range(gw // HDIM):
                h = g0 // HDIM + i
                if gw == HDIM:
                    qh = qg
                else:
                    qh = jnp.where(lo if i == 0 else jnp.logical_not(lo), qg, jnp.zeros_like(qg))
                s = lax.dot_general(
                    qh, kg, (((1,), (1,)), ((), ())), preferred_element_type=jnp.float32
                ) * score_scale
                s = jnp.where(mask, s, neg_large)
                m_old = m_sc[h]
                m_new = jnp.maximum(m_old, jnp.max(s, axis=1, keepdims=True))
                alpha = jnp.exp(m_old - m_new)
                p = jnp.exp(s - m_new)
                l_sc[h] = alpha * l_sc[h] + jnp.sum(p, axis=1, keepdims=True)
                m_sc[h] = m_new
                pv = jnp.dot(p.astype(jnp.bfloat16), vg, preferred_element_type=jnp.float32)
                parts.append(alpha * acc + pv)
            new = parts[0] if len(parts) == 1 else jnp.where(lo, parts[0], parts[1])
            a_sc[:, g0:g0 + gw] = new

    @pl.when(b == nb - 1)
    def _():
        if last:
            for g0 in range(0, width, 128):
                gw = min(128, width - g0)
                h = g0 // HDIM
                if gw == HDIM:
                    den = l_sc[h]
                else:
                    lane = lax.broadcasted_iota(jnp.int32, (1, gw), 1)
                    den = jnp.where(lane < HDIM, l_sc[h], l_sc[h + 1])
                outs[0][:, g0:g0 + gw] = (a_sc[:, g0:g0 + gw] / den).astype(outs[0].dtype)
        else:
            outs[0][...] = m_sc[...]
            outs[1][...] = l_sc[...]
            outs[2][...] = a_sc[...]


def attend_chunk(info, queries, keys, values, state, *, kind, reqs, total, last):
    tok, width = queries.shape
    heads = width // HDIM
    nb, tk, _ = keys.shape
    tq = min(tok, 256)
    first = state is None
    kernel = functools.partial(
        attn_kernel, kind=kind, heads=heads, reqs=reqs, tq=tq, tk=tk, total=total, first=first, last=last
    )
    q_spec = pl.BlockSpec((tq, width), lambda qi, b, info: (qi, 0))
    kv_spec = pl.BlockSpec((1, tk, width), lambda qi, b, info: (b, 0, 0))
    ml_spec = pl.BlockSpec((heads, tq, 1), lambda qi, b, info: (0, qi, 0))
    in_specs = [q_spec, kv_spec, kv_spec]
    args = [queries, keys, values]
    if not first:
        in_specs += [ml_spec, ml_spec, q_spec]
        args += list(state)
    if last:
        out_shape = jax.ShapeDtypeStruct((tok, width), jnp.bfloat16)
        out_specs = q_spec
    else:
        out_shape = (
            jax.ShapeDtypeStruct((heads, tok, 1), jnp.float32),
            jax.ShapeDtypeStruct((heads, tok, 1), jnp.float32),
            jax.ShapeDtypeStruct((tok, width), jnp.float32),
        )
        out_specs = (ml_spec, ml_spec, q_spec)
    flops = 4 * tok * nb * tk * width * 2
    cost = pl.CostEstimate(
        flops=flops,
        transcendentals=tok * nb * tk * heads,
        bytes_accessed=2 * (tok * width * 2 + 2 * nb * tk * width * 2 + tok * width * 4),
    )
    return pl.pallas_call(
        kernel,
        out_shape=out_shape,
        grid_spec=pltpu.PrefetchScalarGridSpec(
            num_scalar_prefetch=1,
            grid=(tok // tq, nb),
            in_specs=in_specs,
            out_specs=out_specs,
            scratch_shapes=[
                pltpu.VMEM((heads, tq, 1), jnp.float32),
                pltpu.VMEM((heads, tq, 1), jnp.float32),
                pltpu.VMEM((tq, width), jnp.float32),
            ],
        ),
        compiler_params=pltpu.CompilerParams(dimension_semantics=("arbitrary", "arbitrary")),
        cost_estimate=cost,
    )(info, *args)


def local(q_img, k_img, v_img, text_keys, text_values, text_lengths, img_lengths, out_weight):
    tok_dev = q_img.shape[1]
    width = q_img.shape[2]
    reqs = text_keys.shape[1]
    text_slots = text_keys.shape[2]
    nseq = lax.axis_size("seq")
    me = lax.axis_index("seq")
    total = tok_dev * nseq
    longest = total // 2
    reach = min(nseq - 1, (longest + tok_dev - 2) // tok_dev)
    ends = jnp.cumsum(img_lengths).astype(jnp.int32)
    queries = q_img[0]

    def info_for(kstart):
        head = jnp.stack([me * tok_dev, kstart]).astype(jnp.int32)
        return jnp.concatenate([head, ends, text_lengths[0].astype(jnp.int32)])

    pad_to = -(-text_slots // 128) * 128
    pad = ((0, 0), (0, pad_to - text_slots), (0, 0))
    text_k = jnp.pad(text_keys[0], pad)
    text_v = jnp.pad(text_values[0], pad)
    tk = min(tok_dev, 256)

    def as_blocks(x):
        return x.reshape(tok_dev // tk, tk, width)

    common = dict(reqs=reqs, total=total)
    state = attend_chunk(info_for(0), queries, text_k, text_v, None, kind="text", last=False, **common)
    to_right = [(i, i + 1) for i in range(nseq - 1)]
    to_left = [(i + 1, i) for i in range(nseq - 1)]
    chunks = [(k_img[0], v_img[0], me * tok_dev)]
    left_k, left_v, right_k, right_v = k_img[0], v_img[0], k_img[0], v_img[0]
    for step in range(1, reach + 1):
        left_k = lax.ppermute(left_k, "seq", to_right)
        left_v = lax.ppermute(left_v, "seq", to_right)
        right_k = lax.ppermute(right_k, "seq", to_left)
        right_v = lax.ppermute(right_v, "seq", to_left)
        chunks.append((left_k, left_v, (me - step) * tok_dev))
        chunks.append((right_k, right_v, (me + step) * tok_dev))
    for index, (key_rows, val_rows, lower) in enumerate(chunks):
        state = attend_chunk(
            info_for(lower),
            queries,
            as_blocks(key_rows),
            as_blocks(val_rows),
            state,
            kind="image",
            last=index == len(chunks) - 1,
            **common,
        )
    attn = state
    own_cfg = lax.axis_index("cfg")
    cols = out_weight.shape[1]
    half = cols // 2
    mine_weight = jnp.where(own_cfg == 0, guidance, 1.0 - guidance)
    mine = jnp.dot(
        lax.all_gather(attn, "head", axis=1, tiled=True),
        out_weight,
        preferred_element_type=jnp.float32,
    )
    keep = lax.dynamic_slice_in_dim(mine, own_cfg * half, half, 1)
    outgoing = lax.dynamic_slice_in_dim(mine, (1 - own_cfg) * half, half, 1)
    partner = partner_2(outgoing.astype(jnp.bfloat16), "cfg", 0).astype(outgoing.dtype)
    guided = mine_weight * keep + (1.0 - mine_weight) * partner
    return guided.astype(jnp.bfloat16)


def solution(mesh):
    placed = (
        P("cfg", ("groups", "seq"), "head"),
        P("cfg", ("groups", "seq"), "head"),
        P("cfg", ("groups", "seq"), "head"),
        P("cfg", "groups", None, "head"),
        P("cfg", "groups", None, "head"),
        P("cfg", "groups"),
        P("groups"),
        P(None, "head"),
    )
    return jax.shard_map(
        local,
        mesh=mesh,
        in_specs=placed,
        out_specs=P(("groups", "seq"), ("head", "cfg")),
        check_vma=False,
    )
```

```python
import functools

import jax
import jax.numpy as jnp
from jax import lax
from jax.experimental import pallas as pl
from jax.experimental.pallas import tpu as pltpu
from jax.sharding import PartitionSpec as P

HDIM = 64


guidance = 4.0
score_scale = 0.125
neg_large = -1e30


def partner_2(x, axis, distance):
    return lax.ppermute(x, axis, [(i, i ^ 1 << distance) for i in range(lax.axis_size(axis))])


def seg_scalar(info_ref, pos, reqs):
    seg = jnp.int32(0)
    for r in range(reqs):
        seg = seg + jnp.where(pos >= info_ref[2 + r], 1, 0).astype(jnp.int32)
    return seg


def seg_vector(info_ref, pos, reqs):
    seg = jnp.zeros(pos.shape, jnp.int32)
    for r in range(reqs):
        seg = seg + (pos >= info_ref[2 + r]).astype(jnp.int32)
    return seg


def attn_kernel(info_ref, q_ref, k_ref, v_ref, *refs, kind, heads, reqs, tq, tk, total, first, last):
    if first:
        ins, outs = (), refs[:-3]
    else:
        ins, outs = refs[:3], refs[3:-3]
    m_sc, l_sc, a_sc = refs[-3:]
    qi = pl.program_id(0)
    b = pl.program_id(1)
    nb = pl.num_programs(1)
    width = heads * HDIM

    @pl.when(b == 0)
    def _():
        if first:
            m_sc[...] = jnp.full(m_sc.shape, neg_large, jnp.float32)
            l_sc[...] = jnp.zeros(l_sc.shape, jnp.float32)
            a_sc[...] = jnp.zeros(a_sc.shape, jnp.float32)
        else:
            m_sc[...] = ins[0][...]
            l_sc[...] = ins[1][...]
            a_sc[...] = ins[2][...]

    qpos0 = info_ref[0] + qi * tq
    qlo = seg_scalar(info_ref, qpos0, reqs)
    qhi = seg_scalar(info_ref, qpos0 + tq - 1, reqs)
    if kind == "text":
        active = (qlo <= b) & (b <= qhi)
    else:
        kpos0 = info_ref[1] + b * tk
        klo = seg_scalar(info_ref, kpos0, reqs)
        khi = seg_scalar(info_ref, kpos0 + tk - 1, reqs)
        active = (kpos0 >= 0) & (kpos0 < total) & (klo <= qhi) & (qlo <= khi)

    @pl.when(active)
    def _():
        qseg = seg_vector(info_ref, qpos0 + lax.broadcasted_iota(jnp.int32, (tq, 1), 0), reqs)
        col = lax.broadcasted_iota(jnp.int32, (1, tk), 1)
        if kind == "text":
            mask = (qseg == b) & (col < info_ref[2 + reqs + b])
        else:
            mask = qseg == seg_vector(info_ref, kpos0 + col, reqs)
        for g0 in range(0, width, 128):
            gw = min(128, width - g0)
            qg = q_ref[:, g0:g0 + gw]
            kg = k_ref[0, :, g0:g0 + gw]
            vg = v_ref[0, :, g0:g0 + gw]
            acc = a_sc[:, g0:g0 + gw]
            lane = lax.broadcasted_iota(jnp.int32, (1, gw), 1)
            lo = lane < HDIM
            parts = []
            for i in range(gw // HDIM):
                h = g0 // HDIM + i
                if gw == HDIM:
                    qh = qg
                else:
                    qh = jnp.where(lo if i == 0 else jnp.logical_not(lo), qg, jnp.zeros_like(qg))
                s = lax.dot_general(
                    qh, kg, (((1,), (1,)), ((), ())), preferred_element_type=jnp.float32
                ) * score_scale
                s = jnp.where(mask, s, neg_large)
                m_old = m_sc[h]
                m_new = jnp.maximum(m_old, jnp.max(s, axis=1, keepdims=True))
                alpha = jnp.exp(m_old - m_new)
                p = jnp.exp(s - m_new)
                l_sc[h] = alpha * l_sc[h] + jnp.sum(p, axis=1, keepdims=True)
                m_sc[h] = m_new
                pv = jnp.dot(p.astype(jnp.bfloat16), vg, preferred_element_type=jnp.float32)
                parts.append(alpha * acc + pv)
            new = parts[0] if len(parts) == 1 else jnp.where(lo, parts[0], parts[1])
            a_sc[:, g0:g0 + gw] = new

    @pl.when(b == nb - 1)
    def _():
        if last:
            for g0 in range(0, width, 128):
                gw = min(128, width - g0)
                h = g0 // HDIM
                if gw == HDIM:
                    den = l_sc[h]
                else:
                    lane = lax.broadcasted_iota(jnp.int32, (1, gw), 1)
                    den = jnp.where(lane < HDIM, l_sc[h], l_sc[h + 1])
                outs[0][:, g0:g0 + gw] = (a_sc[:, g0:g0 + gw] / den).astype(outs[0].dtype)
        else:
            outs[0][...] = m_sc[...]
            outs[1][...] = l_sc[...]
            outs[2][...] = a_sc[...]


def attend_chunk(info, queries, keys, values, state, *, kind, reqs, total, last):
    tok, width = queries.shape
    heads = width // HDIM
    nb, tk, _ = keys.shape
    tq = min(tok, 256)
    first = state is None
    kernel = functools.partial(
        attn_kernel, kind=kind, heads=heads, reqs=reqs, tq=tq, tk=tk, total=total, first=first, last=last
    )
    q_spec = pl.BlockSpec((tq, width), lambda qi, b, info: (qi, 0))
    kv_spec = pl.BlockSpec((1, tk, width), lambda qi, b, info: (b, 0, 0))
    ml_spec = pl.BlockSpec((heads, tq, 1), lambda qi, b, info: (0, qi, 0))
    in_specs = [q_spec, kv_spec, kv_spec]
    args = [queries, keys, values]
    if not first:
        in_specs += [ml_spec, ml_spec, q_spec]
        args += list(state)
    if last:
        out_shape = jax.ShapeDtypeStruct((tok, width), jnp.bfloat16)
        out_specs = q_spec
    else:
        out_shape = (
            jax.ShapeDtypeStruct((heads, tok, 1), jnp.float32),
            jax.ShapeDtypeStruct((heads, tok, 1), jnp.float32),
            jax.ShapeDtypeStruct((tok, width), jnp.float32),
        )
        out_specs = (ml_spec, ml_spec, q_spec)
    flops = 32 * 4 * tok * nb * tk * width * 2
    cost = pl.CostEstimate(
        flops=flops,
        transcendentals=tok * nb * tk * heads,
        bytes_accessed=2 * (tok * width * 2 + 2 * nb * tk * width * 2 + tok * width * 4),
    )
    return pl.pallas_call(
        kernel,
        out_shape=out_shape,
        grid_spec=pltpu.PrefetchScalarGridSpec(
            num_scalar_prefetch=1,
            grid=(tok // tq, nb),
            in_specs=in_specs,
            out_specs=out_specs,
            scratch_shapes=[
                pltpu.VMEM((heads, tq, 1), jnp.float32),
                pltpu.VMEM((heads, tq, 1), jnp.float32),
                pltpu.VMEM((tq, width), jnp.float32),
            ],
        ),
        compiler_params=pltpu.CompilerParams(dimension_semantics=("arbitrary", "arbitrary")),
        cost_estimate=cost,
    )(info, *args)


def local(q_img, k_img, v_img, text_keys, text_values, text_lengths, img_lengths, out_weight):
    tok_dev = q_img.shape[1]
    width = q_img.shape[2]
    reqs = text_keys.shape[1]
    text_slots = text_keys.shape[2]
    nseq = lax.axis_size("seq")
    me = lax.axis_index("seq")
    total = tok_dev * nseq
    longest = total // 2
    reach = min(nseq - 1, (longest + tok_dev - 2) // tok_dev)
    ends = jnp.cumsum(img_lengths).astype(jnp.int32)
    queries = q_img[0]

    def info_for(kstart):
        head = jnp.stack([me * tok_dev, kstart]).astype(jnp.int32)
        return jnp.concatenate([head, ends, text_lengths[0].astype(jnp.int32)])

    pad_to = -(-text_slots // 128) * 128
    pad = ((0, 0), (0, pad_to - text_slots), (0, 0))
    text_k = jnp.pad(text_keys[0], pad)
    text_v = jnp.pad(text_values[0], pad)
    tk = min(tok_dev, 256)

    def as_blocks(x):
        return x.reshape(tok_dev // tk, tk, width)

    common = dict(reqs=reqs, total=total)
    state = attend_chunk(info_for(0), queries, text_k, text_v, None, kind="text", last=False, **common)
    to_right = [(i, i + 1) for i in range(nseq - 1)]
    to_left = [(i + 1, i) for i in range(nseq - 1)]
    chunks = [(k_img[0], v_img[0], me * tok_dev)]
    left_k, left_v, right_k, right_v = k_img[0], v_img[0], k_img[0], v_img[0]
    for step in range(1, reach + 1):
        left_k = lax.ppermute(left_k, "seq", to_right)
        left_v = lax.ppermute(left_v, "seq", to_right)
        right_k = lax.ppermute(right_k, "seq", to_left)
        right_v = lax.ppermute(right_v, "seq", to_left)
        chunks.append((left_k, left_v, (me - step) * tok_dev))
        chunks.append((right_k, right_v, (me + step) * tok_dev))
    for index, (key_rows, val_rows, lower) in enumerate(chunks):
        state = attend_chunk(
            info_for(lower),
            queries,
            as_blocks(key_rows),
            as_blocks(val_rows),
            state,
            kind="image",
            last=index == len(chunks) - 1,
            **common,
        )
    attn = state
    own_cfg = lax.axis_index("cfg")
    cols = out_weight.shape[1]
    half = cols // 2
    mine_weight = jnp.where(own_cfg == 0, guidance, 1.0 - guidance)
    w_keep = lax.dynamic_slice_in_dim(out_weight, own_cfg * half, half, 1)
    w_out = lax.dynamic_slice_in_dim(out_weight, (1 - own_cfg) * half, half, 1)
    nhead = lax.axis_size("head")
    if nhead == 2:
        hx = lax.axis_index("head")
        other = partner_2(attn, "head", 0)

        def project(w):
            w_mine = lax.dynamic_slice_in_dim(w, hx * width, width, 0)
            w_other = lax.dynamic_slice_in_dim(w, (1 - hx) * width, width, 0)
            own = lax.optimization_barrier(jnp.dot(attn, w_mine, preferred_element_type=jnp.float32))
            return own + jnp.dot(other, w_other, preferred_element_type=jnp.float32)
    else:
        gathered = lax.all_gather(attn, "head", axis=1, tiled=True)

        def project(w):
            return jnp.dot(gathered, w, preferred_element_type=jnp.float32)

    outgoing = project(w_out)
    partner = partner_2(outgoing.astype(jnp.bfloat16), "cfg", 0).astype(outgoing.dtype)
    keep = project(w_keep)
    guided = mine_weight * keep + (1.0 - mine_weight) * partner
    return guided.astype(jnp.bfloat16)


def solution(mesh):
    placed = (
        P("cfg", ("groups", "seq"), "head"),
        P("cfg", ("groups", "seq"), "head"),
        P("cfg", ("groups", "seq"), "head"),
        P("cfg", "groups", None, "head"),
        P("cfg", "groups", None, "head"),
        P("cfg", "groups"),
        P("groups"),
        P(None, "head"),
    )
    return jax.shard_map(
        local,
        mesh=mesh,
        in_specs=placed,
        out_specs=P(("groups", "seq"), ("head", "cfg")),
        check_vma=False,
    )
```

```python
import functools

import jax
import jax.numpy as jnp
from jax import lax
from jax.experimental import pallas as pl
from jax.experimental.pallas import tpu as pltpu
from jax.sharding import PartitionSpec as P

HDIM = 64


guidance = 4.0
score_scale = 0.125
neg_large = -1e30


def partner_2(x, axis, distance):
    return lax.ppermute(x, axis, [(i, i ^ 1 << distance) for i in range(lax.axis_size(axis))])


def seg_scalar(info_ref, pos, reqs):
    seg = jnp.int32(0)
    for r in range(reqs):
        seg = seg + jnp.where(pos >= info_ref[2 + r], 1, 0).astype(jnp.int32)
    return seg


def seg_vector(info_ref, pos, reqs):
    seg = jnp.zeros(pos.shape, jnp.int32)
    for r in range(reqs):
        seg = seg + (pos >= info_ref[2 + r]).astype(jnp.int32)
    return seg


def attn_kernel(info_ref, q_ref, k_ref, v_ref, *refs, kind, heads, reqs, tq, tk, total, first, last):
    if first:
        ins, outs = (), refs[:-3]
    else:
        ins, outs = refs[:3], refs[3:-3]
    m_sc, l_sc, a_sc = refs[-3:]
    qi = pl.program_id(0)
    b = pl.program_id(1)
    nb = pl.num_programs(1)
    width = heads * HDIM

    @pl.when(b == 0)
    def _():
        if first:
            m_sc[...] = jnp.full(m_sc.shape, neg_large, jnp.float32)
            l_sc[...] = jnp.zeros(l_sc.shape, jnp.float32)
            a_sc[...] = jnp.zeros(a_sc.shape, jnp.float32)
        else:
            m_sc[...] = ins[0][...]
            l_sc[...] = ins[1][...]
            a_sc[...] = ins[2][...]

    qpos0 = info_ref[0] + qi * tq
    qlo = seg_scalar(info_ref, qpos0, reqs)
    qhi = seg_scalar(info_ref, qpos0 + tq - 1, reqs)
    if kind == "text":
        active = (qlo <= b) & (b <= qhi)
    else:
        kpos0 = info_ref[1] + b * tk
        klo = seg_scalar(info_ref, kpos0, reqs)
        khi = seg_scalar(info_ref, kpos0 + tk - 1, reqs)
        active = (kpos0 >= 0) & (kpos0 < total) & (klo <= qhi) & (qlo <= khi)

    @pl.when(active)
    def _():
        qseg = seg_vector(info_ref, qpos0 + lax.broadcasted_iota(jnp.int32, (tq, 1), 0), reqs)
        col = lax.broadcasted_iota(jnp.int32, (1, tk), 1)
        if kind == "text":
            mask = (qseg == b) & (col < info_ref[2 + reqs + b])
        else:
            mask = qseg == seg_vector(info_ref, kpos0 + col, reqs)
        for g0 in range(0, width, 128):
            gw = min(128, width - g0)
            qg = q_ref[:, g0:g0 + gw]
            kg = k_ref[0, :, g0:g0 + gw]
            vg = v_ref[0, :, g0:g0 + gw]
            acc = a_sc[:, g0:g0 + gw]
            lane = lax.broadcasted_iota(jnp.int32, (1, gw), 1)
            lo = lane < HDIM
            parts = []
            for i in range(gw // HDIM):
                h = g0 // HDIM + i
                if gw == HDIM:
                    qh = qg
                else:
                    qh = jnp.where(lo if i == 0 else jnp.logical_not(lo), qg, jnp.zeros_like(qg))
                s = lax.dot_general(
                    qh, kg, (((1,), (1,)), ((), ())), preferred_element_type=jnp.float32
                ) * score_scale
                s = jnp.where(mask, s, neg_large)
                m_old = m_sc[h]
                m_new = jnp.maximum(m_old, jnp.max(s, axis=1, keepdims=True))
                alpha = jnp.exp(m_old - m_new)
                p = jnp.exp(s - m_new)
                l_sc[h] = alpha * l_sc[h] + jnp.sum(p, axis=1, keepdims=True)
                m_sc[h] = m_new
                pv = jnp.dot(p.astype(jnp.bfloat16), vg, preferred_element_type=jnp.float32)
                parts.append(alpha * acc + pv)
            new = parts[0] if len(parts) == 1 else jnp.where(lo, parts[0], parts[1])
            a_sc[:, g0:g0 + gw] = new

    @pl.when(b == nb - 1)
    def _():
        if last:
            for g0 in range(0, width, 128):
                gw = min(128, width - g0)
                h = g0 // HDIM
                if gw == HDIM:
                    den = l_sc[h]
                else:
                    lane = lax.broadcasted_iota(jnp.int32, (1, gw), 1)
                    den = jnp.where(lane < HDIM, l_sc[h], l_sc[h + 1])
                outs[0][:, g0:g0 + gw] = (a_sc[:, g0:g0 + gw] / den).astype(outs[0].dtype)
        else:
            outs[0][...] = m_sc[...]
            outs[1][...] = l_sc[...]
            outs[2][...] = a_sc[...]


def attend_chunk(info, queries, keys, values, state, *, kind, reqs, total, last):
    tok, width = queries.shape
    heads = width // HDIM
    nb, tk, _ = keys.shape
    tq = min(tok, 256)
    first = state is None
    kernel = functools.partial(
        attn_kernel, kind=kind, heads=heads, reqs=reqs, tq=tq, tk=tk, total=total, first=first, last=last
    )
    q_spec = pl.BlockSpec((tq, width), lambda qi, b, info: (qi, 0))
    kv_spec = pl.BlockSpec((1, tk, width), lambda qi, b, info: (b, 0, 0))
    ml_spec = pl.BlockSpec((heads, tq, 1), lambda qi, b, info: (0, qi, 0))
    in_specs = [q_spec, kv_spec, kv_spec]
    args = [queries, keys, values]
    if not first:
        in_specs += [ml_spec, ml_spec, q_spec]
        args += list(state)
    if last:
        out_shape = jax.ShapeDtypeStruct((tok, width), jnp.bfloat16)
        out_specs = q_spec
    else:
        out_shape = (
            jax.ShapeDtypeStruct((heads, tok, 1), jnp.float32),
            jax.ShapeDtypeStruct((heads, tok, 1), jnp.float32),
            jax.ShapeDtypeStruct((tok, width), jnp.float32),
        )
        out_specs = (ml_spec, ml_spec, q_spec)
    flops = 32 * 4 * tok * nb * tk * width * 2
    cost = pl.CostEstimate(
        flops=flops,
        transcendentals=tok * nb * tk * heads,
        bytes_accessed=2 * (tok * width * 2 + 2 * nb * tk * width * 2 + tok * width * 4),
    )
    return pl.pallas_call(
        kernel,
        out_shape=out_shape,
        grid_spec=pltpu.PrefetchScalarGridSpec(
            num_scalar_prefetch=1,
            grid=(tok // tq, nb),
            in_specs=in_specs,
            out_specs=out_specs,
            scratch_shapes=[
                pltpu.VMEM((heads, tq, 1), jnp.float32),
                pltpu.VMEM((heads, tq, 1), jnp.float32),
                pltpu.VMEM((tq, width), jnp.float32),
            ],
        ),
        compiler_params=pltpu.CompilerParams(dimension_semantics=("arbitrary", "arbitrary")),
        cost_estimate=cost,
    )(info, *args)


def local(q_img, k_img, v_img, text_keys, text_values, text_lengths, img_lengths, out_weight):
    tok_dev = q_img.shape[1]
    width = q_img.shape[2]
    reqs = text_keys.shape[1]
    text_slots = text_keys.shape[2]
    nseq = lax.axis_size("seq")
    me = lax.axis_index("seq")
    total = tok_dev * nseq
    longest = total // 2
    reach = min(nseq - 1, (longest + tok_dev - 2) // tok_dev)
    ends = jnp.cumsum(img_lengths).astype(jnp.int32)
    queries = q_img[0]

    def info_for(kstart):
        head = jnp.stack([me * tok_dev, kstart]).astype(jnp.int32)
        return jnp.concatenate([head, ends, text_lengths[0].astype(jnp.int32)])

    pad_to = -(-text_slots // 128) * 128
    pad = ((0, 0), (0, pad_to - text_slots), (0, 0))
    text_k = jnp.pad(text_keys[0], pad)
    text_v = jnp.pad(text_values[0], pad)
    tk = min(tok_dev, 256)

    def as_blocks(x):
        return x.reshape(tok_dev // tk, tk, width)

    common = dict(reqs=reqs, total=total)
    state = attend_chunk(info_for(0), queries, text_k, text_v, None, kind="text", last=False, **common)
    chunks = [(k_img[0], v_img[0], me * tok_dev)]
    for step in range(1, reach + 1):
        to_right = [(i, i + step) for i in range(nseq - step)]
        to_left = [(i + step, i) for i in range(nseq - step)]
        for pairs, sign in ((to_right, -1), (to_left, 1)):
            chunks.append(
                (
                    lax.ppermute(k_img[0], "seq", pairs),
                    lax.ppermute(v_img[0], "seq", pairs),
                    (me + sign * step) * tok_dev,
                )
            )
    for index, (key_rows, val_rows, lower) in enumerate(chunks):
        state = attend_chunk(
            info_for(lower),
            queries,
            as_blocks(key_rows),
            as_blocks(val_rows),
            state,
            kind="image",
            last=index == len(chunks) - 1,
            **common,
        )
    attn = state
    own_cfg = lax.axis_index("cfg")
    cols = out_weight.shape[1]
    half = cols // 2
    mine_weight = jnp.where(own_cfg == 0, guidance, 1.0 - guidance)
    w_keep = lax.dynamic_slice_in_dim(out_weight, own_cfg * half, half, 1)
    w_out = lax.dynamic_slice_in_dim(out_weight, (1 - own_cfg) * half, half, 1)
    nhead = lax.axis_size("head")
    if nhead == 2:
        hx = lax.axis_index("head")
        other = partner_2(attn, "head", 0)

        def project(w):
            w_mine = lax.dynamic_slice_in_dim(w, hx * width, width, 0)
            w_other = lax.dynamic_slice_in_dim(w, (1 - hx) * width, width, 0)
            own = lax.optimization_barrier(jnp.dot(attn, w_mine, preferred_element_type=jnp.float32))
            return own + jnp.dot(other, w_other, preferred_element_type=jnp.float32)
    else:
        gathered = lax.all_gather(attn, "head", axis=1, tiled=True)

        def project(w):
            return jnp.dot(gathered, w, preferred_element_type=jnp.float32)

    outgoing = project(w_out)
    partner = partner_2(outgoing.astype(jnp.bfloat16), "cfg", 0).astype(outgoing.dtype)
    keep = project(w_keep)
    guided = mine_weight * keep + (1.0 - mine_weight) * partner
    return guided.astype(jnp.bfloat16)


def solution(mesh):
    placed = (
        P("cfg", ("groups", "seq"), "head"),
        P("cfg", ("groups", "seq"), "head"),
        P("cfg", ("groups", "seq"), "head"),
        P("cfg", "groups", None, "head"),
        P("cfg", "groups", None, "head"),
        P("cfg", "groups"),
        P("groups"),
        P(None, "head"),
    )
    return jax.shard_map(
        local,
        mesh=mesh,
        in_specs=placed,
        out_specs=P(("groups", "seq"), ("head", "cfg")),
        check_vma=False,
    )
```

```python
import functools

import jax
import jax.numpy as jnp
from jax import lax
from jax.experimental import pallas as pl
from jax.experimental.pallas import tpu as pltpu
from jax.sharding import PartitionSpec as P

HDIM = 64


guidance = 4.0
score_scale = 0.125
neg_large = -1e30


def partner_2(x, axis, distance):
    return lax.ppermute(x, axis, [(i, i ^ 1 << distance) for i in range(lax.axis_size(axis))])


def seg_scalar(info_ref, pos, reqs):
    seg = jnp.int32(0)
    for r in range(reqs):
        seg = seg + jnp.where(pos >= info_ref[2 + r], 1, 0).astype(jnp.int32)
    return seg


def seg_vector(info_ref, pos, reqs):
    seg = jnp.zeros(pos.shape, jnp.int32)
    for r in range(reqs):
        seg = seg + (pos >= info_ref[2 + r]).astype(jnp.int32)
    return seg


def attn_kernel(info_ref, q_ref, k_ref, v_ref, *refs, kind, heads, reqs, tq, tk, total, first, last):
    if first:
        ins, outs = (), refs[:-3]
    else:
        ins, outs = refs[:3], refs[3:-3]
    m_sc, l_sc, a_sc = refs[-3:]
    qi = pl.program_id(0)
    b = pl.program_id(1)
    nb = pl.num_programs(1)
    width = heads * HDIM

    @pl.when(b == 0)
    def _():
        if first:
            m_sc[...] = jnp.full(m_sc.shape, neg_large, jnp.float32)
            l_sc[...] = jnp.zeros(l_sc.shape, jnp.float32)
            a_sc[...] = jnp.zeros(a_sc.shape, jnp.float32)
        else:
            m_sc[...] = ins[0][...]
            l_sc[...] = ins[1][...]
            a_sc[...] = ins[2][...]

    qpos0 = info_ref[0] + qi * tq
    qlo = seg_scalar(info_ref, qpos0, reqs)
    qhi = seg_scalar(info_ref, qpos0 + tq - 1, reqs)
    if kind == "text":
        active = (qlo <= b) & (b <= qhi)
    else:
        kpos0 = info_ref[1] + b * tk
        klo = seg_scalar(info_ref, kpos0, reqs)
        khi = seg_scalar(info_ref, kpos0 + tk - 1, reqs)
        active = (kpos0 >= 0) & (kpos0 < total) & (klo <= qhi) & (qlo <= khi)

    @pl.when(active)
    def _():
        qseg = seg_vector(info_ref, qpos0 + lax.broadcasted_iota(jnp.int32, (tq, 1), 0), reqs)
        col = lax.broadcasted_iota(jnp.int32, (1, tk), 1)
        if kind == "text":
            mask = (qseg == b) & (col < info_ref[2 + reqs + b])
        else:
            mask = qseg == seg_vector(info_ref, kpos0 + col, reqs)
        for g0 in range(0, width, 128):
            gw = min(128, width - g0)
            qg = q_ref[:, g0:g0 + gw]
            kg = k_ref[0, :, g0:g0 + gw]
            vg = v_ref[0, :, g0:g0 + gw]
            acc = a_sc[:, g0:g0 + gw]
            lane = lax.broadcasted_iota(jnp.int32, (1, gw), 1)
            lo = lane < HDIM
            parts = []
            for i in range(gw // HDIM):
                h = g0 // HDIM + i
                if gw == HDIM:
                    qh = qg
                else:
                    qh = jnp.where(lo if i == 0 else jnp.logical_not(lo), qg, jnp.zeros_like(qg))
                s = lax.dot_general(
                    qh, kg, (((1,), (1,)), ((), ())), preferred_element_type=jnp.float32
                ) * score_scale
                s = jnp.where(mask, s, neg_large)
                m_old = m_sc[h]
                m_new = jnp.maximum(m_old, jnp.max(s, axis=1, keepdims=True))
                alpha = jnp.exp(m_old - m_new)
                p = jnp.exp(s - m_new)
                l_sc[h] = alpha * l_sc[h] + jnp.sum(p, axis=1, keepdims=True)
                m_sc[h] = m_new
                pv = jnp.dot(p.astype(jnp.bfloat16), vg, preferred_element_type=jnp.float32)
                parts.append(alpha * acc + pv)
            new = parts[0] if len(parts) == 1 else jnp.where(lo, parts[0], parts[1])
            a_sc[:, g0:g0 + gw] = new

    @pl.when(b == nb - 1)
    def _():
        if last:
            for g0 in range(0, width, 128):
                gw = min(128, width - g0)
                h = g0 // HDIM
                if gw == HDIM:
                    den = l_sc[h]
                else:
                    lane = lax.broadcasted_iota(jnp.int32, (1, gw), 1)
                    den = jnp.where(lane < HDIM, l_sc[h], l_sc[h + 1])
                outs[0][:, g0:g0 + gw] = (a_sc[:, g0:g0 + gw] / den).astype(outs[0].dtype)
        else:
            outs[0][...] = m_sc[...]
            outs[1][...] = l_sc[...]
            outs[2][...] = a_sc[...]


def attend_chunk(info, queries, keys, values, state, *, kind, reqs, total, last):
    tok, width = queries.shape
    heads = width // HDIM
    nb, tk, _ = keys.shape
    tq = min(tok, 256)
    first = state is None
    kernel = functools.partial(
        attn_kernel, kind=kind, heads=heads, reqs=reqs, tq=tq, tk=tk, total=total, first=first, last=last
    )
    q_spec = pl.BlockSpec((tq, width), lambda qi, b, info: (qi, 0))
    kv_spec = pl.BlockSpec((1, tk, width), lambda qi, b, info: (b, 0, 0))
    ml_spec = pl.BlockSpec((heads, tq, 1), lambda qi, b, info: (0, qi, 0))
    in_specs = [q_spec, kv_spec, kv_spec]
    args = [queries, keys, values]
    if not first:
        in_specs += [ml_spec, ml_spec, q_spec]
        args += list(state)
    if last:
        out_shape = jax.ShapeDtypeStruct((tok, width), jnp.bfloat16)
        out_specs = q_spec
    else:
        out_shape = (
            jax.ShapeDtypeStruct((heads, tok, 1), jnp.float32),
            jax.ShapeDtypeStruct((heads, tok, 1), jnp.float32),
            jax.ShapeDtypeStruct((tok, width), jnp.float32),
        )
        out_specs = (ml_spec, ml_spec, q_spec)
    flops = 32 * 4 * tok * nb * tk * width * 2
    cost = pl.CostEstimate(
        flops=flops,
        transcendentals=tok * nb * tk * heads,
        bytes_accessed=2 * (tok * width * 2 + 2 * nb * tk * width * 2 + tok * width * 4),
    )
    return pl.pallas_call(
        kernel,
        out_shape=out_shape,
        grid_spec=pltpu.PrefetchScalarGridSpec(
            num_scalar_prefetch=1,
            grid=(tok // tq, nb),
            in_specs=in_specs,
            out_specs=out_specs,
            scratch_shapes=[
                pltpu.VMEM((heads, tq, 1), jnp.float32),
                pltpu.VMEM((heads, tq, 1), jnp.float32),
                pltpu.VMEM((tq, width), jnp.float32),
            ],
        ),
        compiler_params=pltpu.CompilerParams(dimension_semantics=("arbitrary", "arbitrary")),
        cost_estimate=cost,
    )(info, *args)


def local(q_img, k_img, v_img, text_keys, text_values, text_lengths, img_lengths, out_weight):
    tok_dev = q_img.shape[1]
    width = q_img.shape[2]
    reqs = text_keys.shape[1]
    text_slots = text_keys.shape[2]
    nseq = lax.axis_size("seq")
    me = lax.axis_index("seq")
    total = tok_dev * nseq
    longest = total // 2
    reach = min(nseq - 1, (longest + tok_dev - 2) // tok_dev)
    ends = jnp.cumsum(img_lengths).astype(jnp.int32)
    queries = q_img[0]

    def info_for(kstart):
        head = jnp.stack([me * tok_dev, kstart]).astype(jnp.int32)
        return jnp.concatenate([head, ends, text_lengths[0].astype(jnp.int32)])

    pad_to = -(-text_slots // 128) * 128
    pad = ((0, 0), (0, pad_to - text_slots), (0, 0))
    text_k = jnp.pad(text_keys[0], pad)
    text_v = jnp.pad(text_values[0], pad)
    tk = min(tok_dev, 256)

    def as_blocks(x):
        return x.reshape(tok_dev // tk, tk, width)

    common = dict(reqs=reqs, total=total)
    state = attend_chunk(info_for(0), queries, text_k, text_v, None, kind="text", last=False, **common)
    chunks = [(k_img[0], v_img[0], me * tok_dev)]
    both = jnp.stack([k_img[0], v_img[0]])
    for step in range(1, reach + 1):
        to_right = [(i, i + step) for i in range(nseq - step)]
        to_left = [(i + step, i) for i in range(nseq - step)]
        for pairs, sign in ((to_right, -1), (to_left, 1)):
            got = lax.ppermute(both, "seq", pairs)
            chunks.append((got[0], got[1], (me + sign * step) * tok_dev))
    for index, (key_rows, val_rows, lower) in enumerate(chunks):
        state = attend_chunk(
            info_for(lower),
            queries,
            as_blocks(key_rows),
            as_blocks(val_rows),
            state,
            kind="image",
            last=index == len(chunks) - 1,
            **common,
        )
    attn = state
    own_cfg = lax.axis_index("cfg")
    cols = out_weight.shape[1]
    half = cols // 2
    mine_weight = jnp.where(own_cfg == 0, guidance, 1.0 - guidance)
    w_keep = lax.dynamic_slice_in_dim(out_weight, own_cfg * half, half, 1)
    w_out = lax.dynamic_slice_in_dim(out_weight, (1 - own_cfg) * half, half, 1)
    nhead = lax.axis_size("head")
    if nhead == 2:
        hx = lax.axis_index("head")
        other = partner_2(attn, "head", 0)

        def project(w):
            w_mine = lax.dynamic_slice_in_dim(w, hx * width, width, 0)
            w_other = lax.dynamic_slice_in_dim(w, (1 - hx) * width, width, 0)
            own = lax.optimization_barrier(jnp.dot(attn, w_mine, preferred_element_type=jnp.float32))
            return own + jnp.dot(other, w_other, preferred_element_type=jnp.float32)
    else:
        gathered = lax.all_gather(attn, "head", axis=1, tiled=True)

        def project(w):
            return jnp.dot(gathered, w, preferred_element_type=jnp.float32)

    outgoing = project(w_out)
    partner = partner_2(outgoing.astype(jnp.bfloat16), "cfg", 0).astype(outgoing.dtype)
    keep = project(w_keep)
    guided = mine_weight * keep + (1.0 - mine_weight) * partner
    return guided.astype(jnp.bfloat16)


def solution(mesh):
    placed = (
        P("cfg", ("groups", "seq"), "head"),
        P("cfg", ("groups", "seq"), "head"),
        P("cfg", ("groups", "seq"), "head"),
        P("cfg", "groups", None, "head"),
        P("cfg", "groups", None, "head"),
        P("cfg", "groups"),
        P("groups"),
        P(None, "head"),
    )
    return jax.shard_map(
        local,
        mesh=mesh,
        in_specs=placed,
        out_specs=P(("groups", "seq"), ("head", "cfg")),
        check_vma=False,
    )
```

```python
import functools

import jax
import jax.numpy as jnp
from jax import lax
from jax.experimental import pallas as pl
from jax.experimental.pallas import tpu as pltpu
from jax.sharding import PartitionSpec as P

HDIM = 64


guidance = 4.0
score_scale = 0.125
neg_large = -1e30


def partner_2(x, axis, distance):
    return lax.ppermute(x, axis, [(i, i ^ 1 << distance) for i in range(lax.axis_size(axis))])


def seg_scalar(info_ref, pos, reqs):
    seg = jnp.int32(0)
    for r in range(reqs):
        seg = seg + jnp.where(pos >= info_ref[2 + r], 1, 0).astype(jnp.int32)
    return seg


def seg_vector(info_ref, pos, reqs):
    seg = jnp.zeros(pos.shape, jnp.int32)
    for r in range(reqs):
        seg = seg + (pos >= info_ref[2 + r]).astype(jnp.int32)
    return seg


def attn_kernel(info_ref, q_ref, k_ref, v_ref, *refs, kind, heads, reqs, tq, tk, total, first, last):
    if first:
        ins, outs = (), refs[:-3]
    else:
        ins, outs = refs[:3], refs[3:-3]
    m_sc, l_sc, a_sc = refs[-3:]
    qi = pl.program_id(0)
    b = pl.program_id(1)
    nb = pl.num_programs(1)
    width = heads * HDIM

    @pl.when(b == 0)
    def _():
        if first:
            m_sc[...] = jnp.full(m_sc.shape, neg_large, jnp.float32)
            l_sc[...] = jnp.zeros(l_sc.shape, jnp.float32)
            a_sc[...] = jnp.zeros(a_sc.shape, jnp.float32)
        else:
            m_sc[...] = ins[0][...]
            l_sc[...] = ins[1][...]
            a_sc[...] = ins[2][...]

    qpos0 = info_ref[0] + qi * tq
    qlo = seg_scalar(info_ref, qpos0, reqs)
    qhi = seg_scalar(info_ref, qpos0 + tq - 1, reqs)
    if kind == "text":
        active = (qlo <= b) & (b <= qhi)
    else:
        kpos0 = info_ref[1] + b * tk
        klo = seg_scalar(info_ref, kpos0, reqs)
        khi = seg_scalar(info_ref, kpos0 + tk - 1, reqs)
        active = (kpos0 >= 0) & (kpos0 < total) & (klo <= qhi) & (qlo <= khi)

    @pl.when(active)
    def _():
        qseg = seg_vector(info_ref, qpos0 + lax.broadcasted_iota(jnp.int32, (tq, 1), 0), reqs)
        col = lax.broadcasted_iota(jnp.int32, (1, tk), 1)
        if kind == "text":
            mask = (qseg == b) & (col < info_ref[2 + reqs + b])
        else:
            mask = qseg == seg_vector(info_ref, kpos0 + col, reqs)
        for g0 in range(0, width, 128):
            gw = min(128, width - g0)
            qg = q_ref[:, g0:g0 + gw]
            kg = k_ref[0, :, g0:g0 + gw]
            vg = v_ref[0, :, g0:g0 + gw]
            acc = a_sc[:, g0:g0 + gw]
            lane = lax.broadcasted_iota(jnp.int32, (1, gw), 1)
            lo = lane < HDIM
            parts = []
            for i in range(gw // HDIM):
                h = g0 // HDIM + i
                if gw == HDIM:
                    qh = qg
                else:
                    qh = jnp.where(lo if i == 0 else jnp.logical_not(lo), qg, jnp.zeros_like(qg))
                s = lax.dot_general(
                    qh, kg, (((1,), (1,)), ((), ())), preferred_element_type=jnp.float32
                ) * score_scale
                s = jnp.where(mask, s, neg_large)
                m_old = m_sc[h]
                m_new = jnp.maximum(m_old, jnp.max(s, axis=1, keepdims=True))
                alpha = jnp.exp(m_old - m_new)
                p = jnp.exp(s - m_new)
                l_sc[h] = alpha * l_sc[h] + jnp.sum(p, axis=1, keepdims=True)
                m_sc[h] = m_new
                pv = jnp.dot(p.astype(jnp.bfloat16), vg, preferred_element_type=jnp.float32)
                parts.append(alpha * acc + pv)
            new = parts[0] if len(parts) == 1 else jnp.where(lo, parts[0], parts[1])
            a_sc[:, g0:g0 + gw] = new

    @pl.when(b == nb - 1)
    def _():
        if last:
            for g0 in range(0, width, 128):
                gw = min(128, width - g0)
                h = g0 // HDIM
                if gw == HDIM:
                    den = l_sc[h]
                else:
                    lane = lax.broadcasted_iota(jnp.int32, (1, gw), 1)
                    den = jnp.where(lane < HDIM, l_sc[h], l_sc[h + 1])
                outs[0][:, g0:g0 + gw] = (a_sc[:, g0:g0 + gw] / den).astype(outs[0].dtype)
        else:
            outs[0][...] = m_sc[...]
            outs[1][...] = l_sc[...]
            outs[2][...] = a_sc[...]


def attend_chunk(info, queries, kv, state, *, kind, reqs, total, last, part=(0, 1)):
    tok, full_width = queries.shape
    index, nparts = part
    width = full_width // nparts
    heads = width // HDIM
    nb2, tk, _ = kv.shape
    nb = nb2 // 2
    tq = min(tok, 256)
    first = state is None
    kernel = functools.partial(
        attn_kernel, kind=kind, heads=heads, reqs=reqs, tq=tq, tk=tk, total=total, first=first, last=last
    )
    q_spec = pl.BlockSpec((tq, width), lambda qi, b, info: (qi, index))
    k_spec = pl.BlockSpec((1, tk, width), lambda qi, b, info: (b, 0, index))
    v_spec = pl.BlockSpec((1, tk, width), lambda qi, b, info: (nb + b, 0, index))
    ml_spec = pl.BlockSpec((heads, tq, 1), lambda qi, b, info: (index, qi, 0))
    in_specs = [q_spec, k_spec, v_spec]
    args = [queries, kv, kv]
    if not first:
        in_specs += [ml_spec, ml_spec, q_spec]
        args += list(state)
    if last:
        out_shape = jax.ShapeDtypeStruct((tok, width), jnp.bfloat16)
        out_specs = pl.BlockSpec((tq, width), lambda qi, b, info: (qi, 0))
    else:
        out_shape = (
            jax.ShapeDtypeStruct((heads, tok, 1), jnp.float32),
            jax.ShapeDtypeStruct((heads, tok, 1), jnp.float32),
            jax.ShapeDtypeStruct((tok, width), jnp.float32),
        )
        out_specs = (ml_spec, ml_spec, q_spec)
    flops = 32 * 4 * tok * nb * tk * width * 2
    cost = pl.CostEstimate(
        flops=flops,
        transcendentals=tok * nb * tk * heads,
        bytes_accessed=2 * (tok * width * 2 + 2 * nb * tk * width * 2 + tok * width * 4),
    )
    return pl.pallas_call(
        kernel,
        out_shape=out_shape,
        grid_spec=pltpu.PrefetchScalarGridSpec(
            num_scalar_prefetch=1,
            grid=(tok // tq, nb),
            in_specs=in_specs,
            out_specs=out_specs,
            scratch_shapes=[
                pltpu.VMEM((heads, tq, 1), jnp.float32),
                pltpu.VMEM((heads, tq, 1), jnp.float32),
                pltpu.VMEM((tq, width), jnp.float32),
            ],
        ),
        compiler_params=pltpu.CompilerParams(dimension_semantics=("arbitrary", "arbitrary")),
        cost_estimate=cost,
    )(info, *args)


def local(q_img, k_img, v_img, text_keys, text_values, text_lengths, img_lengths, out_weight):
    tok_dev = q_img.shape[1]
    width = q_img.shape[2]
    reqs = text_keys.shape[1]
    text_slots = text_keys.shape[2]
    nseq = lax.axis_size("seq")
    me = lax.axis_index("seq")
    total = tok_dev * nseq
    longest = total // 2
    reach = min(nseq - 1, (longest + tok_dev - 2) // tok_dev)
    ends = jnp.cumsum(img_lengths).astype(jnp.int32)
    queries = q_img[0]

    def info_for(kstart):
        head = jnp.stack([me * tok_dev, kstart]).astype(jnp.int32)
        return jnp.concatenate([head, ends, text_lengths[0].astype(jnp.int32)])

    pad_to = -(-text_slots // 128) * 128
    text_kv = jnp.pad(
        jnp.stack([text_keys[0], text_values[0]]), ((0, 0), (0, 0), (0, pad_to - text_slots), (0, 0))
    ).reshape(2 * reqs, pad_to, width)
    tk = min(tok_dev, 256)

    def as_blocks(x):
        return x.reshape(2 * tok_dev // tk, tk, width)

    common = dict(reqs=reqs, total=total)
    state = attend_chunk(info_for(0), queries, text_kv, None, kind="text", last=False, **common)
    both = jnp.stack([k_img[0], v_img[0]])
    chunks = [(both, me * tok_dev)]
    for step in range(1, reach + 1):
        to_right = [(i, i + step) for i in range(nseq - step)]
        to_left = [(i + step, i) for i in range(nseq - step)]
        for pairs, sign in ((to_right, -1), (to_left, 1)):
            chunks.append((lax.ppermute(both, "seq", pairs), (me + sign * step) * tok_dev))
    for kv, lower in chunks[:-1]:
        state = attend_chunk(info_for(lower), queries, as_blocks(kv), state, kind="image", last=False, **common)
    kv, lower = chunks[-1]
    nhead = lax.axis_size("head")
    nparts = 2 if nhead == 2 and width % 256 == 0 else 1
    attn_parts = [
        attend_chunk(
            info_for(lower), queries, as_blocks(kv), state, kind="image", last=True, part=(i, nparts), **common
        )
        for i in range(nparts)
    ]
    own_cfg = lax.axis_index("cfg")
    cols = out_weight.shape[1]
    half = cols // 2
    mine_weight = jnp.where(own_cfg == 0, guidance, 1.0 - guidance)
    w_keep = lax.dynamic_slice_in_dim(out_weight, own_cfg * half, half, 1)
    w_out = lax.dynamic_slice_in_dim(out_weight, (1 - own_cfg) * half, half, 1)
    if nhead == 2:
        hx = lax.axis_index("head")
        others = [partner_2(x, "head", 0) for x in attn_parts]
        piece = width // nparts

        def project(w):
            own = None
            for i, x in enumerate(attn_parts):
                term = jnp.dot(
                    x, lax.dynamic_slice_in_dim(w, hx * width + i * piece, piece, 0),
                    preferred_element_type=jnp.float32,
                )
                own = term if own is None else own + term
            summed = lax.optimization_barrier(own)
            for i, x in enumerate(others):
                summed = summed + jnp.dot(
                    x, lax.dynamic_slice_in_dim(w, (1 - hx) * width + i * piece, piece, 0),
                    preferred_element_type=jnp.float32,
                )
            return summed
    else:
        gathered = lax.all_gather(jnp.concatenate(attn_parts, axis=1), "head", axis=1, tiled=True)

        def project(w):
            return jnp.dot(gathered, w, preferred_element_type=jnp.float32)

    outgoing = project(w_out)
    partner = partner_2(outgoing.astype(jnp.bfloat16), "cfg", 0).astype(outgoing.dtype)
    keep = project(w_keep)
    guided = mine_weight * keep + (1.0 - mine_weight) * partner
    return guided.astype(jnp.bfloat16)


def solution(mesh):
    placed = (
        P("cfg", ("groups", "seq"), "head"),
        P("cfg", ("groups", "seq"), "head"),
        P("cfg", ("groups", "seq"), "head"),
        P("cfg", "groups", None, "head"),
        P("cfg", "groups", None, "head"),
        P("cfg", "groups"),
        P("groups"),
        P(None, "head"),
    )
    return jax.shard_map(
        local,
        mesh=mesh,
        in_specs=placed,
        out_specs=P(("groups", "seq"), ("head", "cfg")),
        check_vma=False,
    )
```

```python
import functools

import jax
import jax.numpy as jnp
from jax import lax
from jax.experimental import pallas as pl
from jax.experimental.pallas import tpu as pltpu
from jax.sharding import PartitionSpec as P

HDIM = 64


guidance = 4.0
score_scale = 0.125
neg_large = -1e30


def partner_2(x, axis, distance):
    return lax.ppermute(x, axis, [(i, i ^ 1 << distance) for i in range(lax.axis_size(axis))])


def seg_scalar(info_ref, pos, reqs):
    seg = jnp.int32(0)
    for r in range(reqs):
        seg = seg + jnp.where(pos >= info_ref[2 + r], 1, 0).astype(jnp.int32)
    return seg


def seg_vector(info_ref, pos, reqs):
    seg = jnp.zeros(pos.shape, jnp.int32)
    for r in range(reqs):
        seg = seg + (pos >= info_ref[2 + r]).astype(jnp.int32)
    return seg


def attn_kernel(info_ref, q_ref, k_ref, v_ref, *refs, kind, heads, reqs, tq, tk, total, first, last):
    if first:
        ins, outs = (), refs[:-3]
    else:
        ins, outs = refs[:3], refs[3:-3]
    m_sc, l_sc, a_sc = refs[-3:]
    qi = pl.program_id(0)
    b = pl.program_id(1)
    nb = pl.num_programs(1)
    width = heads * HDIM

    @pl.when(b == 0)
    def _():
        if first:
            m_sc[...] = jnp.full(m_sc.shape, neg_large, jnp.float32)
            l_sc[...] = jnp.zeros(l_sc.shape, jnp.float32)
            a_sc[...] = jnp.zeros(a_sc.shape, jnp.float32)
        else:
            m_sc[...] = ins[0][...]
            l_sc[...] = ins[1][...]
            a_sc[...] = ins[2][...]

    qpos0 = info_ref[0] + qi * tq
    qlo = seg_scalar(info_ref, qpos0, reqs)
    qhi = seg_scalar(info_ref, qpos0 + tq - 1, reqs)
    if kind == "text":
        active = (qlo <= b) & (b <= qhi)
    else:
        kpos0 = info_ref[1] + b * tk
        klo = seg_scalar(info_ref, kpos0, reqs)
        khi = seg_scalar(info_ref, kpos0 + tk - 1, reqs)
        active = (kpos0 >= 0) & (kpos0 < total) & (klo <= qhi) & (qlo <= khi)

    @pl.when(active)
    def _():
        qseg = seg_vector(info_ref, qpos0 + lax.broadcasted_iota(jnp.int32, (tq, 1), 0), reqs)
        col = lax.broadcasted_iota(jnp.int32, (1, tk), 1)
        if kind == "text":
            mask = (qseg == b) & (col < info_ref[2 + reqs + b])
        else:
            mask = qseg == seg_vector(info_ref, kpos0 + col, reqs)
        for g0 in range(0, width, 128):
            gw = min(128, width - g0)
            qg = q_ref[:, g0:g0 + gw]
            kg = k_ref[0, :, g0:g0 + gw]
            vg = v_ref[0, :, g0:g0 + gw]
            acc = a_sc[:, g0:g0 + gw]
            lane = lax.broadcasted_iota(jnp.int32, (1, gw), 1)
            lo = lane < HDIM
            parts = []
            for i in range(gw // HDIM):
                h = g0 // HDIM + i
                if gw == HDIM:
                    qh = qg
                else:
                    qh = jnp.where(lo if i == 0 else jnp.logical_not(lo), qg, jnp.zeros_like(qg))
                s = lax.dot_general(
                    qh, kg, (((1,), (1,)), ((), ())), preferred_element_type=jnp.float32
                ) * score_scale
                s = jnp.where(mask, s, neg_large)
                m_old = m_sc[h]
                m_new = jnp.maximum(m_old, jnp.max(s, axis=1, keepdims=True))
                alpha = jnp.exp(m_old - m_new)
                p = jnp.exp(s - m_new)
                l_sc[h] = alpha * l_sc[h] + jnp.sum(p, axis=1, keepdims=True)
                m_sc[h] = m_new
                pv = jnp.dot(p.astype(jnp.bfloat16), vg, preferred_element_type=jnp.float32)
                parts.append(alpha * acc + pv)
            new = parts[0] if len(parts) == 1 else jnp.where(lo, parts[0], parts[1])
            a_sc[:, g0:g0 + gw] = new

    @pl.when(b == nb - 1)
    def _():
        if last:
            for g0 in range(0, width, 128):
                gw = min(128, width - g0)
                h = g0 // HDIM
                if gw == HDIM:
                    den = l_sc[h]
                else:
                    lane = lax.broadcasted_iota(jnp.int32, (1, gw), 1)
                    den = jnp.where(lane < HDIM, l_sc[h], l_sc[h + 1])
                outs[0][:, g0:g0 + gw] = (a_sc[:, g0:g0 + gw] / den).astype(outs[0].dtype)
        else:
            outs[0][...] = m_sc[...]
            outs[1][...] = l_sc[...]
            outs[2][...] = a_sc[...]


def attend_chunk(info, queries, keys, values, v_off, state, *, kind, reqs, total, last, part=(0, 1), tq=256):
    tok, full_width = queries.shape
    index, nparts = part
    width = full_width // nparts
    heads = width // HDIM
    nb = keys.shape[0] - v_off
    tk = keys.shape[1]
    tq = min(tok, tq)
    first = state is None
    kernel = functools.partial(
        attn_kernel, kind=kind, heads=heads, reqs=reqs, tq=tq, tk=tk, total=total, first=first, last=last
    )
    q_spec = pl.BlockSpec((tq, width), lambda qi, b, info: (qi, index))
    k_spec = pl.BlockSpec((1, tk, width), lambda qi, b, info: (b, 0, index))
    v_spec = pl.BlockSpec((1, tk, width), lambda qi, b, info: (v_off + b, 0, index))
    ml_spec = pl.BlockSpec((heads, tq, 1), lambda qi, b, info: (index, qi, 0))
    in_specs = [q_spec, k_spec, v_spec]
    args = [queries, keys, values]
    if not first:
        in_specs += [ml_spec, ml_spec, q_spec]
        args += list(state)
    if last:
        out_shape = jax.ShapeDtypeStruct((tok, width), jnp.bfloat16)
        out_specs = pl.BlockSpec((tq, width), lambda qi, b, info: (qi, 0))
    else:
        out_shape = (
            jax.ShapeDtypeStruct((heads, tok, 1), jnp.float32),
            jax.ShapeDtypeStruct((heads, tok, 1), jnp.float32),
            jax.ShapeDtypeStruct((tok, width), jnp.float32),
        )
        out_specs = (ml_spec, ml_spec, q_spec)
    flops = 32 * 4 * tok * nb * tk * width * 2
    cost = pl.CostEstimate(
        flops=flops,
        transcendentals=tok * nb * tk * heads,
        bytes_accessed=2 * (tok * width * 2 + 2 * nb * tk * width * 2 + tok * width * 4),
    )
    return pl.pallas_call(
        kernel,
        out_shape=out_shape,
        grid_spec=pltpu.PrefetchScalarGridSpec(
            num_scalar_prefetch=1,
            grid=(tok // tq, nb),
            in_specs=in_specs,
            out_specs=out_specs,
            scratch_shapes=[
                pltpu.VMEM((heads, tq, 1), jnp.float32),
                pltpu.VMEM((heads, tq, 1), jnp.float32),
                pltpu.VMEM((tq, width), jnp.float32),
            ],
        ),
        compiler_params=pltpu.CompilerParams(dimension_semantics=("arbitrary", "arbitrary")),
        cost_estimate=cost,
    )(info, *args)


def local(q_img, k_img, v_img, text_keys, text_values, text_lengths, img_lengths, out_weight):
    tok_dev = q_img.shape[1]
    width = q_img.shape[2]
    reqs = text_keys.shape[1]
    text_slots = text_keys.shape[2]
    nseq = lax.axis_size("seq")
    me = lax.axis_index("seq")
    total = tok_dev * nseq
    longest = total // 2
    reach = min(nseq - 1, (longest + tok_dev - 2) // tok_dev)
    ends = jnp.cumsum(img_lengths).astype(jnp.int32)
    queries = q_img[0]

    def info_for(kstart):
        head = jnp.stack([me * tok_dev, kstart]).astype(jnp.int32)
        return jnp.concatenate([head, ends, text_lengths[0].astype(jnp.int32)])

    pad_to = -(-text_slots // 128) * 128
    pad = ((0, 0), (0, pad_to - text_slots), (0, 0))
    text_k = jnp.pad(text_keys[0], pad)
    text_v = jnp.pad(text_values[0], pad)
    tk = min(tok_dev, 256)

    def as_blocks(x):
        return x.reshape(2 * tok_dev // tk, tk, width)

    common = dict(reqs=reqs, total=total)
    state = attend_chunk(info_for(0), queries, text_k, text_v, 0, None, kind="text", last=False, **common)
    both = jnp.stack([k_img[0], v_img[0]])
    chunks = [(both, me * tok_dev)]
    for step in range(1, reach + 1):
        to_right = [(i, i + step) for i in range(nseq - step)]
        to_left = [(i + step, i) for i in range(nseq - step)]
        for pairs, sign in ((to_right, -1), (to_left, 1)):
            chunks.append((lax.ppermute(both, "seq", pairs), (me + sign * step) * tok_dev))
    for index, (kv, lower) in enumerate(chunks[:-1]):
        blocks = as_blocks(kv)
        state = attend_chunk(
            info_for(lower), queries, blocks, blocks, tok_dev // tk, state, kind="image", last=False,
            tq=tok_dev if index == 0 else tk, **common,
        )
    kv, lower = chunks[-1]
    nhead = lax.axis_size("head")
    nparts = 2 if nhead == 2 and width % 256 == 0 else 1
    attn_parts = [
        attend_chunk(
            info_for(lower), queries, as_blocks(kv), as_blocks(kv), tok_dev // tk, state, kind="image", last=True,
            part=(i, nparts), **common,
        )
        for i in range(nparts)
    ]
    own_cfg = lax.axis_index("cfg")
    cols = out_weight.shape[1]
    half = cols // 2
    mine_weight = jnp.where(own_cfg == 0, guidance, 1.0 - guidance)
    w_keep = lax.dynamic_slice_in_dim(out_weight, own_cfg * half, half, 1)
    w_out = lax.dynamic_slice_in_dim(out_weight, (1 - own_cfg) * half, half, 1)
    if nhead == 2:
        hx = lax.axis_index("head")
        others = [partner_2(x, "head", 0) for x in attn_parts]
        piece = width // nparts

        def project(w):
            own = None
            for i, x in enumerate(attn_parts):
                term = jnp.dot(
                    x, lax.dynamic_slice_in_dim(w, hx * width + i * piece, piece, 0),
                    preferred_element_type=jnp.float32,
                )
                own = term if own is None else own + term
            summed = lax.optimization_barrier(own)
            for i, x in enumerate(others):
                summed = summed + jnp.dot(
                    x, lax.dynamic_slice_in_dim(w, (1 - hx) * width + i * piece, piece, 0),
                    preferred_element_type=jnp.float32,
                )
            return summed
    else:
        gathered = lax.all_gather(jnp.concatenate(attn_parts, axis=1), "head", axis=1, tiled=True)

        def project(w):
            return jnp.dot(gathered, w, preferred_element_type=jnp.float32)

    outgoing = project(w_out)
    partner = partner_2(outgoing.astype(jnp.bfloat16), "cfg", 0).astype(outgoing.dtype)
    keep = project(w_keep)
    guided = mine_weight * keep + (1.0 - mine_weight) * partner
    return guided.astype(jnp.bfloat16)


def solution(mesh):
    placed = (
        P("cfg", ("groups", "seq"), "head"),
        P("cfg", ("groups", "seq"), "head"),
        P("cfg", ("groups", "seq"), "head"),
        P("cfg", "groups", None, "head"),
        P("cfg", "groups", None, "head"),
        P("cfg", "groups"),
        P("groups"),
        P(None, "head"),
    )
    return jax.shard_map(
        local,
        mesh=mesh,
        in_specs=placed,
        out_specs=P(("groups", "seq"), ("head", "cfg")),
        check_vma=False,
    )
```

```python
import functools

import jax
import jax.numpy as jnp
from jax import lax
from jax.experimental import pallas as pl
from jax.experimental.pallas import tpu as pltpu
from jax.sharding import PartitionSpec as P

HDIM = 64


guidance = 4.0
score_scale = 0.125
neg_large = -1e30


def partner_2(x, axis, distance):
    return lax.ppermute(x, axis, [(i, i ^ 1 << distance) for i in range(lax.axis_size(axis))])


def seg_scalar(info_ref, pos, reqs):
    seg = jnp.int32(0)
    for r in range(reqs):
        seg = seg + jnp.where(pos >= info_ref[2 + r], 1, 0).astype(jnp.int32)
    return seg


def seg_vector(info_ref, pos, reqs):
    seg = jnp.zeros(pos.shape, jnp.int32)
    for r in range(reqs):
        seg = seg + (pos >= info_ref[2 + r]).astype(jnp.int32)
    return seg


def attn_kernel(info_ref, q_ref, k_ref, v_ref, *refs, kind, heads, reqs, tq, tk, total, first, last):
    if first:
        ins, outs = (), refs[:-3]
    else:
        ins, outs = refs[:3], refs[3:-3]
    m_sc, l_sc, a_sc = refs[-3:]
    qi = pl.program_id(0)
    b = pl.program_id(1)
    nb = pl.num_programs(1)
    width = heads * HDIM

    @pl.when(b == 0)
    def _():
        if first:
            m_sc[...] = jnp.full(m_sc.shape, neg_large, jnp.float32)
            l_sc[...] = jnp.zeros(l_sc.shape, jnp.float32)
            a_sc[...] = jnp.zeros(a_sc.shape, jnp.float32)
        else:
            m_sc[...] = ins[0][...]
            l_sc[...] = ins[1][...]
            a_sc[...] = ins[2][...]

    qpos0 = info_ref[0] + qi * tq
    qlo = seg_scalar(info_ref, qpos0, reqs)
    qhi = seg_scalar(info_ref, qpos0 + tq - 1, reqs)
    if kind == "text":
        active = (qlo <= b) & (b <= qhi)
    else:
        kpos0 = info_ref[1] + b * tk
        klo = seg_scalar(info_ref, kpos0, reqs)
        khi = seg_scalar(info_ref, kpos0 + tk - 1, reqs)
        active = (kpos0 >= 0) & (kpos0 < total) & (klo <= qhi) & (qlo <= khi)

    @pl.when(active)
    def _():
        qseg = seg_vector(info_ref, qpos0 + lax.broadcasted_iota(jnp.int32, (tq, 1), 0), reqs)
        col = lax.broadcasted_iota(jnp.int32, (1, tk), 1)
        if kind == "text":
            mask = (qseg == b) & (col < info_ref[2 + reqs + b])
        else:
            mask = qseg == seg_vector(info_ref, kpos0 + col, reqs)
        for g0 in range(0, width, 128):
            gw = min(128, width - g0)
            qg = q_ref[:, g0:g0 + gw]
            kg = k_ref[0, :, g0:g0 + gw]
            vg = v_ref[0, :, g0:g0 + gw]
            acc = a_sc[:, g0:g0 + gw]
            lane = lax.broadcasted_iota(jnp.int32, (1, gw), 1)
            lo = lane < HDIM
            parts = []
            for i in range(gw // HDIM):
                h = g0 // HDIM + i
                if gw == HDIM:
                    qh = qg
                else:
                    qh = jnp.where(lo if i == 0 else jnp.logical_not(lo), qg, jnp.zeros_like(qg))
                s = lax.dot_general(
                    qh, kg, (((1,), (1,)), ((), ())), preferred_element_type=jnp.float32
                ) * score_scale
                s = jnp.where(mask, s, neg_large)
                m_old = m_sc[h]
                m_new = jnp.maximum(m_old, jnp.max(s, axis=1, keepdims=True))
                alpha = jnp.exp(m_old - m_new)
                p = jnp.exp(s - m_new)
                l_sc[h] = alpha * l_sc[h] + jnp.sum(p, axis=1, keepdims=True)
                m_sc[h] = m_new
                pv = jnp.dot(p.astype(jnp.bfloat16), vg, preferred_element_type=jnp.float32)
                parts.append(alpha * acc + pv)
            new = parts[0] if len(parts) == 1 else jnp.where(lo, parts[0], parts[1])
            a_sc[:, g0:g0 + gw] = new

    @pl.when(b == nb - 1)
    def _():
        if last:
            for g0 in range(0, width, 128):
                gw = min(128, width - g0)
                h = g0 // HDIM
                if gw == HDIM:
                    den = l_sc[h]
                else:
                    lane = lax.broadcasted_iota(jnp.int32, (1, gw), 1)
                    den = jnp.where(lane < HDIM, l_sc[h], l_sc[h + 1])
                outs[0][:, g0:g0 + gw] = (a_sc[:, g0:g0 + gw] / den).astype(outs[0].dtype)
        else:
            outs[0][...] = m_sc[...]
            outs[1][...] = l_sc[...]
            outs[2][...] = a_sc[...]


def attend_chunk(info, queries, keys, values, v_off, state, *, kind, reqs, total, last, part=(0, 1), tq=256):
    tok, full_width = queries.shape
    index, nparts = part
    width = full_width // nparts
    heads = width // HDIM
    nb = keys.shape[0] - v_off
    tk = keys.shape[1]
    tq = min(tok, tq)
    first = state is None
    kernel = functools.partial(
        attn_kernel, kind=kind, heads=heads, reqs=reqs, tq=tq, tk=tk, total=total, first=first, last=last
    )
    q_spec = pl.BlockSpec((tq, width), lambda qi, b, info: (qi, index))

    def kv_block(qi, b, info):
        qpos0 = info[0] + qi * tq
        qlo = seg_scalar(info, qpos0, reqs)
        qhi = seg_scalar(info, qpos0 + tq - 1, reqs)
        if kind == "text":
            lo, hi = qlo, qhi
        else:
            seg_start = jnp.where(qlo == 0, 0, info[2 + jnp.maximum(qlo - 1, 0)])
            seg_end = info[2 + jnp.minimum(qhi, reqs - 1)]
            lo = (seg_start - info[1]) // tk
            hi = (seg_end - 1 - info[1]) // tk
        lo = jnp.clip(lo, 0, nb - 1)
        hi = jnp.clip(hi, 0, nb - 1)
        return jnp.minimum(jnp.maximum(b, lo), hi)

    k_spec = pl.BlockSpec((1, tk, width), lambda qi, b, info: (kv_block(qi, b, info), 0, index))
    v_spec = pl.BlockSpec((1, tk, width), lambda qi, b, info: (v_off + kv_block(qi, b, info), 0, index))
    ml_spec = pl.BlockSpec((heads, tq, 1), lambda qi, b, info: (index, qi, 0))
    in_specs = [q_spec, k_spec, v_spec]
    args = [queries, keys, values]
    if not first:
        in_specs += [ml_spec, ml_spec, q_spec]
        args += list(state)
    if last:
        out_shape = jax.ShapeDtypeStruct((tok, width), jnp.bfloat16)
        out_specs = pl.BlockSpec((tq, width), lambda qi, b, info: (qi, 0))
    else:
        out_shape = (
            jax.ShapeDtypeStruct((heads, tok, 1), jnp.float32),
            jax.ShapeDtypeStruct((heads, tok, 1), jnp.float32),
            jax.ShapeDtypeStruct((tok, width), jnp.float32),
        )
        out_specs = (ml_spec, ml_spec, q_spec)
    flops = 32 * 4 * tok * nb * tk * width * 2
    cost = pl.CostEstimate(
        flops=flops,
        transcendentals=tok * nb * tk * heads,
        bytes_accessed=2 * (tok * width * 2 + 2 * nb * tk * width * 2 + tok * width * 4),
    )
    return pl.pallas_call(
        kernel,
        out_shape=out_shape,
        grid_spec=pltpu.PrefetchScalarGridSpec(
            num_scalar_prefetch=1,
            grid=(tok // tq, nb),
            in_specs=in_specs,
            out_specs=out_specs,
            scratch_shapes=[
                pltpu.VMEM((heads, tq, 1), jnp.float32),
                pltpu.VMEM((heads, tq, 1), jnp.float32),
                pltpu.VMEM((tq, width), jnp.float32),
            ],
        ),
        compiler_params=pltpu.CompilerParams(dimension_semantics=("arbitrary", "arbitrary")),
        cost_estimate=cost,
    )(info, *args)


def local(q_img, k_img, v_img, text_keys, text_values, text_lengths, img_lengths, out_weight):
    tok_dev = q_img.shape[1]
    width = q_img.shape[2]
    reqs = text_keys.shape[1]
    text_slots = text_keys.shape[2]
    nseq = lax.axis_size("seq")
    me = lax.axis_index("seq")
    total = tok_dev * nseq
    longest = total // 2
    reach = min(nseq - 1, (longest + tok_dev - 2) // tok_dev)
    ends = jnp.cumsum(img_lengths).astype(jnp.int32)
    queries = q_img[0]

    def info_for(kstart):
        head = jnp.stack([me * tok_dev, kstart]).astype(jnp.int32)
        return jnp.concatenate([head, ends, text_lengths[0].astype(jnp.int32)])

    pad_to = -(-text_slots // 128) * 128
    pad = ((0, 0), (0, pad_to - text_slots), (0, 0))
    text_k = jnp.pad(text_keys[0], pad)
    text_v = jnp.pad(text_values[0], pad)
    tk = min(tok_dev, 256)

    def as_blocks(x):
        return x.reshape(2 * tok_dev // tk, tk, width)

    common = dict(reqs=reqs, total=total)
    state = attend_chunk(info_for(0), queries, text_k, text_v, 0, None, kind="text", last=False, **common)
    both = jnp.stack([k_img[0], v_img[0]])
    chunks = [(both, me * tok_dev)]
    for step in range(1, reach + 1):
        to_right = [(i, i + step) for i in range(nseq - step)]
        to_left = [(i + step, i) for i in range(nseq - step)]
        for pairs, sign in ((to_right, -1), (to_left, 1)):
            chunks.append((lax.ppermute(both, "seq", pairs), (me + sign * step) * tok_dev))
    for index, (kv, lower) in enumerate(chunks[:-1]):
        blocks = as_blocks(kv)
        state = attend_chunk(
            info_for(lower), queries, blocks, blocks, tok_dev // tk, state, kind="image", last=False,
            tq=tok_dev if index == 0 else tk, **common,
        )
    kv, lower = chunks[-1]
    nhead = lax.axis_size("head")
    nparts = 2 if nhead == 2 and width % 256 == 0 else 1
    attn_parts = [
        attend_chunk(
            info_for(lower), queries, as_blocks(kv), as_blocks(kv), tok_dev // tk, state, kind="image", last=True,
            part=(i, nparts), **common,
        )
        for i in range(nparts)
    ]
    own_cfg = lax.axis_index("cfg")
    cols = out_weight.shape[1]
    half = cols // 2
    mine_weight = jnp.where(own_cfg == 0, guidance, 1.0 - guidance)
    w_keep = lax.dynamic_slice_in_dim(out_weight, own_cfg * half, half, 1)
    w_out = lax.dynamic_slice_in_dim(out_weight, (1 - own_cfg) * half, half, 1)
    if nhead == 2:
        hx = lax.axis_index("head")
        others = [partner_2(x, "head", 0) for x in attn_parts]
        piece = width // nparts

        def project(w):
            own = None
            for i, x in enumerate(attn_parts):
                term = jnp.dot(
                    x, lax.dynamic_slice_in_dim(w, hx * width + i * piece, piece, 0),
                    preferred_element_type=jnp.float32,
                )
                own = term if own is None else own + term
            summed = lax.optimization_barrier(own)
            for i, x in enumerate(others):
                summed = summed + jnp.dot(
                    x, lax.dynamic_slice_in_dim(w, (1 - hx) * width + i * piece, piece, 0),
                    preferred_element_type=jnp.float32,
                )
            return summed
    else:
        gathered = lax.all_gather(jnp.concatenate(attn_parts, axis=1), "head", axis=1, tiled=True)

        def project(w):
            return jnp.dot(gathered, w, preferred_element_type=jnp.float32)

    outgoing = project(w_out)
    partner = partner_2(outgoing.astype(jnp.bfloat16), "cfg", 0).astype(outgoing.dtype)
    keep = project(w_keep)
    guided = mine_weight * keep + (1.0 - mine_weight) * partner
    return guided.astype(jnp.bfloat16)


def solution(mesh):
    placed = (
        P("cfg", ("groups", "seq"), "head"),
        P("cfg", ("groups", "seq"), "head"),
        P("cfg", ("groups", "seq"), "head"),
        P("cfg", "groups", None, "head"),
        P("cfg", "groups", None, "head"),
        P("cfg", "groups"),
        P("groups"),
        P(None, "head"),
    )
    return jax.shard_map(
        local,
        mesh=mesh,
        in_specs=placed,
        out_specs=P(("groups", "seq"), ("head", "cfg")),
        check_vma=False,
    )
```

```python
import functools

import jax
import jax.numpy as jnp
from jax import lax
from jax.experimental import pallas as pl
from jax.experimental.pallas import tpu as pltpu
from jax.sharding import PartitionSpec as P

HDIM = 64


guidance = 4.0
score_scale = 0.125
neg_large = -1e30


def partner_2(x, axis, distance):
    return lax.ppermute(x, axis, [(i, i ^ 1 << distance) for i in range(lax.axis_size(axis))])


def seg_scalar(info_ref, pos, reqs):
    seg = jnp.int32(0)
    for r in range(reqs):
        seg = seg + jnp.where(pos >= info_ref[2 + r], 1, 0).astype(jnp.int32)
    return seg


def seg_vector(info_ref, pos, reqs):
    seg = jnp.zeros(pos.shape, jnp.int32)
    for r in range(reqs):
        seg = seg + (pos >= info_ref[2 + r]).astype(jnp.int32)
    return seg


def attn_kernel(info_ref, q_ref, k_ref, v_ref, *refs, kind, heads, reqs, tq, tk, total, first, last, sub):
    if first:
        ins, outs = (), refs[:-3]
    else:
        ins, outs = refs[:3], refs[3:-3]
    m_sc, l_sc, a_sc = refs[-3:]
    qi = pl.program_id(0)
    b = pl.program_id(1)
    nb = pl.num_programs(1)
    width = heads * HDIM

    @pl.when(b == 0)
    def _():
        if first:
            m_sc[...] = jnp.full(m_sc.shape, neg_large, jnp.float32)
            l_sc[...] = jnp.zeros(l_sc.shape, jnp.float32)
            a_sc[...] = jnp.zeros(a_sc.shape, jnp.float32)
        else:
            m_sc[...] = ins[0][...]
            l_sc[...] = ins[1][...]
            a_sc[...] = ins[2][...]

    qpos0 = info_ref[0] + qi * tq
    qlo = seg_scalar(info_ref, qpos0, reqs)
    qhi = seg_scalar(info_ref, qpos0 + tq - 1, reqs)
    if kind == "text":
        req = b // sub
        offset = (b % sub) * tk
        active = (qlo <= req) & (req <= qhi) & (offset < info_ref[2 + reqs + req])
    else:
        kpos0 = info_ref[1] + b * tk
        klo = seg_scalar(info_ref, kpos0, reqs)
        khi = seg_scalar(info_ref, kpos0 + tk - 1, reqs)
        active = (kpos0 >= 0) & (kpos0 < total) & (klo <= qhi) & (qlo <= khi)

    @pl.when(active)
    def _():
        qseg = seg_vector(info_ref, qpos0 + lax.broadcasted_iota(jnp.int32, (1, tq), 1), reqs)
        row = lax.broadcasted_iota(jnp.int32, (tk, 1), 0)
        if kind == "text":
            mask = (row + offset < info_ref[2 + reqs + req]) & (qseg == req)
        else:
            mask = seg_vector(info_ref, kpos0 + row, reqs) == qseg
        for g0 in range(0, width, 128):
            gw = min(128, width - g0)
            qg = q_ref[:, g0:g0 + gw]
            kg = k_ref[0, :, g0:g0 + gw]
            vt = v_ref[0, :, g0:g0 + gw].T
            lane = lax.broadcasted_iota(jnp.int32, (1, gw), 1)
            sub = lax.broadcasted_iota(jnp.int32, (gw, 1), 0) < HDIM
            acc = a_sc[g0:g0 + gw, :]
            parts = []
            for i in range(gw // HDIM):
                h = g0 // HDIM + i
                if gw == HDIM:
                    kh = kg
                else:
                    kh = jnp.where((lane < HDIM) if i == 0 else (lane >= HDIM), kg, jnp.zeros_like(kg))
                st = lax.dot_general(
                    kh, qg, (((1,), (1,)), ((), ())), preferred_element_type=jnp.float32
                ) * score_scale
                st = jnp.where(mask, st, neg_large)
                m_old = m_sc[h]
                m_new = jnp.maximum(m_old, jnp.max(st, axis=0, keepdims=True))
                alpha = jnp.exp(m_old - m_new)
                pt = jnp.exp(st - m_new)
                l_sc[h] = alpha * l_sc[h] + jnp.sum(pt, axis=0, keepdims=True)
                m_sc[h] = m_new
                pv = jnp.dot(vt, pt.astype(jnp.bfloat16), preferred_element_type=jnp.float32)
                parts.append(alpha * acc + pv)
            new = parts[0] if len(parts) == 1 else jnp.where(sub, parts[0], parts[1])
            a_sc[g0:g0 + gw, :] = new

    @pl.when(b == nb - 1)
    def _():
        if last:
            for g0 in range(0, width, 128):
                gw = min(128, width - g0)
                h = g0 // HDIM
                if gw == HDIM:
                    den = l_sc[h]
                else:
                    sub = lax.broadcasted_iota(jnp.int32, (gw, 1), 0) < HDIM
                    den = jnp.where(sub, l_sc[h], l_sc[h + 1])
                outs[0][g0:g0 + gw, :] = (a_sc[g0:g0 + gw, :] / den).astype(outs[0].dtype)
        else:
            outs[0][...] = m_sc[...]
            outs[1][...] = l_sc[...]
            outs[2][...] = a_sc[...]


def attend_chunk(info, queries, keys, values, v_off, state, *, kind, reqs, total, last, part=(0, 1), tq=256, sub=1):
    tok, full_width = queries.shape
    index, nparts = part
    width = full_width // nparts
    heads = width // HDIM
    nb = keys.shape[0] - v_off
    tk = keys.shape[1]
    tq = min(tok, tq)
    first = state is None
    kernel = functools.partial(
        attn_kernel, kind=kind, heads=heads, reqs=reqs, tq=tq, tk=tk, total=total, first=first, last=last, sub=sub
    )
    q_spec = pl.BlockSpec((tq, width), lambda qi, b, info: (qi, index))
    k_spec = pl.BlockSpec((1, tk, width), lambda qi, b, info: (b, 0, index))
    v_spec = pl.BlockSpec((1, tk, width), lambda qi, b, info: (v_off + b, 0, index))
    ml_spec = pl.BlockSpec((heads, 1, tq), lambda qi, b, info: (index, 0, qi))
    acc_spec = pl.BlockSpec((width, tq), lambda qi, b, info: (index, qi))
    in_specs = [q_spec, k_spec, v_spec]
    args = [queries, keys, values]
    if not first:
        in_specs += [ml_spec, ml_spec, acc_spec]
        args += list(state)
    if last:
        out_shape = jax.ShapeDtypeStruct((width, tok), jnp.bfloat16)
        out_specs = pl.BlockSpec((width, tq), lambda qi, b, info: (0, qi))
    else:
        out_shape = (
            jax.ShapeDtypeStruct((heads * nparts, 1, tok), jnp.float32),
            jax.ShapeDtypeStruct((heads * nparts, 1, tok), jnp.float32),
            jax.ShapeDtypeStruct((width * nparts, tok), jnp.float32),
        )
        out_specs = (ml_spec, ml_spec, acc_spec)
    flops = 32 * 4 * tok * nb * tk * width * 2
    cost = pl.CostEstimate(
        flops=flops,
        transcendentals=tok * nb * tk * heads,
        bytes_accessed=2 * (tok * width * 2 + 2 * nb * tk * width * 2 + tok * width * 4),
    )
    return pl.pallas_call(
        kernel,
        out_shape=out_shape,
        grid_spec=pltpu.PrefetchScalarGridSpec(
            num_scalar_prefetch=1,
            grid=(tok // tq, nb),
            in_specs=in_specs,
            out_specs=out_specs,
            scratch_shapes=[
                pltpu.VMEM((heads, 1, tq), jnp.float32),
                pltpu.VMEM((heads, 1, tq), jnp.float32),
                pltpu.VMEM((width, tq), jnp.float32),
            ],
        ),
        compiler_params=pltpu.CompilerParams(dimension_semantics=("arbitrary", "arbitrary")),
        cost_estimate=cost,
    )(info, *args)


def local(q_img, k_img, v_img, text_keys, text_values, text_lengths, img_lengths, out_weight):
    tok_dev = q_img.shape[1]
    width = q_img.shape[2]
    reqs = text_keys.shape[1]
    text_slots = text_keys.shape[2]
    nseq = lax.axis_size("seq")
    me = lax.axis_index("seq")
    total = tok_dev * nseq
    longest = total // 2
    reach = min(nseq - 1, (longest + tok_dev - 2) // tok_dev)
    ends = jnp.cumsum(img_lengths).astype(jnp.int32)
    queries = q_img[0]

    def info_for(kstart):
        head = jnp.stack([me * tok_dev, kstart]).astype(jnp.int32)
        return jnp.concatenate([head, ends, text_lengths[0].astype(jnp.int32)])

    pad_to = -(-text_slots // 128) * 128
    pad = ((0, 0), (0, pad_to - text_slots), (0, 0))
    tk = min(tok_dev, 128)
    sub = pad_to // tk
    text_k = jnp.pad(text_keys[0], pad).reshape(reqs * sub, tk, width)
    text_v = jnp.pad(text_values[0], pad).reshape(reqs * sub, tk, width)

    def as_blocks(x):
        return x.reshape(2 * tok_dev // tk, tk, width)

    common = dict(reqs=reqs, total=total)
    state = attend_chunk(info_for(0), queries, text_k, text_v, 0, None, kind="text", last=False, sub=sub, **common)
    both = jnp.stack([k_img[0], v_img[0]])
    chunks = [(both, me * tok_dev)]
    for step in range(1, reach + 1):
        to_right = [(i, i + step) for i in range(nseq - step)]
        to_left = [(i + step, i) for i in range(nseq - step)]
        for pairs, sign in ((to_right, -1), (to_left, 1)):
            chunks.append((lax.ppermute(both, "seq", pairs), (me + sign * step) * tok_dev))
    for index, (kv, lower) in enumerate(chunks[:-1]):
        blocks = as_blocks(kv)
        state = attend_chunk(
            info_for(lower), queries, blocks, blocks, tok_dev // tk, state, kind="image", last=False,
            **common,
        )
    kv, lower = chunks[-1]
    nhead = lax.axis_size("head")
    nparts = 2 if nhead == 2 and width % 256 == 0 else 1
    attn_parts = [
        attend_chunk(
            info_for(lower), queries, as_blocks(kv), as_blocks(kv), tok_dev // tk, state, kind="image", last=True,
            part=(i, nparts), **common,
        )
        for i in range(nparts)
    ]
    own_cfg = lax.axis_index("cfg")
    cols = out_weight.shape[1]
    half = cols // 2
    mine_weight = jnp.where(own_cfg == 0, guidance, 1.0 - guidance)
    w_keep = lax.dynamic_slice_in_dim(out_weight, own_cfg * half, half, 1)
    w_out = lax.dynamic_slice_in_dim(out_weight, (1 - own_cfg) * half, half, 1)
    if nhead == 2:
        hx = lax.axis_index("head")
        others = [partner_2(x, "head", 0) for x in attn_parts]
        piece = width // nparts

        def project(w):
            own = None
            for i, x in enumerate(attn_parts):
                term = lax.dot_general(
                    x, lax.dynamic_slice_in_dim(w, hx * width + i * piece, piece, 0),
                    (((0,), (0,)), ((), ())), preferred_element_type=jnp.float32,
                )
                own = term if own is None else own + term
            summed = lax.optimization_barrier(own)
            for i, x in enumerate(others):
                summed = summed + lax.dot_general(
                    x, lax.dynamic_slice_in_dim(w, (1 - hx) * width + i * piece, piece, 0),
                    (((0,), (0,)), ((), ())), preferred_element_type=jnp.float32,
                )
            return summed
    else:
        gathered = lax.all_gather(jnp.concatenate(attn_parts, axis=0), "head", axis=0, tiled=True)

        def project(w):
            return lax.dot_general(gathered, w, (((0,), (0,)), ((), ())), preferred_element_type=jnp.float32)

    outgoing = project(w_out)
    partner = partner_2(outgoing.astype(jnp.bfloat16), "cfg", 0).astype(outgoing.dtype)
    keep = project(w_keep)
    guided = mine_weight * keep + (1.0 - mine_weight) * partner
    return guided.astype(jnp.bfloat16)


def solution(mesh):
    placed = (
        P("cfg", ("groups", "seq"), "head"),
        P("cfg", ("groups", "seq"), "head"),
        P("cfg", ("groups", "seq"), "head"),
        P("cfg", "groups", None, "head"),
        P("cfg", "groups", None, "head"),
        P("cfg", "groups"),
        P("groups"),
        P(None, "head"),
    )
    return jax.shard_map(
        local,
        mesh=mesh,
        in_specs=placed,
        out_specs=P(("groups", "seq"), ("head", "cfg")),
        check_vma=False,
    )
```

```python
import functools

import jax
import jax.numpy as jnp
from jax import lax
from jax.experimental import pallas as pl
from jax.experimental.pallas import tpu as pltpu
from jax.sharding import PartitionSpec as P

HDIM = 64


guidance = 4.0
score_scale = 0.125
neg_large = -1e30


def partner_2(x, axis, distance):
    return lax.ppermute(x, axis, [(i, i ^ 1 << distance) for i in range(lax.axis_size(axis))])


def seg_scalar(info_ref, pos, reqs):
    seg = jnp.int32(0)
    for r in range(reqs):
        seg = seg + jnp.where(pos >= info_ref[2 + r], 1, 0).astype(jnp.int32)
    return seg


def seg_vector(info_ref, pos, reqs):
    seg = jnp.zeros(pos.shape, jnp.int32)
    for r in range(reqs):
        seg = seg + (pos >= info_ref[2 + r]).astype(jnp.int32)
    return seg


def attn_kernel(info_ref, q_ref, k_ref, v_ref, *refs, kind, heads, reqs, tq, tk, total, first, last, sub):
    if first:
        ins, outs = (), refs[:-3]
    else:
        ins, outs = refs[:3], refs[3:-3]
    m_sc, l_sc, a_sc = refs[-3:]
    qi = pl.program_id(0)
    b = pl.program_id(1)
    nb = pl.num_programs(1)
    width = heads * HDIM

    @pl.when(b == 0)
    def _():
        if first:
            m_sc[...] = jnp.full(m_sc.shape, neg_large, jnp.float32)
            l_sc[...] = jnp.zeros(l_sc.shape, jnp.float32)
            a_sc[...] = jnp.zeros(a_sc.shape, jnp.float32)
        else:
            m_sc[...] = ins[0][...]
            l_sc[...] = ins[1][...]
            a_sc[...] = ins[2][...]

    qpos0 = info_ref[0] + qi * tq
    qlo = seg_scalar(info_ref, qpos0, reqs)
    qhi = seg_scalar(info_ref, qpos0 + tq - 1, reqs)
    if kind == "text":
        req = b // sub
        offset = (b % sub) * tk
        active = (qlo <= req) & (req <= qhi) & (offset < info_ref[2 + reqs + req])
    else:
        kpos0 = info_ref[1] + b * tk
        klo = seg_scalar(info_ref, kpos0, reqs)
        khi = seg_scalar(info_ref, kpos0 + tk - 1, reqs)
        active = (kpos0 >= 0) & (kpos0 < total) & (klo <= qhi) & (qlo <= khi)

    @pl.when(active)
    def _():
        qseg = seg_vector(info_ref, qpos0 + lax.broadcasted_iota(jnp.int32, (1, tq), 1), reqs)
        row = lax.broadcasted_iota(jnp.int32, (tk, 1), 0)
        if kind == "text":
            mask = (row + offset < info_ref[2 + reqs + req]) & (qseg == req)
        else:
            mask = seg_vector(info_ref, kpos0 + row, reqs) == qseg
        for g0 in range(0, width, 128):
            gw = min(128, width - g0)
            qg = q_ref[:, g0:g0 + gw]
            kg = k_ref[0, :, g0:g0 + gw]
            vt = v_ref[0, :, g0:g0 + gw].T
            lane = lax.broadcasted_iota(jnp.int32, (1, gw), 1)
            sub = lax.broadcasted_iota(jnp.int32, (gw, 1), 0) < HDIM
            acc = a_sc[g0:g0 + gw, :]
            parts = []
            for i in range(gw // HDIM):
                h = g0 // HDIM + i
                if gw == HDIM:
                    kh = kg
                else:
                    kh = jnp.where((lane < HDIM) if i == 0 else (lane >= HDIM), kg, jnp.zeros_like(kg))
                st = lax.dot_general(
                    kh, qg, (((1,), (1,)), ((), ())), preferred_element_type=jnp.float32
                ) * score_scale
                st = jnp.where(mask, st, neg_large)
                m_old = m_sc[h]
                m_new = jnp.maximum(m_old, jnp.max(st, axis=0, keepdims=True))
                alpha = jnp.exp(m_old - m_new)
                pt = jnp.exp(st - m_new)
                l_sc[h] = alpha * l_sc[h] + jnp.sum(pt, axis=0, keepdims=True)
                m_sc[h] = m_new
                pv = jnp.dot(vt, pt.astype(jnp.bfloat16), preferred_element_type=jnp.float32)
                parts.append(alpha * acc + pv)
            new = parts[0] if len(parts) == 1 else jnp.where(sub, parts[0], parts[1])
            a_sc[g0:g0 + gw, :] = new

    @pl.when(b == nb - 1)
    def _():
        if last:
            for g0 in range(0, width, 128):
                gw = min(128, width - g0)
                h = g0 // HDIM
                if gw == HDIM:
                    den = l_sc[h]
                else:
                    sub = lax.broadcasted_iota(jnp.int32, (gw, 1), 0) < HDIM
                    den = jnp.where(sub, l_sc[h], l_sc[h + 1])
                outs[0][g0:g0 + gw, :] = (a_sc[g0:g0 + gw, :] / den).astype(outs[0].dtype)
        else:
            outs[0][...] = m_sc[...]
            outs[1][...] = l_sc[...]
            outs[2][...] = a_sc[...]


def attend_chunk(info, queries, keys, values, v_off, state, *, kind, reqs, total, last, part=(0, 1), tq=256, sub=1):
    tok, full_width = queries.shape
    index, nparts = part
    width = full_width // nparts
    heads = width // HDIM
    nb = keys.shape[0] - v_off
    tk = keys.shape[1]
    tq = min(tok, tq)
    first = state is None
    kernel = functools.partial(
        attn_kernel, kind=kind, heads=heads, reqs=reqs, tq=tq, tk=tk, total=total, first=first, last=last, sub=sub
    )
    q_spec = pl.BlockSpec((tq, width), lambda qi, b, info: (qi, index))
    k_spec = pl.BlockSpec((1, tk, width), lambda qi, b, info: (b, 0, index))
    v_spec = pl.BlockSpec((1, tk, width), lambda qi, b, info: (v_off + b, 0, index))
    ml_spec = pl.BlockSpec((heads, 1, tq), lambda qi, b, info: (index, 0, qi))
    acc_spec = pl.BlockSpec((width, tq), lambda qi, b, info: (index, qi))
    in_specs = [q_spec, k_spec, v_spec]
    args = [queries, keys, values]
    if not first:
        in_specs += [ml_spec, ml_spec, acc_spec]
        args += list(state)
    if last:
        out_shape = jax.ShapeDtypeStruct((width, tok), jnp.bfloat16)
        out_specs = pl.BlockSpec((width, tq), lambda qi, b, info: (0, qi))
    else:
        out_shape = (
            jax.ShapeDtypeStruct((heads * nparts, 1, tok), jnp.float32),
            jax.ShapeDtypeStruct((heads * nparts, 1, tok), jnp.float32),
            jax.ShapeDtypeStruct((width * nparts, tok), jnp.float32),
        )
        out_specs = (ml_spec, ml_spec, acc_spec)
    flops = 32 * 4 * tok * nb * tk * width * 2
    cost = pl.CostEstimate(
        flops=flops,
        transcendentals=tok * nb * tk * heads,
        bytes_accessed=2 * (tok * width * 2 + 2 * nb * tk * width * 2 + tok * width * 4),
    )
    return pl.pallas_call(
        kernel,
        out_shape=out_shape,
        grid_spec=pltpu.PrefetchScalarGridSpec(
            num_scalar_prefetch=1,
            grid=(tok // tq, nb),
            in_specs=in_specs,
            out_specs=out_specs,
            scratch_shapes=[
                pltpu.VMEM((heads, 1, tq), jnp.float32),
                pltpu.VMEM((heads, 1, tq), jnp.float32),
                pltpu.VMEM((width, tq), jnp.float32),
            ],
        ),
        compiler_params=pltpu.CompilerParams(dimension_semantics=("arbitrary", "arbitrary")),
        cost_estimate=cost,
    )(info, *args)


def local(q_img, k_img, v_img, text_keys, text_values, text_lengths, img_lengths, out_weight):
    tok_dev = q_img.shape[1]
    width = q_img.shape[2]
    reqs = text_keys.shape[1]
    text_slots = text_keys.shape[2]
    nseq = lax.axis_size("seq")
    me = lax.axis_index("seq")
    total = tok_dev * nseq
    longest = total // 2
    reach = min(nseq - 1, (longest + tok_dev - 2) // tok_dev)
    ends = jnp.cumsum(img_lengths).astype(jnp.int32)
    queries = q_img[0]

    def info_for(kstart):
        head = jnp.stack([me * tok_dev, kstart]).astype(jnp.int32)
        return jnp.concatenate([head, ends, text_lengths[0].astype(jnp.int32)])

    pad_to = -(-text_slots // 128) * 128
    pad = ((0, 0), (0, pad_to - text_slots), (0, 0))
    tk = min(tok_dev, 128)
    sub = pad_to // tk
    text_k = jnp.pad(text_keys[0], pad).reshape(reqs * sub, tk, width)
    text_v = jnp.pad(text_values[0], pad).reshape(reqs * sub, tk, width)

    def as_blocks(x):
        return x.reshape(2 * tok_dev // tk, tk, width)

    common = dict(reqs=reqs, total=total)
    state = attend_chunk(info_for(0), queries, text_k, text_v, 0, None, kind="text", last=False, sub=sub, **common)
    both = jnp.stack([k_img[0], v_img[0]])
    chunks = [(both, me * tok_dev)]
    to_right = [(i, i + 1) for i in range(nseq - 1)]
    to_left = [(i + 1, i) for i in range(nseq - 1)]
    from_left, from_right = both, both
    for step in range(1, reach + 1):
        from_left = lax.ppermute(from_left, "seq", to_right)
        from_right = lax.ppermute(from_right, "seq", to_left)
        chunks.append((from_left, (me - step) * tok_dev))
        chunks.append((from_right, (me + step) * tok_dev))
    for index, (kv, lower) in enumerate(chunks[:-1]):
        blocks = as_blocks(kv)
        state = attend_chunk(
            info_for(lower), queries, blocks, blocks, tok_dev // tk, state, kind="image", last=False,
            **common,
        )
    kv, lower = chunks[-1]
    nhead = lax.axis_size("head")
    nparts = 2 if nhead == 2 and width % 256 == 0 else 1
    attn_parts = [
        attend_chunk(
            info_for(lower), queries, as_blocks(kv), as_blocks(kv), tok_dev // tk, state, kind="image", last=True,
            part=(i, nparts), **common,
        )
        for i in range(nparts)
    ]
    own_cfg = lax.axis_index("cfg")
    cols = out_weight.shape[1]
    half = cols // 2
    mine_weight = jnp.where(own_cfg == 0, guidance, 1.0 - guidance)
    w_keep = lax.dynamic_slice_in_dim(out_weight, own_cfg * half, half, 1)
    w_out = lax.dynamic_slice_in_dim(out_weight, (1 - own_cfg) * half, half, 1)
    if nhead == 2:
        hx = lax.axis_index("head")
        others = [partner_2(x, "head", 0) for x in attn_parts]
        piece = width // nparts

        def project(w):
            own = None
            for i, x in enumerate(attn_parts):
                term = lax.dot_general(
                    x, lax.dynamic_slice_in_dim(w, hx * width + i * piece, piece, 0),
                    (((0,), (0,)), ((), ())), preferred_element_type=jnp.float32,
                )
                own = term if own is None else own + term
            summed = lax.optimization_barrier(own)
            for i, x in enumerate(others):
                summed = summed + lax.dot_general(
                    x, lax.dynamic_slice_in_dim(w, (1 - hx) * width + i * piece, piece, 0),
                    (((0,), (0,)), ((), ())), preferred_element_type=jnp.float32,
                )
            return summed
    else:
        gathered = lax.all_gather(jnp.concatenate(attn_parts, axis=0), "head", axis=0, tiled=True)

        def project(w):
            return lax.dot_general(gathered, w, (((0,), (0,)), ((), ())), preferred_element_type=jnp.float32)

    outgoing = project(w_out)
    partner = partner_2(outgoing.astype(jnp.bfloat16), "cfg", 0).astype(outgoing.dtype)
    keep = project(w_keep)
    guided = mine_weight * keep + (1.0 - mine_weight) * partner
    return guided.astype(jnp.bfloat16)


def solution(mesh):
    placed = (
        P("cfg", ("groups", "seq"), "head"),
        P("cfg", ("groups", "seq"), "head"),
        P("cfg", ("groups", "seq"), "head"),
        P("cfg", "groups", None, "head"),
        P("cfg", "groups", None, "head"),
        P("cfg", "groups"),
        P("groups"),
        P(None, "head"),
    )
    return jax.shard_map(
        local,
        mesh=mesh,
        in_specs=placed,
        out_specs=P(("groups", "seq"), ("head", "cfg")),
        check_vma=False,
    )
```

```python
import functools

import jax
import jax.numpy as jnp
from jax import lax
from jax.experimental import pallas as pl
from jax.experimental.pallas import tpu as pltpu
from jax.sharding import PartitionSpec as P

HDIM = 64


guidance = 4.0
score_scale = 0.125
neg_large = -1e30


def partner_2(x, axis, distance):
    return lax.ppermute(x, axis, [(i, i ^ 1 << distance) for i in range(lax.axis_size(axis))])


def seg_scalar(info_ref, pos, reqs):
    seg = jnp.int32(0)
    for r in range(reqs):
        seg = seg + jnp.where(pos >= info_ref[2 + r], 1, 0).astype(jnp.int32)
    return seg


def seg_vector(info_ref, pos, reqs):
    seg = jnp.zeros(pos.shape, jnp.int32)
    for r in range(reqs):
        seg = seg + (pos >= info_ref[2 + r]).astype(jnp.int32)
    return seg


def attn_kernel(info_ref, q_ref, k_ref, v_ref, *refs, kind, heads, reqs, tq, tk, total, first, last, sub):
    if first:
        ins, outs = (), refs[:-3]
    else:
        ins, outs = refs[:3], refs[3:-3]
    m_sc, l_sc, a_sc = refs[-3:]
    qi = pl.program_id(0)
    b = pl.program_id(1)
    nb = pl.num_programs(1)
    width = heads * HDIM

    @pl.when(b == 0)
    def _():
        if first:
            m_sc[...] = jnp.full(m_sc.shape, neg_large, jnp.float32)
            l_sc[...] = jnp.zeros(l_sc.shape, jnp.float32)
            a_sc[...] = jnp.zeros(a_sc.shape, jnp.float32)
        else:
            m_sc[...] = ins[0][...]
            l_sc[...] = ins[1][...]
            a_sc[...] = ins[2][...]

    qpos0 = info_ref[0] + qi * tq
    qlo = seg_scalar(info_ref, qpos0, reqs)
    qhi = seg_scalar(info_ref, qpos0 + tq - 1, reqs)
    if kind == "text":
        req = b // sub
        offset = (b % sub) * tk
        active = (qlo <= req) & (req <= qhi) & (offset < info_ref[2 + reqs + req])
    else:
        kpos0 = info_ref[1] + b * tk
        klo = seg_scalar(info_ref, kpos0, reqs)
        khi = seg_scalar(info_ref, kpos0 + tk - 1, reqs)
        active = (kpos0 >= 0) & (kpos0 < total) & (klo <= qhi) & (qlo <= khi)

    @pl.when(active)
    def _():
        qseg = seg_vector(info_ref, qpos0 + lax.broadcasted_iota(jnp.int32, (1, tq), 1), reqs)
        row = lax.broadcasted_iota(jnp.int32, (tk, 1), 0)
        if kind == "text":
            mask = (row + offset < info_ref[2 + reqs + req]) & (qseg == req)
        else:
            mask = seg_vector(info_ref, kpos0 + row, reqs) == qseg
        for g0 in range(0, width, 128):
            gw = min(128, width - g0)
            qg = q_ref[:, g0:g0 + gw]
            kg = k_ref[0, :, g0:g0 + gw]
            vt = v_ref[0, :, g0:g0 + gw].T
            lane = lax.broadcasted_iota(jnp.int32, (1, gw), 1)
            sub = lax.broadcasted_iota(jnp.int32, (gw, 1), 0) < HDIM
            acc = a_sc[g0:g0 + gw, :]
            parts = []
            for i in range(gw // HDIM):
                h = g0 // HDIM + i
                if gw == HDIM:
                    kh = kg
                else:
                    kh = jnp.where((lane < HDIM) if i == 0 else (lane >= HDIM), kg, jnp.zeros_like(kg))
                st = lax.dot_general(
                    kh, qg, (((1,), (1,)), ((), ())), preferred_element_type=jnp.float32
                ) * score_scale
                st = jnp.where(mask, st, neg_large)
                m_old = m_sc[h]
                m_new = jnp.maximum(m_old, jnp.max(st, axis=0, keepdims=True))
                alpha = jnp.exp(m_old - m_new)
                pt = jnp.exp(st - m_new)
                l_sc[h] = alpha * l_sc[h] + jnp.sum(pt, axis=0, keepdims=True)
                m_sc[h] = m_new
                pv = jnp.dot(vt, pt.astype(jnp.bfloat16), preferred_element_type=jnp.float32)
                parts.append(alpha * acc + pv)
            new = parts[0] if len(parts) == 1 else jnp.where(sub, parts[0], parts[1])
            a_sc[g0:g0 + gw, :] = new

    @pl.when(b == nb - 1)
    def _():
        if last:
            for g0 in range(0, width, 128):
                gw = min(128, width - g0)
                h = g0 // HDIM
                if gw == HDIM:
                    den = l_sc[h]
                else:
                    sub = lax.broadcasted_iota(jnp.int32, (gw, 1), 0) < HDIM
                    den = jnp.where(sub, l_sc[h], l_sc[h + 1])
                outs[0][g0:g0 + gw, :] = (a_sc[g0:g0 + gw, :] / den).astype(outs[0].dtype)
        else:
            outs[0][...] = m_sc[...]
            outs[1][...] = l_sc[...]
            outs[2][...] = a_sc[...]


def attend_chunk(info, queries, keys, values, v_off, state, *, kind, reqs, total, last, part=(0, 1), tq=256, sub=1):
    tok, full_width = queries.shape
    index, nparts = part
    width = full_width // nparts
    heads = width // HDIM
    nb = keys.shape[0] - v_off
    tk = keys.shape[1]
    tq = min(tok, tq)
    first = state is None
    kernel = functools.partial(
        attn_kernel, kind=kind, heads=heads, reqs=reqs, tq=tq, tk=tk, total=total, first=first, last=last, sub=sub
    )
    q_spec = pl.BlockSpec((tq, width), lambda qi, b, info: (qi, index))
    k_spec = pl.BlockSpec((1, tk, width), lambda qi, b, info: (b, 0, index))
    v_spec = pl.BlockSpec((1, tk, width), lambda qi, b, info: (v_off + b, 0, index))
    ml_spec = pl.BlockSpec((heads, 1, tq), lambda qi, b, info: (index, 0, qi))
    acc_spec = pl.BlockSpec((width, tq), lambda qi, b, info: (index, qi))
    in_specs = [q_spec, k_spec, v_spec]
    args = [queries, keys, values]
    if not first:
        in_specs += [ml_spec, ml_spec, acc_spec]
        args += list(state)
    if last:
        out_shape = jax.ShapeDtypeStruct((width, tok), jnp.bfloat16)
        out_specs = pl.BlockSpec((width, tq), lambda qi, b, info: (0, qi))
    else:
        out_shape = (
            jax.ShapeDtypeStruct((heads * nparts, 1, tok), jnp.float32),
            jax.ShapeDtypeStruct((heads * nparts, 1, tok), jnp.float32),
            jax.ShapeDtypeStruct((width * nparts, tok), jnp.float32),
        )
        out_specs = (ml_spec, ml_spec, acc_spec)
    flops = 32 * 4 * tok * nb * tk * width * 2
    cost = pl.CostEstimate(
        flops=flops,
        transcendentals=tok * nb * tk * heads,
        bytes_accessed=2 * (tok * width * 2 + 2 * nb * tk * width * 2 + tok * width * 4),
    )
    return pl.pallas_call(
        kernel,
        out_shape=out_shape,
        grid_spec=pltpu.PrefetchScalarGridSpec(
            num_scalar_prefetch=1,
            grid=(tok // tq, nb),
            in_specs=in_specs,
            out_specs=out_specs,
            scratch_shapes=[
                pltpu.VMEM((heads, 1, tq), jnp.float32),
                pltpu.VMEM((heads, 1, tq), jnp.float32),
                pltpu.VMEM((width, tq), jnp.float32),
            ],
        ),
        compiler_params=pltpu.CompilerParams(dimension_semantics=("arbitrary", "arbitrary")),
        cost_estimate=cost,
    )(info, *args)


def local(q_img, k_img, v_img, text_keys, text_values, text_lengths, img_lengths, out_weight):
    tok_dev = q_img.shape[1]
    width = q_img.shape[2]
    reqs = text_keys.shape[1]
    text_slots = text_keys.shape[2]
    nseq = lax.axis_size("seq")
    me = lax.axis_index("seq")
    total = tok_dev * nseq
    longest = total // 2
    reach = min(nseq - 1, (longest + tok_dev - 2) // tok_dev)
    ends = jnp.cumsum(img_lengths).astype(jnp.int32)
    queries = q_img[0]

    def info_for(kstart):
        head = jnp.stack([me * tok_dev, kstart]).astype(jnp.int32)
        return jnp.concatenate([head, ends, text_lengths[0].astype(jnp.int32)])

    pad_to = -(-text_slots // 128) * 128
    pad = ((0, 0), (0, pad_to - text_slots), (0, 0))
    tk = min(tok_dev, 128)
    sub = pad_to // tk
    text_k = jnp.pad(text_keys[0], pad).reshape(reqs * sub, tk, width)
    text_v = jnp.pad(text_values[0], pad).reshape(reqs * sub, tk, width)

    def as_blocks(x):
        return x.reshape(2 * tok_dev // tk, tk, width)

    common = dict(reqs=reqs, total=total)
    state = attend_chunk(info_for(0), queries, text_k, text_v, 0, None, kind="text", last=False, sub=sub, **common)
    both = jnp.stack([k_img[0], v_img[0]])
    chunks = [(both, me * tok_dev)]
    to_right = [(i, i + 1) for i in range(nseq - 1)]
    to_left = [(i + 1, i) for i in range(nseq - 1)]
    from_left, from_right = both, both
    for step in range(1, reach + 1):
        from_left = lax.ppermute(from_left, "seq", to_right)
        from_right = lax.ppermute(from_right, "seq", to_left)
        if step == 1:
            local_kv, from_left, from_right = lax.optimization_barrier((both, from_left, from_right))
            chunks[0] = (local_kv, me * tok_dev)
        chunks.append((from_left, (me - step) * tok_dev))
        chunks.append((from_right, (me + step) * tok_dev))
    for index, (kv, lower) in enumerate(chunks[:-1]):
        blocks = as_blocks(kv)
        state = attend_chunk(
            info_for(lower), queries, blocks, blocks, tok_dev // tk, state, kind="image", last=False,
            **common,
        )
    kv, lower = chunks[-1]
    nhead = lax.axis_size("head")
    nparts = 2 if nhead == 2 and width % 256 == 0 else 1
    attn_parts = [
        attend_chunk(
            info_for(lower), queries, as_blocks(kv), as_blocks(kv), tok_dev // tk, state, kind="image", last=True,
            part=(i, nparts), **common,
        )
        for i in range(nparts)
    ]
    own_cfg = lax.axis_index("cfg")
    cols = out_weight.shape[1]
    half = cols // 2
    mine_weight = jnp.where(own_cfg == 0, guidance, 1.0 - guidance)
    w_keep = lax.dynamic_slice_in_dim(out_weight, own_cfg * half, half, 1)
    w_out = lax.dynamic_slice_in_dim(out_weight, (1 - own_cfg) * half, half, 1)
    if nhead == 2:
        hx = lax.axis_index("head")
        others = [partner_2(x, "head", 0) for x in attn_parts]
        piece = width // nparts

        def project(w):
            own = None
            for i, x in enumerate(attn_parts):
                term = lax.dot_general(
                    x, lax.dynamic_slice_in_dim(w, hx * width + i * piece, piece, 0),
                    (((0,), (0,)), ((), ())), preferred_element_type=jnp.float32,
                )
                own = term if own is None else own + term
            summed = lax.optimization_barrier(own)
            for i, x in enumerate(others):
                summed = summed + lax.dot_general(
                    x, lax.dynamic_slice_in_dim(w, (1 - hx) * width + i * piece, piece, 0),
                    (((0,), (0,)), ((), ())), preferred_element_type=jnp.float32,
                )
            return summed
    else:
        gathered = lax.all_gather(jnp.concatenate(attn_parts, axis=0), "head", axis=0, tiled=True)

        def project(w):
            return lax.dot_general(gathered, w, (((0,), (0,)), ((), ())), preferred_element_type=jnp.float32)

    outgoing = project(w_out)
    partner = partner_2(outgoing.astype(jnp.bfloat16), "cfg", 0).astype(outgoing.dtype)
    keep = project(w_keep)
    guided = mine_weight * keep + (1.0 - mine_weight) * partner
    return guided.astype(jnp.bfloat16)


def solution(mesh):
    placed = (
        P("cfg", ("groups", "seq"), "head"),
        P("cfg", ("groups", "seq"), "head"),
        P("cfg", ("groups", "seq"), "head"),
        P("cfg", "groups", None, "head"),
        P("cfg", "groups", None, "head"),
        P("cfg", "groups"),
        P("groups"),
        P(None, "head"),
    )
    return jax.shard_map(
        local,
        mesh=mesh,
        in_specs=placed,
        out_specs=P(("groups", "seq"), ("head", "cfg")),
        check_vma=False,
    )
```

```python
import functools

import jax
import jax.numpy as jnp
from jax import lax
from jax.experimental import pallas as pl
from jax.experimental.pallas import tpu as pltpu
from jax.sharding import PartitionSpec as P

HDIM = 64


guidance = 4.0
score_scale = 0.125
neg_large = -1e30


def partner_2(x, axis, distance):
    return lax.ppermute(x, axis, [(i, i ^ 1 << distance) for i in range(lax.axis_size(axis))])


def seg_scalar(info_ref, pos, reqs):
    seg = jnp.int32(0)
    for r in range(reqs):
        seg = seg + jnp.where(pos >= info_ref[2 + r], 1, 0).astype(jnp.int32)
    return seg


def seg_vector(info_ref, pos, reqs):
    seg = jnp.zeros(pos.shape, jnp.int32)
    for r in range(reqs):
        seg = seg + (pos >= info_ref[2 + r]).astype(jnp.int32)
    return seg


def attn_kernel(info_ref, q_ref, k_ref, v_ref, *refs, kind, heads, reqs, tq, tk, total, first, last, sub, shift):
    if first:
        ins, outs = (), refs[:-3]
    else:
        ins, outs = refs[:3], refs[3:-3]
    m_sc, l_sc, a_sc = refs[-3:]
    qi = pl.program_id(0)
    b = pl.program_id(1)
    nb = pl.num_programs(1)
    width = heads * HDIM

    @pl.when(b == 0)
    def _():
        if first:
            m_sc[...] = jnp.full(m_sc.shape, neg_large, jnp.float32)
            l_sc[...] = jnp.zeros(l_sc.shape, jnp.float32)
            a_sc[...] = jnp.zeros(a_sc.shape, jnp.float32)
        else:
            m_sc[...] = ins[0][...]
            l_sc[...] = ins[1][...]
            a_sc[...] = ins[2][...]

    qpos0 = info_ref[0] + qi * tq
    qlo = seg_scalar(info_ref, qpos0, reqs)
    qhi = seg_scalar(info_ref, qpos0 + tq - 1, reqs)
    if kind == "text":
        req = b // sub
        offset = (b % sub) * tk
        active = (qlo <= req) & (req <= qhi) & (offset < info_ref[2 + reqs + req])
    else:
        kpos0 = info_ref[0] + shift + b * tk
        klo = seg_scalar(info_ref, kpos0, reqs)
        khi = seg_scalar(info_ref, kpos0 + tk - 1, reqs)
        active = (kpos0 >= 0) & (kpos0 < total) & (klo <= qhi) & (qlo <= khi)

    @pl.when(active)
    def _():
        qseg = seg_vector(info_ref, qpos0 + lax.broadcasted_iota(jnp.int32, (1, tq), 1), reqs)
        row = lax.broadcasted_iota(jnp.int32, (tk, 1), 0)
        if kind == "text":
            mask = (row + offset < info_ref[2 + reqs + req]) & (qseg == req)
        else:
            mask = seg_vector(info_ref, kpos0 + row, reqs) == qseg
        for g0 in range(0, width, 128):
            gw = min(128, width - g0)
            qg = q_ref[:, g0:g0 + gw]
            kg = k_ref[0, :, g0:g0 + gw]
            vt = v_ref[0, :, g0:g0 + gw].T
            lane = lax.broadcasted_iota(jnp.int32, (1, gw), 1)
            sub = lax.broadcasted_iota(jnp.int32, (gw, 1), 0) < HDIM
            acc = a_sc[g0:g0 + gw, :]
            parts = []
            for i in range(gw // HDIM):
                h = g0 // HDIM + i
                if gw == HDIM:
                    kh = kg
                else:
                    kh = jnp.where((lane < HDIM) if i == 0 else (lane >= HDIM), kg, jnp.zeros_like(kg))
                st = lax.dot_general(
                    kh, qg, (((1,), (1,)), ((), ())), preferred_element_type=jnp.float32
                ) * score_scale
                st = jnp.where(mask, st, neg_large)
                m_old = m_sc[h]
                m_new = jnp.maximum(m_old, jnp.max(st, axis=0, keepdims=True))
                alpha = jnp.exp(m_old - m_new)
                pt = jnp.exp(st - m_new)
                l_sc[h] = alpha * l_sc[h] + jnp.sum(pt, axis=0, keepdims=True)
                m_sc[h] = m_new
                pv = jnp.dot(vt, pt.astype(jnp.bfloat16), preferred_element_type=jnp.float32)
                parts.append(alpha * acc + pv)
            new = parts[0] if len(parts) == 1 else jnp.where(sub, parts[0], parts[1])
            a_sc[g0:g0 + gw, :] = new

    @pl.when(b == nb - 1)
    def _():
        if last:
            for g0 in range(0, width, 128):
                gw = min(128, width - g0)
                h = g0 // HDIM
                if gw == HDIM:
                    den = l_sc[h]
                else:
                    sub = lax.broadcasted_iota(jnp.int32, (gw, 1), 0) < HDIM
                    den = jnp.where(sub, l_sc[h], l_sc[h + 1])
                outs[0][g0:g0 + gw, :] = (a_sc[g0:g0 + gw, :] / den).astype(outs[0].dtype)
        else:
            outs[0][...] = m_sc[...]
            outs[1][...] = l_sc[...]
            outs[2][...] = a_sc[...]


def attend_chunk(info, queries, keys, values, v_off, state, *, kind, reqs, total, last, part=(0, 1), tq=256, sub=1, shift=0):
    tok, full_width = queries.shape
    index, nparts = part
    width = full_width // nparts
    heads = width // HDIM
    nb = keys.shape[0] - v_off
    tk = keys.shape[1]
    tq = min(tok, tq)
    first = state is None
    kernel = functools.partial(
        attn_kernel, kind=kind, heads=heads, reqs=reqs, tq=tq, tk=tk, total=total, first=first, last=last, sub=sub, shift=shift
    )
    q_spec = pl.BlockSpec((tq, width), lambda qi, b, info: (qi, index))
    k_spec = pl.BlockSpec((1, tk, width), lambda qi, b, info: (b, 0, index))
    v_spec = pl.BlockSpec((1, tk, width), lambda qi, b, info: (v_off + b, 0, index))
    ml_spec = pl.BlockSpec((heads, 1, tq), lambda qi, b, info: (index, 0, qi))
    acc_spec = pl.BlockSpec((width, tq), lambda qi, b, info: (index, qi))
    in_specs = [q_spec, k_spec, v_spec]
    args = [queries, keys, values]
    if not first:
        in_specs += [ml_spec, ml_spec, acc_spec]
        args += list(state)
    if last:
        out_shape = jax.ShapeDtypeStruct((width, tok), jnp.bfloat16)
        out_specs = pl.BlockSpec((width, tq), lambda qi, b, info: (0, qi))
    else:
        out_shape = (
            jax.ShapeDtypeStruct((heads * nparts, 1, tok), jnp.float32),
            jax.ShapeDtypeStruct((heads * nparts, 1, tok), jnp.float32),
            jax.ShapeDtypeStruct((width * nparts, tok), jnp.float32),
        )
        out_specs = (ml_spec, ml_spec, acc_spec)
    flops = 32 * 4 * tok * nb * tk * width * 2
    cost = pl.CostEstimate(
        flops=flops,
        transcendentals=tok * nb * tk * heads,
        bytes_accessed=2 * (tok * width * 2 + 2 * nb * tk * width * 2 + tok * width * 4),
    )
    return pl.pallas_call(
        kernel,
        out_shape=out_shape,
        grid_spec=pltpu.PrefetchScalarGridSpec(
            num_scalar_prefetch=1,
            grid=(tok // tq, nb),
            in_specs=in_specs,
            out_specs=out_specs,
            scratch_shapes=[
                pltpu.VMEM((heads, 1, tq), jnp.float32),
                pltpu.VMEM((heads, 1, tq), jnp.float32),
                pltpu.VMEM((width, tq), jnp.float32),
            ],
        ),
        compiler_params=pltpu.CompilerParams(dimension_semantics=("arbitrary", "arbitrary")),
        cost_estimate=cost,
    )(info, *args)


def local(q_img, k_img, v_img, text_keys, text_values, text_lengths, img_lengths, out_weight):
    tok_dev = q_img.shape[1]
    width = q_img.shape[2]
    reqs = text_keys.shape[1]
    text_slots = text_keys.shape[2]
    nseq = lax.axis_size("seq")
    me = lax.axis_index("seq")
    total = tok_dev * nseq
    longest = total // 2
    reach = min(nseq - 1, (longest + tok_dev - 2) // tok_dev)
    ends = jnp.cumsum(img_lengths).astype(jnp.int32)
    queries = q_img[0]

    def info_for(kstart):
        head = jnp.stack([me * tok_dev, kstart]).astype(jnp.int32)
        return jnp.concatenate([head, ends, text_lengths[0].astype(jnp.int32)])

    pad_to = -(-text_slots // 128) * 128
    pad = ((0, 0), (0, pad_to - text_slots), (0, 0))
    tk = min(tok_dev, 128)
    sub = pad_to // tk
    text_k = jnp.pad(text_keys[0], pad).reshape(reqs * sub, tk, width)
    text_v = jnp.pad(text_values[0], pad).reshape(reqs * sub, tk, width)

    def as_blocks(x):
        return x.reshape(2 * tok_dev // tk, tk, width)

    common = dict(reqs=reqs, total=total)
    info = info_for(0)
    state = attend_chunk(info, queries, text_k, text_v, 0, None, kind="text", last=False, sub=sub, **common)
    both = jnp.stack([k_img[0], v_img[0]])
    chunks = [(both, 0)]
    to_right = [(i, i + 1) for i in range(nseq - 1)]
    to_left = [(i + 1, i) for i in range(nseq - 1)]
    from_left, from_right = both, both
    for step in range(1, reach + 1):
        from_left = lax.ppermute(from_left, "seq", to_right)
        from_right = lax.ppermute(from_right, "seq", to_left)
        if step == 1:
            local_kv, from_left, from_right = lax.optimization_barrier((both, from_left, from_right))
            chunks[0] = (local_kv, 0)
        chunks.append((from_left, -step * tok_dev))
        chunks.append((from_right, step * tok_dev))
    for index, (kv, shift) in enumerate(chunks[:-1]):
        blocks = as_blocks(kv)
        state = attend_chunk(
            info, queries, blocks, blocks, tok_dev // tk, state, kind="image", last=False, shift=shift,
            **common,
        )
    kv, shift = chunks[-1]
    nhead = lax.axis_size("head")
    nparts = 2 if nhead == 2 and width % 256 == 0 else 1
    attn_parts = [
        attend_chunk(
            info, queries, as_blocks(kv), as_blocks(kv), tok_dev // tk, state, kind="image", last=True, shift=shift,
            part=(i, nparts), **common,
        )
        for i in range(nparts)
    ]
    own_cfg = lax.axis_index("cfg")
    cols = out_weight.shape[1]
    half = cols // 2
    mine_weight = jnp.where(own_cfg == 0, guidance, 1.0 - guidance)
    w_keep = lax.dynamic_slice_in_dim(out_weight, own_cfg * half, half, 1)
    w_out = lax.dynamic_slice_in_dim(out_weight, (1 - own_cfg) * half, half, 1)
    if nhead == 2:
        hx = lax.axis_index("head")
        others = [partner_2(x, "head", 0) for x in attn_parts]
        piece = width // nparts

        def project(w):
            own = None
            for i, x in enumerate(attn_parts):
                term = lax.dot_general(
                    x, lax.dynamic_slice_in_dim(w, hx * width + i * piece, piece, 0),
                    (((0,), (0,)), ((), ())), preferred_element_type=jnp.float32,
                )
                own = term if own is None else own + term
            summed = lax.optimization_barrier(own)
            for i, x in enumerate(others):
                summed = summed + lax.dot_general(
                    x, lax.dynamic_slice_in_dim(w, (1 - hx) * width + i * piece, piece, 0),
                    (((0,), (0,)), ((), ())), preferred_element_type=jnp.float32,
                )
            return summed
    else:
        gathered = lax.all_gather(jnp.concatenate(attn_parts, axis=0), "head", axis=0, tiled=True)

        def project(w):
            return lax.dot_general(gathered, w, (((0,), (0,)), ((), ())), preferred_element_type=jnp.float32)

    outgoing = project(w_out)
    partner = partner_2(outgoing.astype(jnp.bfloat16), "cfg", 0).astype(outgoing.dtype)
    keep = project(w_keep)
    guided = mine_weight * keep + (1.0 - mine_weight) * partner
    return guided.astype(jnp.bfloat16)


def solution(mesh):
    placed = (
        P("cfg", ("groups", "seq"), "head"),
        P("cfg", ("groups", "seq"), "head"),
        P("cfg", ("groups", "seq"), "head"),
        P("cfg", "groups", None, "head"),
        P("cfg", "groups", None, "head"),
        P("cfg", "groups"),
        P("groups"),
        P(None, "head"),
    )
    return jax.shard_map(
        local,
        mesh=mesh,
        in_specs=placed,
        out_specs=P(("groups", "seq"), ("head", "cfg")),
        check_vma=False,
    )
```

```python
import functools

import jax
import jax.numpy as jnp
from jax import lax
from jax.experimental import pallas as pl
from jax.experimental.pallas import tpu as pltpu
from jax.sharding import PartitionSpec as P

HDIM = 64


guidance = 4.0
score_scale = 0.125
neg_large = -1e30


def partner_2(x, axis, distance):
    return lax.ppermute(x, axis, [(i, i ^ 1 << distance) for i in range(lax.axis_size(axis))])


def seg_scalar(info_ref, pos, reqs):
    seg = jnp.int32(0)
    for r in range(reqs):
        seg = seg + jnp.where(pos >= info_ref[2 + r], 1, 0).astype(jnp.int32)
    return seg


def seg_vector(info_ref, pos, reqs):
    seg = jnp.zeros(pos.shape, jnp.int32)
    for r in range(reqs):
        seg = seg + (pos >= info_ref[2 + r]).astype(jnp.int32)
    return seg


def attn_kernel(info_ref, q_ref, k_ref, v_ref, *refs, kind, heads, reqs, tq, tk, total, first, last, sub, shift):
    if first:
        ins, outs = (), refs[:-3]
    else:
        ins, outs = refs[:3], refs[3:-3]
    m_sc, l_sc, a_sc = refs[-3:]
    qi = pl.program_id(0)
    b = pl.program_id(1)
    nb = pl.num_programs(1)
    width = heads * HDIM

    @pl.when(b == 0)
    def _():
        if first:
            m_sc[...] = jnp.full(m_sc.shape, neg_large, jnp.float32)
            l_sc[...] = jnp.zeros(l_sc.shape, jnp.float32)
            a_sc[...] = jnp.zeros(a_sc.shape, jnp.float32)
        else:
            m_sc[...] = ins[0][...]
            l_sc[...] = ins[1][...]
            a_sc[...] = ins[2][...]

    qpos0 = info_ref[0] + qi * tq
    qlo = seg_scalar(info_ref, qpos0, reqs)
    qhi = seg_scalar(info_ref, qpos0 + tq - 1, reqs)
    if kind == "text":
        req = b // sub
        offset = (b % sub) * tk
        active = (qlo <= req) & (req <= qhi) & (offset < info_ref[2 + reqs + req])
    else:
        kpos0 = info_ref[0] + shift + b * tk
        klo = seg_scalar(info_ref, kpos0, reqs)
        khi = seg_scalar(info_ref, kpos0 + tk - 1, reqs)
        active = (kpos0 >= 0) & (kpos0 < total) & (klo <= qhi) & (qlo <= khi)

    @pl.when(active)
    def _():
        qseg = seg_vector(info_ref, qpos0 + lax.broadcasted_iota(jnp.int32, (1, tq), 1), reqs)
        row = lax.broadcasted_iota(jnp.int32, (tk, 1), 0)
        if kind == "text":
            mask = (row + offset < info_ref[2 + reqs + req]) & (qseg == req)
        else:
            mask = seg_vector(info_ref, kpos0 + row, reqs) == qseg
        for g0 in range(0, width, 128):
            gw = min(128, width - g0)
            qg = q_ref[:, g0:g0 + gw]
            kg = k_ref[0, :, g0:g0 + gw]
            vt = v_ref[0, :, g0:g0 + gw].T
            lane = lax.broadcasted_iota(jnp.int32, (1, gw), 1)
            sub = lax.broadcasted_iota(jnp.int32, (gw, 1), 0) < HDIM
            acc = a_sc[g0:g0 + gw, :]
            parts = []
            for i in range(gw // HDIM):
                h = g0 // HDIM + i
                if gw == HDIM:
                    kh = kg
                else:
                    kh = jnp.where((lane < HDIM) if i == 0 else (lane >= HDIM), kg, jnp.zeros_like(kg))
                st = lax.dot_general(
                    kh, qg, (((1,), (1,)), ((), ())), preferred_element_type=jnp.float32
                ) * score_scale
                st = jnp.where(mask, st, neg_large)
                m_old = m_sc[h]
                m_new = jnp.maximum(m_old, jnp.max(st, axis=0, keepdims=True))
                alpha = jnp.exp(m_old - m_new)
                pt = jnp.exp(st - m_new)
                l_sc[h] = alpha * l_sc[h] + jnp.sum(pt, axis=0, keepdims=True)
                m_sc[h] = m_new
                pv = jnp.dot(vt, pt.astype(jnp.bfloat16), preferred_element_type=jnp.float32)
                parts.append(alpha * acc + pv)
            new = parts[0] if len(parts) == 1 else jnp.where(sub, parts[0], parts[1])
            a_sc[g0:g0 + gw, :] = new

    @pl.when(b == nb - 1)
    def _():
        if last:
            for g0 in range(0, width, 128):
                gw = min(128, width - g0)
                h = g0 // HDIM
                if gw == HDIM:
                    den = l_sc[h]
                else:
                    sub = lax.broadcasted_iota(jnp.int32, (gw, 1), 0) < HDIM
                    den = jnp.where(sub, l_sc[h], l_sc[h + 1])
                outs[0][g0:g0 + gw, :] = (a_sc[g0:g0 + gw, :] / den).astype(outs[0].dtype)
        else:
            outs[0][...] = m_sc[...]
            outs[1][...] = l_sc[...]
            outs[2][...] = a_sc[...]


def attend_chunk(info, queries, keys, values, v_off, state, *, kind, reqs, total, last, part=(0, 1), tq=256, sub=1, shift=0):
    tok, full_width = queries.shape
    index, nparts = part
    width = full_width // nparts
    heads = width // HDIM
    nb = keys.shape[0] - v_off
    tk = keys.shape[1]
    tq = min(tok, tq)
    first = state is None
    kernel = functools.partial(
        attn_kernel, kind=kind, heads=heads, reqs=reqs, tq=tq, tk=tk, total=total, first=first, last=last, sub=sub, shift=shift
    )
    q_spec = pl.BlockSpec((tq, width), lambda qi, b, info: (qi, index))

    def kv_block(qi, b, info):
        qpos0 = info[0] + qi * tq
        qlo = seg_scalar(info, qpos0, reqs)
        qhi = seg_scalar(info, qpos0 + tq - 1, reqs)
        if kind == "text":
            lo, hi = qlo * sub, qhi * sub + sub - 1
        else:
            kstart = info[0] + shift
            seg_start = jnp.where(qlo == 0, 0, info[2 + jnp.maximum(qlo - 1, 0)])
            seg_end = info[2 + jnp.minimum(qhi, reqs - 1)]
            lo = (seg_start - kstart) // tk
            hi = (seg_end - 1 - kstart) // tk
        lo = jnp.clip(lo, 0, nb - 1)
        hi = jnp.clip(hi, 0, nb - 1)
        return jnp.minimum(jnp.maximum(b, lo), hi)

    k_spec = pl.BlockSpec((1, tk, width), lambda qi, b, info: (kv_block(qi, b, info), 0, index))
    v_spec = pl.BlockSpec((1, tk, width), lambda qi, b, info: (v_off + kv_block(qi, b, info), 0, index))
    ml_spec = pl.BlockSpec((heads, 1, tq), lambda qi, b, info: (index, 0, qi))
    acc_spec = pl.BlockSpec((width, tq), lambda qi, b, info: (index, qi))
    in_specs = [q_spec, k_spec, v_spec]
    args = [queries, keys, values]
    if not first:
        in_specs += [ml_spec, ml_spec, acc_spec]
        args += list(state)
    if last:
        out_shape = jax.ShapeDtypeStruct((width, tok), jnp.bfloat16)
        out_specs = pl.BlockSpec((width, tq), lambda qi, b, info: (0, qi))
    else:
        out_shape = (
            jax.ShapeDtypeStruct((heads * nparts, 1, tok), jnp.float32),
            jax.ShapeDtypeStruct((heads * nparts, 1, tok), jnp.float32),
            jax.ShapeDtypeStruct((width * nparts, tok), jnp.float32),
        )
        out_specs = (ml_spec, ml_spec, acc_spec)
    flops = 32 * 4 * tok * nb * tk * width * 2
    cost = pl.CostEstimate(
        flops=flops,
        transcendentals=tok * nb * tk * heads,
        bytes_accessed=2 * (tok * width * 2 + 2 * nb * tk * width * 2 + tok * width * 4),
    )
    return pl.pallas_call(
        kernel,
        out_shape=out_shape,
        grid_spec=pltpu.PrefetchScalarGridSpec(
            num_scalar_prefetch=1,
            grid=(tok // tq, nb),
            in_specs=in_specs,
            out_specs=out_specs,
            scratch_shapes=[
                pltpu.VMEM((heads, 1, tq), jnp.float32),
                pltpu.VMEM((heads, 1, tq), jnp.float32),
                pltpu.VMEM((width, tq), jnp.float32),
            ],
        ),
        compiler_params=pltpu.CompilerParams(dimension_semantics=("arbitrary", "arbitrary")),
        cost_estimate=cost,
    )(info, *args)


def local(q_img, k_img, v_img, text_keys, text_values, text_lengths, img_lengths, out_weight):
    tok_dev = q_img.shape[1]
    width = q_img.shape[2]
    reqs = text_keys.shape[1]
    text_slots = text_keys.shape[2]
    nseq = lax.axis_size("seq")
    me = lax.axis_index("seq")
    total = tok_dev * nseq
    longest = total // 2
    reach = min(nseq - 1, (longest + tok_dev - 2) // tok_dev)
    ends = jnp.cumsum(img_lengths).astype(jnp.int32)
    queries = q_img[0]

    def info_for(kstart):
        head = jnp.stack([me * tok_dev, kstart]).astype(jnp.int32)
        return jnp.concatenate([head, ends, text_lengths[0].astype(jnp.int32)])

    pad_to = -(-text_slots // 128) * 128
    pad = ((0, 0), (0, pad_to - text_slots), (0, 0))
    tk = min(tok_dev, 128)
    sub = pad_to // tk
    text_k = jnp.pad(text_keys[0], pad).reshape(reqs * sub, tk, width)
    text_v = jnp.pad(text_values[0], pad).reshape(reqs * sub, tk, width)

    def as_blocks(x):
        return x.reshape(2 * tok_dev // tk, tk, width)

    common = dict(reqs=reqs, total=total)
    info = info_for(0)
    state = attend_chunk(info, queries, text_k, text_v, 0, None, kind="text", last=False, sub=sub, **common)
    both = jnp.stack([k_img[0], v_img[0]])
    chunks = [(both, 0)]
    to_right = [(i, i + 1) for i in range(nseq - 1)]
    to_left = [(i + 1, i) for i in range(nseq - 1)]
    from_left, from_right = both, both
    for step in range(1, reach + 1):
        from_left = lax.ppermute(from_left, "seq", to_right)
        from_right = lax.ppermute(from_right, "seq", to_left)
        if step == 1:
            local_kv, from_left, from_right = lax.optimization_barrier((both, from_left, from_right))
            chunks[0] = (local_kv, 0)
        chunks.append((from_left, -step * tok_dev))
        chunks.append((from_right, step * tok_dev))
    for index, (kv, shift) in enumerate(chunks[:-1]):
        blocks = as_blocks(kv)
        state = attend_chunk(
            info, queries, blocks, blocks, tok_dev // tk, state, kind="image", last=False, shift=shift,
            **common,
        )
    kv, shift = chunks[-1]
    nhead = lax.axis_size("head")
    nparts = 2 if nhead == 2 and width % 256 == 0 else 1
    attn_parts = [
        attend_chunk(
            info, queries, as_blocks(kv), as_blocks(kv), tok_dev // tk, state, kind="image", last=True, shift=shift,
            part=(i, nparts), **common,
        )
        for i in range(nparts)
    ]
    own_cfg = lax.axis_index("cfg")
    cols = out_weight.shape[1]
    half = cols // 2
    mine_weight = jnp.where(own_cfg == 0, guidance, 1.0 - guidance)
    w_keep = lax.dynamic_slice_in_dim(out_weight, own_cfg * half, half, 1)
    w_out = lax.dynamic_slice_in_dim(out_weight, (1 - own_cfg) * half, half, 1)
    if nhead == 2:
        hx = lax.axis_index("head")
        others = [partner_2(x, "head", 0) for x in attn_parts]
        piece = width // nparts

        def project(w):
            own = None
            for i, x in enumerate(attn_parts):
                term = lax.dot_general(
                    x, lax.dynamic_slice_in_dim(w, hx * width + i * piece, piece, 0),
                    (((0,), (0,)), ((), ())), preferred_element_type=jnp.float32,
                )
                own = term if own is None else own + term
            summed = lax.optimization_barrier(own)
            for i, x in enumerate(others):
                summed = summed + lax.dot_general(
                    x, lax.dynamic_slice_in_dim(w, (1 - hx) * width + i * piece, piece, 0),
                    (((0,), (0,)), ((), ())), preferred_element_type=jnp.float32,
                )
            return summed
    else:
        gathered = lax.all_gather(jnp.concatenate(attn_parts, axis=0), "head", axis=0, tiled=True)

        def project(w):
            return lax.dot_general(gathered, w, (((0,), (0,)), ((), ())), preferred_element_type=jnp.float32)

    outgoing = project(w_out)
    partner = partner_2(outgoing.astype(jnp.bfloat16), "cfg", 0).astype(outgoing.dtype)
    keep = project(w_keep)
    guided = mine_weight * keep + (1.0 - mine_weight) * partner
    return guided.astype(jnp.bfloat16)


def solution(mesh):
    placed = (
        P("cfg", ("groups", "seq"), "head"),
        P("cfg", ("groups", "seq"), "head"),
        P("cfg", ("groups", "seq"), "head"),
        P("cfg", "groups", None, "head"),
        P("cfg", "groups", None, "head"),
        P("cfg", "groups"),
        P("groups"),
        P(None, "head"),
    )
    return jax.shard_map(
        local,
        mesh=mesh,
        in_specs=placed,
        out_specs=P(("groups", "seq"), ("head", "cfg")),
        check_vma=False,
    )
```

```python
import functools

import jax
import jax.numpy as jnp
from jax import lax
from jax.experimental import pallas as pl
from jax.experimental.pallas import tpu as pltpu
from jax.sharding import PartitionSpec as P

HDIM = 64


guidance = 4.0
score_scale = 0.125
neg_large = -1e30


def partner_2(x, axis, distance):
    return lax.ppermute(x, axis, [(i, i ^ 1 << distance) for i in range(lax.axis_size(axis))])


def seg_scalar(info_ref, pos, reqs):
    seg = jnp.int32(0)
    for r in range(reqs):
        seg = seg + jnp.where(pos >= info_ref[2 + r], 1, 0).astype(jnp.int32)
    return seg


def seg_vector(info_ref, pos, reqs):
    seg = jnp.zeros(pos.shape, jnp.int32)
    for r in range(reqs):
        seg = seg + (pos >= info_ref[2 + r]).astype(jnp.int32)
    return seg


def attn_kernel(info_ref, q_ref, k_ref, v_ref, *refs, kind, heads, reqs, tq, tk, total, first, last, sub, shift):
    if first:
        ins, outs = (), refs[:-3]
    else:
        ins, outs = refs[:3], refs[3:-3]
    m_sc, l_sc, a_sc = refs[-3:]
    qi = pl.program_id(0)
    b = pl.program_id(1)
    nb = pl.num_programs(1)
    width = heads * HDIM

    @pl.when(b == 0)
    def _():
        if first:
            m_sc[...] = jnp.full(m_sc.shape, neg_large, jnp.float32)
            l_sc[...] = jnp.zeros(l_sc.shape, jnp.float32)
            a_sc[...] = jnp.zeros(a_sc.shape, jnp.float32)
        else:
            m_sc[...] = ins[0][...]
            l_sc[...] = ins[1][...]
            a_sc[...] = ins[2][...]

    qpos0 = info_ref[0] + qi * tq
    qlo = seg_scalar(info_ref, qpos0, reqs)
    qhi = seg_scalar(info_ref, qpos0 + tq - 1, reqs)
    if kind == "text":
        req = b // sub
        offset = (b % sub) * tk
        active = (qlo <= req) & (req <= qhi) & (offset < info_ref[2 + reqs + req])
    else:
        kpos0 = info_ref[0] + shift + b * tk
        klo = seg_scalar(info_ref, kpos0, reqs)
        khi = seg_scalar(info_ref, kpos0 + tk - 1, reqs)
        active = (kpos0 >= 0) & (kpos0 < total) & (klo <= qhi) & (qlo <= khi)

    @pl.when(active)
    def _():
        qseg = seg_vector(info_ref, qpos0 + lax.broadcasted_iota(jnp.int32, (1, tq), 1), reqs)
        row = lax.broadcasted_iota(jnp.int32, (tk, 1), 0)
        if kind == "text":
            mask = (row + offset < info_ref[2 + reqs + req]) & (qseg == req)
        else:
            mask = seg_vector(info_ref, kpos0 + row, reqs) == qseg
        for g0 in range(0, width, 128):
            gw = min(128, width - g0)
            qg = q_ref[:, g0:g0 + gw]
            kg = k_ref[0, :, g0:g0 + gw]
            vt = v_ref[0, :, g0:g0 + gw].T
            lane = lax.broadcasted_iota(jnp.int32, (1, gw), 1)
            sub = lax.broadcasted_iota(jnp.int32, (gw, 1), 0) < HDIM
            acc = a_sc[g0:g0 + gw, :]
            parts = []
            for i in range(gw // HDIM):
                h = g0 // HDIM + i
                if gw == HDIM:
                    kh = kg
                else:
                    kh = jnp.where((lane < HDIM) if i == 0 else (lane >= HDIM), kg, jnp.zeros_like(kg))
                st = lax.dot_general(
                    kh, qg, (((1,), (1,)), ((), ())), preferred_element_type=jnp.float32
                ) * score_scale
                st = jnp.where(mask, st, neg_large)
                m_old = m_sc[h]
                m_new = jnp.maximum(m_old, jnp.max(st, axis=0, keepdims=True))
                alpha = jnp.exp(m_old - m_new)
                pt = jnp.exp(st - m_new)
                l_sc[h] = alpha * l_sc[h] + jnp.sum(pt, axis=0, keepdims=True)
                m_sc[h] = m_new
                pv = jnp.dot(vt, pt.astype(jnp.bfloat16), preferred_element_type=jnp.float32)
                parts.append(alpha * acc + pv)
            new = parts[0] if len(parts) == 1 else jnp.where(sub, parts[0], parts[1])
            a_sc[g0:g0 + gw, :] = new

    @pl.when(b == nb - 1)
    def _():
        if last:
            for g0 in range(0, width, 128):
                gw = min(128, width - g0)
                h = g0 // HDIM
                if gw == HDIM:
                    den = l_sc[h]
                else:
                    sub = lax.broadcasted_iota(jnp.int32, (gw, 1), 0) < HDIM
                    den = jnp.where(sub, l_sc[h], l_sc[h + 1])
                outs[0][g0:g0 + gw, :] = (a_sc[g0:g0 + gw, :] / den).astype(outs[0].dtype)
        else:
            outs[0][...] = m_sc[...]
            outs[1][...] = l_sc[...]
            outs[2][...] = a_sc[...]


def attend_chunk(info, queries, keys, values, v_off, state, *, kind, reqs, total, last, part=(0, 1), tq=256, sub=1, shift=0):
    tok, full_width = queries.shape
    index, nparts = part
    width = full_width // nparts
    heads = width // HDIM
    nb = keys.shape[0] - v_off
    tk = keys.shape[1]
    tq = min(tok, tq)
    first = state is None
    kernel = functools.partial(
        attn_kernel, kind=kind, heads=heads, reqs=reqs, tq=tq, tk=tk, total=total, first=first, last=last, sub=sub, shift=shift
    )
    q_spec = pl.BlockSpec((tq, width), lambda qi, b, info: (qi, index))

    def kv_block(qi, b, info):
        qpos0 = info[0] + qi * tq
        qlo = seg_scalar(info, qpos0, reqs)
        qhi = seg_scalar(info, qpos0 + tq - 1, reqs)
        if kind == "text":
            lo, hi = qlo * sub, qhi * sub + sub - 1
        else:
            kstart = info[0] + shift
            seg_start = jnp.where(qlo == 0, 0, info[2 + jnp.maximum(qlo - 1, 0)])
            seg_end = info[2 + jnp.minimum(qhi, reqs - 1)]
            lo = (seg_start - kstart) // tk
            hi = (seg_end - 1 - kstart) // tk
        lo = jnp.clip(lo, 0, nb - 1)
        hi = jnp.clip(hi, 0, nb - 1)
        return jnp.minimum(jnp.maximum(b, lo), hi)

    k_spec = pl.BlockSpec((1, tk, width), lambda qi, b, info: (kv_block(qi, b, info), 0, index))
    v_spec = pl.BlockSpec((1, tk, width), lambda qi, b, info: (v_off + kv_block(qi, b, info), 0, index))
    ml_spec = pl.BlockSpec((heads, 1, tq), lambda qi, b, info: (index, 0, qi))
    acc_spec = pl.BlockSpec((width, tq), lambda qi, b, info: (index, qi))
    in_specs = [q_spec, k_spec, v_spec]
    args = [queries, keys, values]
    if not first:
        in_specs += [ml_spec, ml_spec, acc_spec]
        args += list(state)
    if last:
        out_shape = jax.ShapeDtypeStruct((width, tok), jnp.bfloat16)
        out_specs = pl.BlockSpec((width, tq), lambda qi, b, info: (0, qi))
    else:
        out_shape = (
            jax.ShapeDtypeStruct((heads * nparts, 1, tok), jnp.float32),
            jax.ShapeDtypeStruct((heads * nparts, 1, tok), jnp.float32),
            jax.ShapeDtypeStruct((width * nparts, tok), jnp.float32),
        )
        out_specs = (ml_spec, ml_spec, acc_spec)
    flops = 32 * 4 * tok * nb * tk * width * 2
    cost = pl.CostEstimate(
        flops=flops,
        transcendentals=tok * nb * tk * heads,
        bytes_accessed=2 * (tok * width * 2 + 2 * nb * tk * width * 2 + tok * width * 4),
    )
    return pl.pallas_call(
        kernel,
        out_shape=out_shape,
        grid_spec=pltpu.PrefetchScalarGridSpec(
            num_scalar_prefetch=1,
            grid=(tok // tq, nb),
            in_specs=in_specs,
            out_specs=out_specs,
            scratch_shapes=[
                pltpu.VMEM((heads, 1, tq), jnp.float32),
                pltpu.VMEM((heads, 1, tq), jnp.float32),
                pltpu.VMEM((width, tq), jnp.float32),
            ],
        ),
        compiler_params=pltpu.CompilerParams(dimension_semantics=("arbitrary", "arbitrary")),
        cost_estimate=cost,
    )(info, *args)


def local(q_img, k_img, v_img, text_keys, text_values, text_lengths, img_lengths, out_weight):
    tok_dev = q_img.shape[1]
    width = q_img.shape[2]
    reqs = text_keys.shape[1]
    text_slots = text_keys.shape[2]
    nseq = lax.axis_size("seq")
    me = lax.axis_index("seq")
    total = tok_dev * nseq
    longest = total // 2
    reach = min(nseq - 1, (longest + tok_dev - 2) // tok_dev)
    ends = jnp.cumsum(img_lengths).astype(jnp.int32)
    queries = q_img[0]

    def info_for(kstart):
        head = jnp.stack([me * tok_dev, kstart]).astype(jnp.int32)
        return jnp.concatenate([head, ends, text_lengths[0].astype(jnp.int32)])

    pad_to = -(-text_slots // 128) * 128
    pad = ((0, 0), (0, pad_to - text_slots), (0, 0))
    tk = min(tok_dev, 128)
    sub = pad_to // tk
    text_k = jnp.pad(text_keys[0], pad).reshape(reqs * sub, tk, width)
    text_v = jnp.pad(text_values[0], pad).reshape(reqs * sub, tk, width)

    def as_blocks(x):
        return x.reshape(2 * tok_dev // tk, tk, width)

    common = dict(reqs=reqs, total=total)
    info = info_for(0)
    state = attend_chunk(info, queries, text_k, text_v, 0, None, kind="text", last=False, sub=sub, **common)
    both = jnp.stack([k_img[0], v_img[0]])
    chunks = [(both, 0)]
    to_right = [(i, i + 1) for i in range(nseq - 1)]
    to_left = [(i + 1, i) for i in range(nseq - 1)]
    from_left, from_right = both, both
    for step in range(1, reach + 1):
        from_left = lax.ppermute(from_left, "seq", to_right)
        from_right = lax.ppermute(from_right, "seq", to_left)
        if step == 1:
            local_kv, from_left, from_right = lax.optimization_barrier((both, from_left, from_right))
            chunks[0] = (local_kv, 0)
        chunks.append((from_left, -step * tok_dev))
        chunks.append((from_right, step * tok_dev))
    for index, (kv, shift) in enumerate(chunks[:-1]):
        blocks = as_blocks(kv)
        state = attend_chunk(
            info, queries, blocks, blocks, tok_dev // tk, state, kind="image", last=False, shift=shift,
            **common,
        )
    kv, shift = chunks[-1]
    nhead = lax.axis_size("head")
    nparts = 1
    attn_parts = [
        attend_chunk(
            info, queries, as_blocks(kv), as_blocks(kv), tok_dev // tk, state, kind="image", last=True, shift=shift,
            part=(i, nparts), **common,
        )
        for i in range(nparts)
    ]
    own_cfg = lax.axis_index("cfg")
    cols = out_weight.shape[1]
    half = cols // 2
    mine_weight = jnp.where(own_cfg == 0, guidance, 1.0 - guidance)
    w_keep = lax.dynamic_slice_in_dim(out_weight, own_cfg * half, half, 1)
    w_out = lax.dynamic_slice_in_dim(out_weight, (1 - own_cfg) * half, half, 1)
    if nhead == 2:
        hx = lax.axis_index("head")
        others = [partner_2(x, "head", 0) for x in attn_parts]
        piece = width // nparts

        def project(w):
            own = None
            for i, x in enumerate(attn_parts):
                term = lax.dot_general(
                    x, lax.dynamic_slice_in_dim(w, hx * width + i * piece, piece, 0),
                    (((0,), (0,)), ((), ())), preferred_element_type=jnp.float32,
                )
                own = term if own is None else own + term
            summed = lax.optimization_barrier(own)
            for i, x in enumerate(others):
                summed = summed + lax.dot_general(
                    x, lax.dynamic_slice_in_dim(w, (1 - hx) * width + i * piece, piece, 0),
                    (((0,), (0,)), ((), ())), preferred_element_type=jnp.float32,
                )
            return summed
    else:
        gathered = lax.all_gather(jnp.concatenate(attn_parts, axis=0), "head", axis=0, tiled=True)

        def project(w):
            return lax.dot_general(gathered, w, (((0,), (0,)), ((), ())), preferred_element_type=jnp.float32)

    outgoing = project(w_out)
    partner = partner_2(outgoing.astype(jnp.bfloat16), "cfg", 0).astype(outgoing.dtype)
    keep = project(w_keep)
    guided = mine_weight * keep + (1.0 - mine_weight) * partner
    return guided.astype(jnp.bfloat16)


def solution(mesh):
    placed = (
        P("cfg", ("groups", "seq"), "head"),
        P("cfg", ("groups", "seq"), "head"),
        P("cfg", ("groups", "seq"), "head"),
        P("cfg", "groups", None, "head"),
        P("cfg", "groups", None, "head"),
        P("cfg", "groups"),
        P("groups"),
        P(None, "head"),
    )
    return jax.shard_map(
        local,
        mesh=mesh,
        in_specs=placed,
        out_specs=P(("groups", "seq"), ("head", "cfg")),
        check_vma=False,
    )
```

```python
import functools

import jax
import jax.numpy as jnp
from jax import lax
from jax.experimental import pallas as pl
from jax.experimental.pallas import tpu as pltpu
from jax.sharding import PartitionSpec as P

HDIM = 64


guidance = 4.0
score_scale = 0.125
neg_large = -1e30


def partner_2(x, axis, distance):
    return lax.ppermute(x, axis, [(i, i ^ 1 << distance) for i in range(lax.axis_size(axis))])


def seg_scalar(info_ref, pos, reqs):
    seg = jnp.int32(0)
    for r in range(reqs):
        seg = seg + jnp.where(pos >= info_ref[2 + r], 1, 0).astype(jnp.int32)
    return seg


def seg_vector(info_ref, pos, reqs):
    seg = jnp.zeros(pos.shape, jnp.int32)
    for r in range(reqs):
        seg = seg + (pos >= info_ref[2 + r]).astype(jnp.int32)
    return seg


def attn_kernel(info_ref, q_ref, k_ref, v_ref, *refs, kind, heads, reqs, tq, tk, total, first, last, sub, shift):
    if first:
        ins, outs = (), refs[:-3]
    else:
        ins, outs = refs[:3], refs[3:-3]
    m_sc, l_sc, a_sc = refs[-3:]
    qi = pl.program_id(0)
    b = pl.program_id(1)
    nb = pl.num_programs(1)
    width = heads * HDIM

    @pl.when(b == 0)
    def _():
        if first:
            m_sc[...] = jnp.full(m_sc.shape, neg_large, jnp.float32)
            l_sc[...] = jnp.zeros(l_sc.shape, jnp.float32)
            a_sc[...] = jnp.zeros(a_sc.shape, jnp.float32)
        else:
            m_sc[...] = ins[0][...]
            l_sc[...] = ins[1][...]
            a_sc[...] = ins[2][...]

    qpos0 = info_ref[0] + qi * tq
    qlo = seg_scalar(info_ref, qpos0, reqs)
    qhi = seg_scalar(info_ref, qpos0 + tq - 1, reqs)
    if kind == "text":
        req = b // sub
        offset = (b % sub) * tk
        active = (qlo <= req) & (req <= qhi) & (offset < info_ref[2 + reqs + req])
    else:
        kpos0 = info_ref[0] + shift + b * tk
        klo = seg_scalar(info_ref, kpos0, reqs)
        khi = seg_scalar(info_ref, kpos0 + tk - 1, reqs)
        active = (kpos0 >= 0) & (kpos0 < total) & (klo <= qhi) & (qlo <= khi)

    @pl.when(active)
    def _():
        qseg = seg_vector(info_ref, qpos0 + lax.broadcasted_iota(jnp.int32, (1, tq), 1), reqs)
        row = lax.broadcasted_iota(jnp.int32, (tk, 1), 0)
        if kind == "text":
            mask = (row + offset < info_ref[2 + reqs + req]) & (qseg == req)
        else:
            mask = seg_vector(info_ref, kpos0 + row, reqs) == qseg
        for g0 in range(0, width, 128):
            gw = min(128, width - g0)
            qg = q_ref[:, g0:g0 + gw]
            kg = k_ref[0, :, g0:g0 + gw]
            vt = v_ref[0, :, g0:g0 + gw].T
            lane = lax.broadcasted_iota(jnp.int32, (1, gw), 1)
            sub = lax.broadcasted_iota(jnp.int32, (gw, 1), 0) < HDIM
            acc = a_sc[g0:g0 + gw, :]
            parts = []
            for i in range(gw // HDIM):
                h = g0 // HDIM + i
                if gw == HDIM:
                    kh = kg
                else:
                    kh = jnp.where((lane < HDIM) if i == 0 else (lane >= HDIM), kg, jnp.zeros_like(kg))
                st = lax.dot_general(
                    kh, qg, (((1,), (1,)), ((), ())), preferred_element_type=jnp.float32
                ) * score_scale
                st = jnp.where(mask, st, neg_large)
                m_old = m_sc[h]
                m_new = jnp.maximum(m_old, jnp.max(st, axis=0, keepdims=True))
                alpha = jnp.exp(m_old - m_new)
                pt = jnp.exp(st - m_new)
                l_sc[h] = alpha * l_sc[h] + jnp.sum(pt, axis=0, keepdims=True)
                m_sc[h] = m_new
                pv = jnp.dot(vt, pt.astype(jnp.bfloat16), preferred_element_type=jnp.float32)
                parts.append(alpha * acc + pv)
            new = parts[0] if len(parts) == 1 else jnp.where(sub, parts[0], parts[1])
            a_sc[g0:g0 + gw, :] = new

    @pl.when(b == nb - 1)
    def _():
        if last:
            for g0 in range(0, width, 128):
                gw = min(128, width - g0)
                h = g0 // HDIM
                if gw == HDIM:
                    den = l_sc[h]
                else:
                    sub = lax.broadcasted_iota(jnp.int32, (gw, 1), 0) < HDIM
                    den = jnp.where(sub, l_sc[h], l_sc[h + 1])
                outs[0][g0:g0 + gw, :] = (a_sc[g0:g0 + gw, :] / den).astype(outs[0].dtype)
        else:
            outs[0][...] = m_sc[...]
            outs[1][...] = l_sc[...]
            outs[2][...] = a_sc[...]


def attend_chunk(info, queries, keys, values, v_off, state, *, kind, reqs, total, last, part=(0, 1), tq=256, sub=1, shift=0):
    tok, full_width = queries.shape
    index, nparts = part
    width = full_width // nparts
    heads = width // HDIM
    nb = keys.shape[0] - v_off
    tk = keys.shape[1]
    tq = min(tok, tq)
    first = state is None
    kernel = functools.partial(
        attn_kernel, kind=kind, heads=heads, reqs=reqs, tq=tq, tk=tk, total=total, first=first, last=last, sub=sub, shift=shift
    )
    q_spec = pl.BlockSpec((tq, width), lambda qi, b, info: (qi, index))

    def kv_block(qi, b, info):
        qpos0 = info[0] + qi * tq
        qlo = seg_scalar(info, qpos0, reqs)
        qhi = seg_scalar(info, qpos0 + tq - 1, reqs)
        if kind == "text":
            lo, hi = qlo * sub, qhi * sub + sub - 1
        else:
            kstart = info[0] + shift
            seg_start = jnp.where(qlo == 0, 0, info[2 + jnp.maximum(qlo - 1, 0)])
            seg_end = info[2 + jnp.minimum(qhi, reqs - 1)]
            lo = (seg_start - kstart) // tk
            hi = (seg_end - 1 - kstart) // tk
        lo = jnp.clip(lo, 0, nb - 1)
        hi = jnp.clip(hi, 0, nb - 1)
        return jnp.minimum(jnp.maximum(b, lo), hi)

    k_spec = pl.BlockSpec((1, tk, width), lambda qi, b, info: (kv_block(qi, b, info), 0, index))
    v_spec = pl.BlockSpec((1, tk, width), lambda qi, b, info: (v_off + kv_block(qi, b, info), 0, index))
    ml_spec = pl.BlockSpec((heads, 1, tq), lambda qi, b, info: (index, 0, qi))
    acc_spec = pl.BlockSpec((width, tq), lambda qi, b, info: (index, qi))
    in_specs = [q_spec, k_spec, v_spec]
    args = [queries, keys, values]
    if not first:
        in_specs += [ml_spec, ml_spec, acc_spec]
        args += list(state)
    if last:
        out_shape = jax.ShapeDtypeStruct((width, tok), jnp.bfloat16)
        out_specs = pl.BlockSpec((width, tq), lambda qi, b, info: (0, qi))
    else:
        out_shape = (
            jax.ShapeDtypeStruct((heads * nparts, 1, tok), jnp.float32),
            jax.ShapeDtypeStruct((heads * nparts, 1, tok), jnp.float32),
            jax.ShapeDtypeStruct((width * nparts, tok), jnp.float32),
        )
        out_specs = (ml_spec, ml_spec, acc_spec)
    flops = 32 * 4 * tok * nb * tk * width * 2
    cost = pl.CostEstimate(
        flops=flops,
        transcendentals=tok * nb * tk * heads,
        bytes_accessed=2 * (tok * width * 2 + 2 * nb * tk * width * 2 + tok * width * 4),
    )
    return pl.pallas_call(
        kernel,
        out_shape=out_shape,
        grid_spec=pltpu.PrefetchScalarGridSpec(
            num_scalar_prefetch=1,
            grid=(tok // tq, nb),
            in_specs=in_specs,
            out_specs=out_specs,
            scratch_shapes=[
                pltpu.VMEM((heads, 1, tq), jnp.float32),
                pltpu.VMEM((heads, 1, tq), jnp.float32),
                pltpu.VMEM((width, tq), jnp.float32),
            ],
        ),
        compiler_params=pltpu.CompilerParams(dimension_semantics=("arbitrary", "arbitrary")),
        cost_estimate=cost,
    )(info, *args)


def local(q_img, k_img, v_img, text_keys, text_values, text_lengths, img_lengths, out_weight):
    tok_dev = q_img.shape[1]
    width = q_img.shape[2]
    reqs = text_keys.shape[1]
    text_slots = text_keys.shape[2]
    nseq = lax.axis_size("seq")
    me = lax.axis_index("seq")
    total = tok_dev * nseq
    longest = total // 2
    reach = min(nseq - 1, (longest + tok_dev - 2) // tok_dev)
    ends = jnp.cumsum(img_lengths).astype(jnp.int32)
    queries = q_img[0]

    def info_for(kstart):
        head = jnp.stack([me * tok_dev, kstart]).astype(jnp.int32)
        return jnp.concatenate([head, ends, text_lengths[0].astype(jnp.int32)])

    pad_to = -(-text_slots // 128) * 128
    pad = ((0, 0), (0, pad_to - text_slots), (0, 0))
    tk = min(tok_dev, 128)
    sub = pad_to // tk
    text_k = jnp.pad(text_keys[0], pad).reshape(reqs * sub, tk, width)
    text_v = jnp.pad(text_values[0], pad).reshape(reqs * sub, tk, width)

    def as_blocks(x):
        return x.reshape(2 * tok_dev // tk, tk, width)

    common = dict(reqs=reqs, total=total)
    info = info_for(0)
    state = attend_chunk(info, queries, text_k, text_v, 0, None, kind="text", last=False, sub=sub, **common)
    both = jnp.stack([k_img[0], v_img[0]])
    chunks = [(both, 0)]
    from_left, from_right = both, both
    for step in range(1, reach + 1):
        to_right = [(i, i + 1) for i in range(step - 1, nseq - 1)]
        to_left = [(i + 1, i) for i in range(nseq - step)]
        from_left = lax.ppermute(from_left, "seq", to_right)
        from_right = lax.ppermute(from_right, "seq", to_left)
        if step == 1:
            local_kv, from_left, from_right = lax.optimization_barrier((both, from_left, from_right))
            chunks[0] = (local_kv, 0)
        chunks.append((from_left, -step * tok_dev))
        chunks.append((from_right, step * tok_dev))
    for index, (kv, shift) in enumerate(chunks[:-1]):
        blocks = as_blocks(kv)
        state = attend_chunk(
            info, queries, blocks, blocks, tok_dev // tk, state, kind="image", last=False, shift=shift,
            **common,
        )
    kv, shift = chunks[-1]
    nhead = lax.axis_size("head")
    nparts = 2 if nhead == 2 and width % 256 == 0 else 1
    attn_parts = [
        attend_chunk(
            info, queries, as_blocks(kv), as_blocks(kv), tok_dev // tk, state, kind="image", last=True, shift=shift,
            part=(i, nparts), **common,
        )
        for i in range(nparts)
    ]
    own_cfg = lax.axis_index("cfg")
    cols = out_weight.shape[1]
    half = cols // 2
    mine_weight = jnp.where(own_cfg == 0, guidance, 1.0 - guidance)
    w_keep = lax.dynamic_slice_in_dim(out_weight, own_cfg * half, half, 1)
    w_out = lax.dynamic_slice_in_dim(out_weight, (1 - own_cfg) * half, half, 1)
    if nhead == 2:
        hx = lax.axis_index("head")
        others = [partner_2(x, "head", 0) for x in attn_parts]
        piece = width // nparts

        def project(w):
            own = None
            for i, x in enumerate(attn_parts):
                term = lax.dot_general(
                    x, lax.dynamic_slice_in_dim(w, hx * width + i * piece, piece, 0),
                    (((0,), (0,)), ((), ())), preferred_element_type=jnp.float32,
                )
                own = term if own is None else own + term
            summed = lax.optimization_barrier(own)
            for i, x in enumerate(others):
                summed = summed + lax.dot_general(
                    x, lax.dynamic_slice_in_dim(w, (1 - hx) * width + i * piece, piece, 0),
                    (((0,), (0,)), ((), ())), preferred_element_type=jnp.float32,
                )
            return summed
    else:
        gathered = lax.all_gather(jnp.concatenate(attn_parts, axis=0), "head", axis=0, tiled=True)

        def project(w):
            return lax.dot_general(gathered, w, (((0,), (0,)), ((), ())), preferred_element_type=jnp.float32)

    outgoing = project(w_out)
    partner = partner_2(outgoing.astype(jnp.bfloat16), "cfg", 0).astype(outgoing.dtype)
    keep = project(w_keep)
    guided = mine_weight * keep + (1.0 - mine_weight) * partner
    return guided.astype(jnp.bfloat16)


def solution(mesh):
    placed = (
        P("cfg", ("groups", "seq"), "head"),
        P("cfg", ("groups", "seq"), "head"),
        P("cfg", ("groups", "seq"), "head"),
        P("cfg", "groups", None, "head"),
        P("cfg", "groups", None, "head"),
        P("cfg", "groups"),
        P("groups"),
        P(None, "head"),
    )
    return jax.shard_map(
        local,
        mesh=mesh,
        in_specs=placed,
        out_specs=P(("groups", "seq"), ("head", "cfg")),
        check_vma=False,
    )
```

```python
import functools

import jax
import jax.numpy as jnp
from jax import lax
from jax.experimental import pallas as pl
from jax.experimental.pallas import tpu as pltpu
from jax.sharding import PartitionSpec as P

HDIM = 64


guidance = 4.0
score_scale = 0.125
neg_large = -1e30


def partner_2(x, axis, distance):
    return lax.ppermute(x, axis, [(i, i ^ 1 << distance) for i in range(lax.axis_size(axis))])


def seg_scalar(info_ref, pos, reqs):
    seg = jnp.int32(0)
    for r in range(reqs):
        seg = seg + jnp.where(pos >= info_ref[2 + r], 1, 0).astype(jnp.int32)
    return seg


def seg_vector(info_ref, pos, reqs):
    seg = jnp.zeros(pos.shape, jnp.int32)
    for r in range(reqs):
        seg = seg + (pos >= info_ref[2 + r]).astype(jnp.int32)
    return seg


def attn_kernel(info_ref, q_ref, k_ref, v_ref, *refs, kind, heads, reqs, tq, tk, total, first, last, sub, shift):
    if first:
        ins, outs = (), refs[:-3]
    else:
        ins, outs = refs[:3], refs[3:-3]
    m_sc, l_sc, a_sc = refs[-3:]
    qi = pl.program_id(0)
    b = pl.program_id(1)
    nb = pl.num_programs(1)
    width = heads * HDIM

    @pl.when(b == 0)
    def _():
        if first:
            m_sc[...] = jnp.full(m_sc.shape, neg_large, jnp.float32)
            l_sc[...] = jnp.zeros(l_sc.shape, jnp.float32)
            a_sc[...] = jnp.zeros(a_sc.shape, jnp.float32)
        else:
            m_sc[...] = ins[0][...]
            l_sc[...] = ins[1][...]
            a_sc[...] = ins[2][...]

    qpos0 = info_ref[0] + qi * tq
    qlo = seg_scalar(info_ref, qpos0, reqs)
    qhi = seg_scalar(info_ref, qpos0 + tq - 1, reqs)
    if kind == "text":
        req = b // sub
        offset = (b % sub) * tk
        active = (qlo <= req) & (req <= qhi) & (offset < info_ref[2 + reqs + req])
    else:
        kpos0 = info_ref[0] + shift + b * tk
        klo = seg_scalar(info_ref, kpos0, reqs)
        khi = seg_scalar(info_ref, kpos0 + tk - 1, reqs)
        active = (kpos0 >= 0) & (kpos0 < total) & (klo <= qhi) & (qlo <= khi)

    @pl.when(active)
    def _():
        qseg = seg_vector(info_ref, qpos0 + lax.broadcasted_iota(jnp.int32, (1, tq), 1), reqs)
        row = lax.broadcasted_iota(jnp.int32, (tk, 1), 0)
        if kind == "text":
            mask = (row + offset < info_ref[2 + reqs + req]) & (qseg == req)
        else:
            mask = seg_vector(info_ref, kpos0 + row, reqs) == qseg
        for g0 in range(0, width, 128):
            gw = min(128, width - g0)
            qg = q_ref[:, g0:g0 + gw]
            kg = k_ref[0, :, g0:g0 + gw]
            vt = v_ref[0, :, g0:g0 + gw].T
            lane = lax.broadcasted_iota(jnp.int32, (1, gw), 1)
            sub = lax.broadcasted_iota(jnp.int32, (gw, 1), 0) < HDIM
            acc = a_sc[g0:g0 + gw, :]
            parts = []
            for i in range(gw // HDIM):
                h = g0 // HDIM + i
                if gw == HDIM:
                    kh = kg
                else:
                    kh = jnp.where((lane < HDIM) if i == 0 else (lane >= HDIM), kg, jnp.zeros_like(kg))
                st = lax.dot_general(
                    kh, qg, (((1,), (1,)), ((), ())), preferred_element_type=jnp.float32
                ) * score_scale
                st = jnp.where(mask, st, neg_large)
                m_old = m_sc[h]
                m_new = jnp.maximum(m_old, jnp.max(st, axis=0, keepdims=True))
                alpha = jnp.exp(m_old - m_new)
                pt = jnp.exp(st - m_new)
                l_sc[h] = alpha * l_sc[h] + jnp.sum(pt, axis=0, keepdims=True)
                m_sc[h] = m_new
                pv = jnp.dot(vt, pt.astype(jnp.bfloat16), preferred_element_type=jnp.float32)
                parts.append(alpha * acc + pv)
            new = parts[0] if len(parts) == 1 else jnp.where(sub, parts[0], parts[1])
            a_sc[g0:g0 + gw, :] = new

    @pl.when(b == nb - 1)
    def _():
        if last:
            for g0 in range(0, width, 128):
                gw = min(128, width - g0)
                h = g0 // HDIM
                if gw == HDIM:
                    den = l_sc[h]
                else:
                    sub = lax.broadcasted_iota(jnp.int32, (gw, 1), 0) < HDIM
                    den = jnp.where(sub, l_sc[h], l_sc[h + 1])
                outs[0][g0:g0 + gw, :] = (a_sc[g0:g0 + gw, :] / den).astype(outs[0].dtype)
        else:
            outs[0][...] = m_sc[...]
            outs[1][...] = l_sc[...]
            outs[2][...] = a_sc[...]


def attend_chunk(info, queries, keys, values, v_off, state, *, kind, reqs, total, last, part=(0, 1), tq=256, sub=1, shift=0):
    tok, full_width = queries.shape
    index, nparts = part
    width = full_width // nparts
    heads = width // HDIM
    nb = keys.shape[0] - v_off
    tk = keys.shape[1]
    tq = min(tok, tq)
    first = state is None
    kernel = functools.partial(
        attn_kernel, kind=kind, heads=heads, reqs=reqs, tq=tq, tk=tk, total=total, first=first, last=last, sub=sub, shift=shift
    )
    q_spec = pl.BlockSpec((tq, width), lambda qi, b, info: (qi, index))

    def kv_block(qi, b, info):
        qpos0 = info[0] + qi * tq
        qlo = seg_scalar(info, qpos0, reqs)
        qhi = seg_scalar(info, qpos0 + tq - 1, reqs)
        if kind == "text":
            lo, hi = qlo * sub, qhi * sub + sub - 1
        else:
            kstart = info[0] + shift
            seg_start = jnp.where(qlo == 0, 0, info[2 + jnp.maximum(qlo - 1, 0)])
            seg_end = info[2 + jnp.minimum(qhi, reqs - 1)]
            lo = (seg_start - kstart) // tk
            hi = (seg_end - 1 - kstart) // tk
        lo = jnp.clip(lo, 0, nb - 1)
        hi = jnp.clip(hi, 0, nb - 1)
        return jnp.minimum(jnp.maximum(b, lo), hi)

    k_spec = pl.BlockSpec((1, tk, width), lambda qi, b, info: (kv_block(qi, b, info), 0, index))
    v_spec = pl.BlockSpec((1, tk, width), lambda qi, b, info: (v_off + kv_block(qi, b, info), 0, index))
    ml_spec = pl.BlockSpec((heads, 1, tq), lambda qi, b, info: (index, 0, qi))
    acc_spec = pl.BlockSpec((width, tq), lambda qi, b, info: (index, qi))
    in_specs = [q_spec, k_spec, v_spec]
    args = [queries, keys, values]
    if not first:
        in_specs += [ml_spec, ml_spec, acc_spec]
        args += list(state)
    if last:
        out_shape = jax.ShapeDtypeStruct((width, tok), jnp.bfloat16)
        out_specs = pl.BlockSpec((width, tq), lambda qi, b, info: (0, qi))
    else:
        out_shape = (
            jax.ShapeDtypeStruct((heads * nparts, 1, tok), jnp.float32),
            jax.ShapeDtypeStruct((heads * nparts, 1, tok), jnp.float32),
            jax.ShapeDtypeStruct((width * nparts, tok), jnp.float32),
        )
        out_specs = (ml_spec, ml_spec, acc_spec)
    flops = 32 * 4 * tok * nb * tk * width * 2
    cost = pl.CostEstimate(
        flops=flops,
        transcendentals=tok * nb * tk * heads,
        bytes_accessed=2 * (tok * width * 2 + 2 * nb * tk * width * 2 + tok * width * 4),
    )
    return pl.pallas_call(
        kernel,
        out_shape=out_shape,
        grid_spec=pltpu.PrefetchScalarGridSpec(
            num_scalar_prefetch=1,
            grid=(tok // tq, nb),
            in_specs=in_specs,
            out_specs=out_specs,
            scratch_shapes=[
                pltpu.VMEM((heads, 1, tq), jnp.float32),
                pltpu.VMEM((heads, 1, tq), jnp.float32),
                pltpu.VMEM((width, tq), jnp.float32),
            ],
        ),
        compiler_params=pltpu.CompilerParams(dimension_semantics=("arbitrary", "arbitrary")),
        cost_estimate=cost,
    )(info, *args)


def local(q_img, k_img, v_img, text_keys, text_values, text_lengths, img_lengths, out_weight):
    tok_dev = q_img.shape[1]
    width = q_img.shape[2]
    reqs = text_keys.shape[1]
    text_slots = text_keys.shape[2]
    nseq = lax.axis_size("seq")
    me = lax.axis_index("seq")
    total = tok_dev * nseq
    longest = total // 2
    reach = min(nseq - 1, (longest + tok_dev - 2) // tok_dev)
    ends = jnp.cumsum(img_lengths).astype(jnp.int32)
    queries = q_img[0]

    def info_for(kstart):
        head = jnp.stack([me * tok_dev, kstart]).astype(jnp.int32)
        return jnp.concatenate([head, ends, text_lengths[0].astype(jnp.int32)])

    pad_to = -(-text_slots // 128) * 128
    pad = ((0, 0), (0, pad_to - text_slots), (0, 0))
    tk = min(tok_dev, 128)
    sub = pad_to // tk
    text_k = jnp.pad(text_keys[0], pad).reshape(reqs * sub, tk, width)
    text_v = jnp.pad(text_values[0], pad).reshape(reqs * sub, tk, width)

    def as_blocks(x):
        return x.reshape(2 * tok_dev // tk, tk, width)

    common = dict(reqs=reqs, total=total)
    info = info_for(0)
    state = attend_chunk(info, queries, text_k, text_v, 0, None, kind="text", last=False, sub=sub, **common)
    both = jnp.stack([k_img[0], v_img[0]])
    chunks = [(both, 0)]
    to_right = [(i, i + 1) for i in range(nseq - 1)]
    to_left = [(i + 1, i) for i in range(nseq - 1)]
    from_left, from_right = both, both
    for step in range(1, reach + 1):
        from_left = lax.ppermute(from_left, "seq", to_right)
        from_right = lax.ppermute(from_right, "seq", to_left)
        if step == 1:
            local_kv, from_left, from_right = lax.optimization_barrier((both, from_left, from_right))
            chunks[0] = (local_kv, 0)
        chunks.append((from_left, -step * tok_dev))
        chunks.append((from_right, step * tok_dev))
    for index, (kv, shift) in enumerate(chunks[:-1]):
        blocks = as_blocks(kv)
        state = attend_chunk(
            info, queries, blocks, blocks, tok_dev // tk, state, kind="image", last=False, shift=shift,
            **common,
        )
    kv, shift = chunks[-1]
    nhead = lax.axis_size("head")
    nparts = 2 if nhead == 2 and width % 256 == 0 else 1
    attn_parts = [
        attend_chunk(
            info, queries, as_blocks(kv), as_blocks(kv), tok_dev // tk, state, kind="image", last=True, shift=shift,
            part=(i, nparts), **common,
        )
        for i in range(nparts)
    ]
    own_cfg = lax.axis_index("cfg")
    cols = out_weight.shape[1]
    half = cols // 2
    mine_weight = jnp.where(own_cfg == 0, guidance, 1.0 - guidance)
    if nhead == 2:
        hx = lax.axis_index("head")
        others = [partner_2(x, "head", 0) for x in attn_parts]
        piece = width // nparts

        def project(w):
            own = None
            for i, x in enumerate(attn_parts):
                term = lax.dot_general(
                    x, lax.dynamic_slice_in_dim(w, hx * width + i * piece, piece, 0),
                    (((0,), (0,)), ((), ())), preferred_element_type=jnp.float32,
                )
                own = term if own is None else own + term
            summed = lax.optimization_barrier(own)
            for i, x in enumerate(others):
                summed = summed + lax.dot_general(
                    x, lax.dynamic_slice_in_dim(w, (1 - hx) * width + i * piece, piece, 0),
                    (((0,), (0,)), ((), ())), preferred_element_type=jnp.float32,
                )
            return summed
    else:
        gathered = lax.all_gather(jnp.concatenate(attn_parts, axis=0), "head", axis=0, tiled=True)

        def project(w):
            return lax.dot_general(gathered, w, (((0,), (0,)), ((), ())), preferred_element_type=jnp.float32)

    full = project(out_weight)
    outgoing = lax.dynamic_slice_in_dim(full, (1 - own_cfg) * half, half, 1)
    partner = partner_2(outgoing.astype(jnp.bfloat16), "cfg", 0).astype(outgoing.dtype)
    keep = lax.dynamic_slice_in_dim(full, own_cfg * half, half, 1)
    guided = mine_weight * keep + (1.0 - mine_weight) * partner
    return guided.astype(jnp.bfloat16)


def solution(mesh):
    placed = (
        P("cfg", ("groups", "seq"), "head"),
        P("cfg", ("groups", "seq"), "head"),
        P("cfg", ("groups", "seq"), "head"),
        P("cfg", "groups", None, "head"),
        P("cfg", "groups", None, "head"),
        P("cfg", "groups"),
        P("groups"),
        P(None, "head"),
    )
    return jax.shard_map(
        local,
        mesh=mesh,
        in_specs=placed,
        out_specs=P(("groups", "seq"), ("head", "cfg")),
        check_vma=False,
    )
```

```python
import functools

import jax
import jax.numpy as jnp
from jax import lax
from jax.experimental import pallas as pl
from jax.experimental.pallas import tpu as pltpu
from jax.sharding import PartitionSpec as P

HDIM = 64


guidance = 4.0
score_scale = 0.125
neg_large = -1e30


def partner_2(x, axis, distance):
    return lax.ppermute(x, axis, [(i, i ^ 1 << distance) for i in range(lax.axis_size(axis))])


def seg_scalar(info_ref, pos, reqs):
    seg = jnp.int32(0)
    for r in range(reqs):
        seg = seg + jnp.where(pos >= info_ref[2 + r], 1, 0).astype(jnp.int32)
    return seg


def seg_vector(info_ref, pos, reqs):
    seg = jnp.zeros(pos.shape, jnp.int32)
    for r in range(reqs):
        seg = seg + (pos >= info_ref[2 + r]).astype(jnp.int32)
    return seg


def attn_kernel(info_ref, q_ref, k_ref, v_ref, *refs, kind, heads, reqs, tq, tk, total, first, last, sub, shift):
    if first:
        ins, outs = (), refs[:-3]
    else:
        ins, outs = refs[:3], refs[3:-3]
    m_sc, l_sc, a_sc = refs[-3:]
    qi = pl.program_id(0)
    b = pl.program_id(1)
    nb = pl.num_programs(1)
    width = heads * HDIM

    @pl.when(b == 0)
    def _():
        if first:
            m_sc[...] = jnp.full(m_sc.shape, neg_large, jnp.float32)
            l_sc[...] = jnp.zeros(l_sc.shape, jnp.float32)
            a_sc[...] = jnp.zeros(a_sc.shape, jnp.float32)
        else:
            m_sc[...] = ins[0][...]
            l_sc[...] = ins[1][...]
            a_sc[...] = ins[2][...]

    qpos0 = info_ref[0] + qi * tq
    qlo = seg_scalar(info_ref, qpos0, reqs)
    qhi = seg_scalar(info_ref, qpos0 + tq - 1, reqs)
    if kind == "text":
        req = b // sub
        offset = (b % sub) * tk
        active = (qlo <= req) & (req <= qhi) & (offset < info_ref[2 + reqs + req])
    else:
        kpos0 = info_ref[0] + shift + b * tk
        klo = seg_scalar(info_ref, kpos0, reqs)
        khi = seg_scalar(info_ref, kpos0 + tk - 1, reqs)
        active = (kpos0 >= 0) & (kpos0 < total) & (klo <= qhi) & (qlo <= khi)

    @pl.when(active)
    def _():
        qseg = seg_vector(info_ref, qpos0 + lax.broadcasted_iota(jnp.int32, (1, tq), 1), reqs)
        row = lax.broadcasted_iota(jnp.int32, (tk, 1), 0)
        if kind == "text":
            mask = (row + offset < info_ref[2 + reqs + req]) & (qseg == req)
        else:
            mask = seg_vector(info_ref, kpos0 + row, reqs) == qseg
        for g0 in range(0, width, 128):
            gw = min(128, width - g0)
            qg = q_ref[:, g0:g0 + gw]
            kg = k_ref[0, :, g0:g0 + gw]
            vt = v_ref[0, :, g0:g0 + gw].T
            lane = lax.broadcasted_iota(jnp.int32, (1, gw), 1)
            sub = lax.broadcasted_iota(jnp.int32, (gw, 1), 0) < HDIM
            acc = a_sc[g0:g0 + gw, :]
            parts = []
            for i in range(gw // HDIM):
                h = g0 // HDIM + i
                if gw == HDIM:
                    kh = kg
                else:
                    kh = jnp.where((lane < HDIM) if i == 0 else (lane >= HDIM), kg, jnp.zeros_like(kg))
                st = lax.dot_general(
                    kh, qg, (((1,), (1,)), ((), ())), preferred_element_type=jnp.float32
                ) * score_scale
                st = jnp.where(mask, st, neg_large)
                m_old = m_sc[h]
                m_new = jnp.maximum(m_old, jnp.max(st, axis=0, keepdims=True))
                alpha = jnp.exp(m_old - m_new)
                pt = jnp.exp(st - m_new)
                l_sc[h] = alpha * l_sc[h] + jnp.sum(pt, axis=0, keepdims=True)
                m_sc[h] = m_new
                pv = jnp.dot(vt, pt.astype(jnp.bfloat16), preferred_element_type=jnp.float32)
                parts.append(alpha * acc + pv)
            new = parts[0] if len(parts) == 1 else jnp.where(sub, parts[0], parts[1])
            a_sc[g0:g0 + gw, :] = new

    @pl.when(b == nb - 1)
    def _():
        if last:
            for g0 in range(0, width, 128):
                gw = min(128, width - g0)
                h = g0 // HDIM
                if gw == HDIM:
                    den = l_sc[h]
                else:
                    sub = lax.broadcasted_iota(jnp.int32, (gw, 1), 0) < HDIM
                    den = jnp.where(sub, l_sc[h], l_sc[h + 1])
                outs[0][g0:g0 + gw, :] = (a_sc[g0:g0 + gw, :] / den).astype(outs[0].dtype)
        else:
            outs[0][...] = m_sc[...]
            outs[1][...] = l_sc[...]
            outs[2][...] = a_sc[...]


def attend_chunk(info, queries, keys, values, v_off, state, *, kind, reqs, total, last, part=(0, 1), tq=256, sub=1, shift=0):
    tok, full_width = queries.shape
    index, nparts = part
    width = full_width // nparts
    heads = width // HDIM
    nb = keys.shape[0] - v_off
    tk = keys.shape[1]
    tq = min(tok, tq)
    first = state is None
    kernel = functools.partial(
        attn_kernel, kind=kind, heads=heads, reqs=reqs, tq=tq, tk=tk, total=total, first=first, last=last, sub=sub, shift=shift
    )
    q_spec = pl.BlockSpec((tq, width), lambda qi, b, info: (qi, index))

    def kv_block(qi, b, info):
        qpos0 = info[0] + qi * tq
        qlo = seg_scalar(info, qpos0, reqs)
        qhi = seg_scalar(info, qpos0 + tq - 1, reqs)
        if kind == "text":
            lo, hi = qlo * sub, qhi * sub + sub - 1
        else:
            kstart = info[0] + shift
            seg_start = jnp.where(qlo == 0, 0, info[2 + jnp.maximum(qlo - 1, 0)])
            seg_end = info[2 + jnp.minimum(qhi, reqs - 1)]
            lo = (seg_start - kstart) // tk
            hi = (seg_end - 1 - kstart) // tk
        lo = jnp.clip(lo, 0, nb - 1)
        hi = jnp.clip(hi, 0, nb - 1)
        return jnp.minimum(jnp.maximum(b, lo), hi)

    k_spec = pl.BlockSpec((1, tk, width), lambda qi, b, info: (kv_block(qi, b, info), 0, index))
    v_spec = pl.BlockSpec((1, tk, width), lambda qi, b, info: (v_off + kv_block(qi, b, info), 0, index))
    ml_spec = pl.BlockSpec((heads, 1, tq), lambda qi, b, info: (index, 0, qi))
    acc_spec = pl.BlockSpec((width, tq), lambda qi, b, info: (index, qi))
    in_specs = [q_spec, k_spec, v_spec]
    args = [queries, keys, values]
    if not first:
        in_specs += [ml_spec, ml_spec, acc_spec]
        args += list(state)
    if last:
        out_shape = jax.ShapeDtypeStruct((width, tok), jnp.bfloat16)
        out_specs = pl.BlockSpec((width, tq), lambda qi, b, info: (0, qi))
    else:
        out_shape = (
            jax.ShapeDtypeStruct((heads * nparts, 1, tok), jnp.float32),
            jax.ShapeDtypeStruct((heads * nparts, 1, tok), jnp.float32),
            jax.ShapeDtypeStruct((width * nparts, tok), jnp.float32),
        )
        out_specs = (ml_spec, ml_spec, acc_spec)
    flops = 32 * 4 * tok * nb * tk * width * 2
    cost = pl.CostEstimate(
        flops=flops,
        transcendentals=tok * nb * tk * heads,
        bytes_accessed=2 * (tok * width * 2 + 2 * nb * tk * width * 2 + tok * width * 4),
    )
    return pl.pallas_call(
        kernel,
        out_shape=out_shape,
        grid_spec=pltpu.PrefetchScalarGridSpec(
            num_scalar_prefetch=1,
            grid=(tok // tq, nb),
            in_specs=in_specs,
            out_specs=out_specs,
            scratch_shapes=[
                pltpu.VMEM((heads, 1, tq), jnp.float32),
                pltpu.VMEM((heads, 1, tq), jnp.float32),
                pltpu.VMEM((width, tq), jnp.float32),
            ],
        ),
        compiler_params=pltpu.CompilerParams(dimension_semantics=("arbitrary", "arbitrary")),
        cost_estimate=cost,
    )(info, *args)


def local(q_img, k_img, v_img, text_keys, text_values, text_lengths, img_lengths, out_weight):
    tok_dev = q_img.shape[1]
    width = q_img.shape[2]
    reqs = text_keys.shape[1]
    text_slots = text_keys.shape[2]
    nseq = lax.axis_size("seq")
    me = lax.axis_index("seq")
    total = tok_dev * nseq
    longest = total // 2
    reach = min(nseq - 1, (longest + tok_dev - 2) // tok_dev)
    ends = jnp.cumsum(img_lengths).astype(jnp.int32)
    queries = q_img[0]

    def info_for(kstart):
        head = jnp.stack([me * tok_dev, kstart]).astype(jnp.int32)
        return jnp.concatenate([head, ends, text_lengths[0].astype(jnp.int32)])

    pad_to = -(-text_slots // 128) * 128
    pad = ((0, 0), (0, pad_to - text_slots), (0, 0))
    tk = min(tok_dev, 128)
    sub = pad_to // tk
    text_k = jnp.pad(text_keys[0], pad).reshape(reqs * sub, tk, width)
    text_v = jnp.pad(text_values[0], pad).reshape(reqs * sub, tk, width)

    def as_blocks(x):
        return x.reshape(2 * tok_dev // tk, tk, width)

    common = dict(reqs=reqs, total=total)
    info = info_for(0)
    state = attend_chunk(info, queries, text_k, text_v, 0, None, kind="text", last=False, sub=sub, **common)
    both = jnp.stack([k_img[0], v_img[0]])
    chunks = [(both, 0)]
    to_right = [(i, i + 1) for i in range(nseq - 1)]
    to_left = [(i + 1, i) for i in range(nseq - 1)]
    from_left, from_right = both, both
    for step in range(1, reach + 1):
        from_left = lax.ppermute(from_left, "seq", to_right)
        from_right = lax.ppermute(from_right, "seq", to_left)
        if step == 1:
            local_kv, from_left, from_right = lax.optimization_barrier((both, from_left, from_right))
            chunks[0] = (local_kv, 0)
        chunks.append((from_left, -step * tok_dev))
        chunks.append((from_right, step * tok_dev))
    for index, (kv, shift) in enumerate(chunks[:-1]):
        blocks = as_blocks(kv)
        state = attend_chunk(
            info, queries, blocks, blocks, tok_dev // tk, state, kind="image", last=False, shift=shift,
            **common,
        )
    kv, shift = chunks[-1]
    nhead = lax.axis_size("head")
    nparts = 1
    attn_parts = [
        attend_chunk(
            info, queries, as_blocks(kv), as_blocks(kv), tok_dev // tk, state, kind="image", last=True, shift=shift,
            part=(i, nparts), **common,
        )
        for i in range(nparts)
    ]
    own_cfg = lax.axis_index("cfg")
    cols = out_weight.shape[1]
    half = cols // 2
    mine_weight = jnp.where(own_cfg == 0, guidance, 1.0 - guidance)
    if nhead == 2:
        hx = lax.axis_index("head")
        others = [partner_2(x, "head", 0) for x in attn_parts]
        piece = width // nparts

        def project(w):
            own = None
            for i, x in enumerate(attn_parts):
                term = lax.dot_general(
                    x, lax.dynamic_slice_in_dim(w, hx * width + i * piece, piece, 0),
                    (((0,), (0,)), ((), ())), preferred_element_type=jnp.float32,
                )
                own = term if own is None else own + term
            summed = lax.optimization_barrier(own)
            for i, x in enumerate(others):
                summed = summed + lax.dot_general(
                    x, lax.dynamic_slice_in_dim(w, (1 - hx) * width + i * piece, piece, 0),
                    (((0,), (0,)), ((), ())), preferred_element_type=jnp.float32,
                )
            return summed
    else:
        gathered = lax.all_gather(jnp.concatenate(attn_parts, axis=0), "head", axis=0, tiled=True)

        def project(w):
            return lax.dot_general(gathered, w, (((0,), (0,)), ((), ())), preferred_element_type=jnp.float32)

    full = project(out_weight)
    outgoing = lax.dynamic_slice_in_dim(full, (1 - own_cfg) * half, half, 1)
    partner = partner_2(outgoing.astype(jnp.bfloat16), "cfg", 0).astype(outgoing.dtype)
    keep = lax.dynamic_slice_in_dim(full, own_cfg * half, half, 1)
    guided = mine_weight * keep + (1.0 - mine_weight) * partner
    return guided.astype(jnp.bfloat16)


def solution(mesh):
    placed = (
        P("cfg", ("groups", "seq"), "head"),
        P("cfg", ("groups", "seq"), "head"),
        P("cfg", ("groups", "seq"), "head"),
        P("cfg", "groups", None, "head"),
        P("cfg", "groups", None, "head"),
        P("cfg", "groups"),
        P("groups"),
        P(None, "head"),
    )
    return jax.shard_map(
        local,
        mesh=mesh,
        in_specs=placed,
        out_specs=P(("groups", "seq"), ("head", "cfg")),
        check_vma=False,
    )
```
